32 devices in a mesh: row: 4 (over y, x), col: 4 (over z), pts: 2 (over core).
Axes of the slice: x: 2, y: 2, z: 4, core: 2. Of those that a mesh axis runs over, the one named last changes fastest.
Arguments:
- green_panel: bfloat16 [4, 2, 512, 6144], P(None, None, 'col', 'pts'), may hold values from -6 to 6
- log_psd: float32 [2, 4, 3072], P('pts', None, ('row', 'col')), may hold values from -1.1 to 1.1
- observed: float32 [4, 2, 512, 512], P(None, None, 'row', 'col'), may hold values from -1 to 1
- pair_weights: int32 [512, 512], P('row', 'col'), may hold values from 0 to 4, as said below
Outputs:
- updated_log_psd: float32 [2, 4, 3072], P('pts', None, ('row', 'col'))
The draws below stay inside these ranges and needn't reach their ends.
Inputs may be any that keep to these rules, and one draw needn't show every extreme that they name: pair_weights is 0 for pairs that are not listed and for every station paired with itself; the share of listed pairs differs from one block of 128 x 128 pairs (one index of row by one of col) to another, and some such blocks list no pair.
All inputs are finite; a program needn't handle non-finite values.
Results may differ from the reference program's by a relative error of at most 0.0014.
Values may be sent and summed in bfloat16 or wider, within the bound.
No kernel may reach another device: no remote copies, remote signals or barrier semaphores. Data moves between devices by JAX's collectives and lax.ppermute only.
A program may use at most 64 MiB of HBM per device.

```python
import jax
import jax.numpy as jnp
from jax import lax

NS = 512
F = 4
PT_DEV = 3072
ITERS = 2
PTS = 6144
GI = 128
GJ = 128
N_PTS = 2


def draw_pair_weights(key, part):
    key_list = jax.random.split(key, 5)
    row_blocks = NS // GI
    col_blocks = NS // GJ
    block_count = row_blocks * col_blocks
    block_level = jax.random.randint(key_list[0], (block_count,), 0, 4)
    empty_block = jax.random.randint(key_list[1], (), 0, block_count)
    full_block = (empty_block + 1 + jax.random.randint(key_list[2], (), 0, block_count - 1)) % block_count
    block_ids = jnp.arange(block_count)
    block_level = jnp.where(block_ids == empty_block, 0, jnp.where(block_ids == full_block, 3, block_level))
    block_share = jnp.array([0, 15, 40, 90], jnp.int32)[block_level].reshape(row_blocks, col_blocks)
    row_block = jnp.arange(NS) // GI
    col_block = jnp.arange(NS) // GJ
    pair_share = block_share[row_block][:, col_block]
    pick_draw = jax.random.randint(key_list[3], (NS, NS), 0, 100)
    pair_value = jax.random.randint(key_list[4], (NS, NS), 1, 5)
    self_pair = jnp.arange(NS)[:, None] == jnp.arange(NS)[None, :]
    chosen = jnp.logical_and(pick_draw < pair_share, jnp.logical_not(self_pair))
    return jnp.where(chosen, pair_value, 0).astype(jnp.int32)


def draw_log_psd(key, part):
    array_shape = (N_PTS, F, PT_DEV)
    position = (jnp.arange(N_PTS)[:, None, None] * PT_DEV + jnp.arange(PT_DEV)[None, None, :]).astype(jnp.float32)
    position = position / (N_PTS * PT_DEV)
    rough_part = 0.3 * jax.random.truncated_normal(key, -2.0, 2.0, array_shape, jnp.float32)
    return (rough_part + position - 0.5).astype(jnp.float32)


def draw_observed(key, part):
    array_shape = (F, 2, NS, NS)
    spread_scale = 1.7 * float(PTS) ** (-0.5)
    raw_values = jax.random.truncated_normal(key, -3.0, 3.0, array_shape, jnp.float32)
    return (spread_scale * raw_values).astype(jnp.float32)


def level_of(key, extent, pieces, low, largest):
    loudness = 1.0
    for axis_at, blocks in pieces:
        steps = jax.random.uniform(jax.random.fold_in(jax.random.fold_in(key, 6), axis_at), (blocks,), jnp.float32, low / len(pieces), largest / len(pieces))
        loudness = loudness * jnp.repeat(jnp.exp(steps), extent[axis_at] // blocks).reshape((-1,) + (1,) * (len(extent) - 1 - axis_at))
    return loudness


def normal_values(own_key, shape, spread, limit, pieces=(), kind=jnp.bfloat16):
    values = jax.random.normal(own_key, shape, jnp.float32) * spread
    if len(pieces) > 0:
        values = level_of(own_key, shape, pieces, -0.22, 0.18) * values
    return jnp.clip(values, min=-limit, max=limit).astype(kind)


def setup_inputs(seed: int = 0) -> dict:
    arg_keys = jax.random.split(jax.random.key(seed), 5)
    return {
        "green_panel": normal_values(arg_keys[0], (F, 2, NS, PTS), 1.0, 6.0, ((2, 4), (3, 2))),
        "log_psd": draw_log_psd(jax.random.fold_in(arg_keys[4], 71), 0),
        "observed": draw_observed(jax.random.fold_in(arg_keys[4], 71), 0),
        "pair_weights": draw_pair_weights(jax.random.fold_in(arg_keys[4], 71), 0),
    }


epsilon = 1e-06
descent = 0.1

def reference(green_panel, log_psd, observed, pair_weights):
    quad_weight = 1.0 / (N_PTS * PT_DEV)
    pair_scale = pair_weights.astype(jnp.float32)
    log_start = jnp.transpose(log_psd, (1, 0, 2)).reshape(F, N_PTS * PT_DEV)

    def run_sweep(sweep_idx, log_field):
        psd_field = jnp.exp(log_field)
        gradient_rows = []
        for channel in range(F):
            real_part = green_panel[channel, 0]
            imag_part = green_panel[channel, 1]
            weight_real = (real_part.astype(jnp.float32) * psd_field[channel][None, :]).astype(jnp.bfloat16)
            weight_imag = (imag_part.astype(jnp.float32) * psd_field[channel][None, :]).astype(jnp.bfloat16)
            corr_real = (jnp.dot(real_part, weight_real.T, preferred_element_type=jnp.float32) + jnp.dot(imag_part, weight_imag.T, preferred_element_type=jnp.float32)) * quad_weight
            corr_imag = (jnp.dot(imag_part, weight_real.T, preferred_element_type=jnp.float32) - jnp.dot(real_part, weight_imag.T, preferred_element_type=jnp.float32)) * quad_weight
            adj_real = (pair_scale * (corr_real - observed[channel, 0])).astype(jnp.bfloat16)
            adj_imag = (pair_scale * (corr_imag - observed[channel, 1])).astype(jnp.bfloat16)
            accum_real = jnp.dot(adj_real, real_part, preferred_element_type=jnp.float32) - jnp.dot(adj_imag, imag_part, preferred_element_type=jnp.float32)
            accum_imag = jnp.dot(adj_real, imag_part, preferred_element_type=jnp.float32) + jnp.dot(adj_imag, real_part, preferred_element_type=jnp.float32)
            inner_sum = lax.optimization_barrier(jnp.sum(real_part.astype(jnp.float32) * accum_real + imag_part.astype(jnp.float32) * accum_imag, axis=0))
            gradient_rows.append(quad_weight * psd_field[channel] * inner_sum)
        gradient = jnp.stack(gradient_rows)
        grad_scale = jnp.sqrt(jnp.mean(gradient * gradient) + epsilon)
        return log_field - descent * gradient / grad_scale
    log_final = lax.fori_loop(0, ITERS, run_sweep, log_start)
    return jnp.transpose(log_final.reshape(F, N_PTS, PT_DEV), (1, 0, 2))
```

```python
import jax
import jax.numpy as jnp
from jax import lax
from jax.sharding import PartitionSpec as P

ITERS = 2


epsilon = 1e-06
descent = 0.1


def from_root(block, axis, source):
    block = jnp.where(lax.axis_index(axis) == source, block, jnp.zeros_like(block))
    return lax.psum(block, axis)


def butterfly_sum(value, axes):
    for axis in axes:
        size = lax.axis_size(axis)
        if size & (size - 1):
            value = lax.psum(value, axis)
            continue
        bit = 1
        while bit < size:
            pairs = [(i, i ^ bit) for i in range(size)]
            value = value + lax.ppermute(value, axis, pairs)
            bit *= 2
    return value


def swap_add(value, axis):
    size = lax.axis_size(axis)
    if size != 2:
        return lax.psum(value, axis)
    return value + lax.ppermute(value, axis, [(0, 1), (1, 0)])


def correlate(left_rows, weighted):
    half_a = left_rows.shape[1] // 2
    half_b = weighted.shape[1] // 2
    products = jnp.einsum("fan,fbn->fab", left_rows, weighted, preferred_element_type=jnp.float32)
    corr_real = products[:, :half_a, :half_b] + products[:, half_a:, half_b:]
    corr_imag = products[:, half_a:, :half_b] - products[:, :half_a, half_b:]
    return jnp.stack([corr_real, corr_imag], axis=1)


def adjoint_block(adjoint):
    adj_real = adjoint[:, 0]
    adj_imag = adjoint[:, 1]
    top_half = jnp.concatenate([adj_real, -adj_imag], axis=2)
    low_half = jnp.concatenate([adj_imag, adj_real], axis=2)
    return jnp.concatenate([top_half, low_half], axis=1)


def point_terms(adjoint, right_rows, left_rows, psd_field, quad_weight):
    accumulated = jnp.einsum(
        "fab,fbn->fan", adjoint_block(adjoint), right_rows, preferred_element_type=jnp.float32
    )
    return quad_weight * psd_field * jnp.sum(left_rows * accumulated, axis=1)


def body(green_panel, log_psd, observed, pair_weights):
    freq_count, comp_count, span_j, local_pts = green_panel.shape
    span_i = observed.shape[2]
    piece = log_psd.shape[2]
    row_count = lax.axis_size("row")
    col_count = lax.axis_size("col")
    pts_count = lax.axis_size("pts")
    quad_weight = 1.0 / (pts_count * local_pts)
    entry_count = freq_count * pts_count * local_pts
    pair_scale = pair_weights.astype(jnp.float32)
    group_ratio = col_count // row_count
    pieces = []
    for member in range(group_ratio):
        pieces.append(from_root(green_panel, "col", lax.axis_index("row") * group_ratio + member))
    rows_block = jnp.concatenate(pieces, axis=2).reshape(freq_count, 2 * span_i, local_pts)
    cols_block = green_panel.reshape(freq_count, 2 * span_j, local_pts)

    slot = lax.axis_index("row") * col_count + lax.axis_index("col")
    offset = slot * piece
    placed = lax.dynamic_update_slice_in_dim(
        jnp.zeros((freq_count, local_pts), jnp.float32), log_psd[0], offset, axis=1
    )
    log_field = butterfly_sum(placed, ("row", "col"))

    for _ in range(ITERS):
        psd_field = jnp.exp(log_field)
        weighted = (green_panel * psd_field[:, None, None, :]).astype(jnp.bfloat16)
        weighted = weighted.reshape(freq_count, 2 * span_j, local_pts)
        pair_sum = swap_add(correlate(rows_block, weighted), "pts")
        adjoint = (pair_scale * (quad_weight * pair_sum - observed)).astype(jnp.bfloat16)
        point_part = point_terms(adjoint, cols_block, rows_block, psd_field, quad_weight)
        gradient = butterfly_sum(point_part, ("row", "col"))
        squares = swap_add(jnp.sum(gradient * gradient), "pts")
        log_field = log_field - descent * gradient / jnp.sqrt(squares / entry_count + epsilon)

    own = lax.dynamic_slice_in_dim(log_field, offset, piece, axis=1)
    return own[None]


def solution(mesh):
    return jax.shard_map(
        body,
        mesh=mesh,
        in_specs=(
            P(None, None, "col", "pts"),
            P("pts", None, ("row", "col")),
            P(None, None, "row", "col"),
            P("row", "col"),
        ),
        out_specs=P("pts", None, ("row", "col")),
        check_vma=False,
    )
```

```python
import jax
import jax.numpy as jnp
from jax import lax
from jax.sharding import PartitionSpec as P

ITERS = 2


epsilon = 1e-06
descent = 0.1


def from_root(block, axis, source):
    block = jnp.where(lax.axis_index(axis) == source, block, jnp.zeros_like(block))
    return lax.psum(block, axis)


def butterfly_sum(value, axes):
    for axis in axes:
        size = lax.axis_size(axis)
        if size & (size - 1):
            value = lax.psum(value, axis)
            continue
        me = lax.axis_index(axis)
        bit = 1
        while bit < size:
            radix = 4 if bit * 4 <= size else 2
            got = [value]
            for m in range(1, radix):
                mask = m * bit
                got.append(lax.ppermute(value, axis, [(i, i ^ mask) for i in range(size)]))
            stacked = jnp.stack(got)
            local = (me // bit) % radix
            ordered = [stacked[local ^ j] for j in range(radix)]
            if radix == 4:
                value = (ordered[0] + ordered[1]) + (ordered[2] + ordered[3])
            else:
                value = ordered[0] + ordered[1]
            bit *= radix
    return value


def swap_add(value, axis):
    size = lax.axis_size(axis)
    if size != 2:
        return lax.psum(value, axis)
    return value + lax.ppermute(value, axis, [(0, 1), (1, 0)])


def correlate(left_rows, weighted):
    half_a = left_rows.shape[1] // 2
    half_b = weighted.shape[1] // 2
    products = jnp.einsum("fan,fbn->fab", left_rows, weighted, preferred_element_type=jnp.float32)
    corr_real = products[:, :half_a, :half_b] + products[:, half_a:, half_b:]
    corr_imag = products[:, half_a:, :half_b] - products[:, :half_a, half_b:]
    return jnp.stack([corr_real, corr_imag], axis=1)


def adjoint_block(adjoint):
    adj_real = adjoint[:, 0]
    adj_imag = adjoint[:, 1]
    top_half = jnp.concatenate([adj_real, -adj_imag], axis=2)
    low_half = jnp.concatenate([adj_imag, adj_real], axis=2)
    return jnp.concatenate([top_half, low_half], axis=1)


def point_terms(adjoint, right_rows, left_rows, psd_field, quad_weight):
    accumulated = jnp.einsum(
        "fab,fbn->fan", adjoint_block(adjoint), right_rows, preferred_element_type=jnp.float32
    )
    return quad_weight * psd_field * jnp.sum(left_rows * accumulated, axis=1)


def body(green_panel, log_psd, observed, pair_weights):
    freq_count, comp_count, span_j, local_pts = green_panel.shape
    span_i = observed.shape[2]
    piece = log_psd.shape[2]
    row_count = lax.axis_size("row")
    col_count = lax.axis_size("col")
    pts_count = lax.axis_size("pts")
    quad_weight = 1.0 / (pts_count * local_pts)
    entry_count = freq_count * pts_count * local_pts
    pair_scale = pair_weights.astype(jnp.float32)
    group_ratio = col_count // row_count
    pieces = []
    for member in range(group_ratio):
        pieces.append(from_root(green_panel, "col", lax.axis_index("row") * group_ratio + member))
    rows_block = jnp.concatenate(pieces, axis=2).reshape(freq_count, 2 * span_i, local_pts)
    cols_block = green_panel.reshape(freq_count, 2 * span_j, local_pts)

    slot = lax.axis_index("row") * col_count + lax.axis_index("col")
    offset = slot * piece
    placed = lax.dynamic_update_slice_in_dim(
        jnp.zeros((freq_count, local_pts), jnp.float32), log_psd[0], offset, axis=1
    )
    log_field = butterfly_sum(placed, ("row", "col"))

    for _ in range(ITERS):
        psd_field = jnp.exp(log_field)
        weighted = (green_panel * psd_field[:, None, None, :]).astype(jnp.bfloat16)
        weighted = weighted.reshape(freq_count, 2 * span_j, local_pts)
        pair_sum = swap_add(correlate(rows_block, weighted), "pts")
        adjoint = (pair_scale * (quad_weight * pair_sum - observed)).astype(jnp.bfloat16)
        point_part = point_terms(adjoint, cols_block, rows_block, psd_field, quad_weight)
        gradient = butterfly_sum(point_part, ("row", "col"))
        squares = swap_add(jnp.sum(gradient * gradient), "pts")
        log_field = log_field - descent * gradient / jnp.sqrt(squares / entry_count + epsilon)

    own = lax.dynamic_slice_in_dim(log_field, offset, piece, axis=1)
    return own[None]


def solution(mesh):
    return jax.shard_map(
        body,
        mesh=mesh,
        in_specs=(
            P(None, None, "col", "pts"),
            P("pts", None, ("row", "col")),
            P(None, None, "row", "col"),
            P("row", "col"),
        ),
        out_specs=P("pts", None, ("row", "col")),
        check_vma=False,
    )
```

```python
import jax
import jax.numpy as jnp
from jax import lax
from jax.sharding import PartitionSpec as P

ITERS = 2


epsilon = 1e-06
descent = 0.1


def from_root(block, axis, source):
    block = jnp.where(lax.axis_index(axis) == source, block, jnp.zeros_like(block))
    return lax.psum(block, axis)


def butterfly_sum(value, axes):
    for axis in axes:
        size = lax.axis_size(axis)
        if size & (size - 1):
            value = lax.psum(value, axis)
            continue
        me = lax.axis_index(axis)
        bit = 1
        while bit < size:
            radix = 4 if bit * 4 <= size else 2
            got = [value]
            for m in range(1, radix):
                mask = m * bit
                got.append(lax.ppermute(value, axis, [(i, i ^ mask) for i in range(size)]))
            stacked = jnp.stack(got)
            local = (me // bit) % radix
            ordered = [stacked[local ^ j] for j in range(radix)]
            if radix == 4:
                value = (ordered[0] + ordered[1]) + (ordered[2] + ordered[3])
            else:
                value = ordered[0] + ordered[1]
            bit *= radix
    return value


def swap_add(value, axis):
    size = lax.axis_size(axis)
    if size != 2:
        return lax.psum(value, axis)
    return value + lax.ppermute(value, axis, [(0, 1), (1, 0)])


def correlate(left_rows, weighted):
    half_a = left_rows.shape[1] // 2
    half_b = weighted.shape[1] // 2
    products = jnp.einsum("fan,fbn->fab", left_rows, weighted, preferred_element_type=jnp.float32)
    corr_real = products[:, :half_a, :half_b] + products[:, half_a:, half_b:]
    corr_imag = products[:, half_a:, :half_b] - products[:, :half_a, half_b:]
    return jnp.stack([corr_real, corr_imag], axis=1)


def adjoint_block(adjoint):
    adj_real = adjoint[:, 0]
    adj_imag = adjoint[:, 1]
    top_half = jnp.concatenate([adj_real, -adj_imag], axis=2)
    low_half = jnp.concatenate([adj_imag, adj_real], axis=2)
    return jnp.concatenate([top_half, low_half], axis=1)


def point_terms(adjoint, right_rows, left_rows, psd_field, quad_weight):
    accumulated = jnp.einsum(
        "fab,fbn->fan", adjoint_block(adjoint), right_rows, preferred_element_type=jnp.float32
    )
    return quad_weight * psd_field * jnp.sum(left_rows * accumulated, axis=1)


def broadcast_body(green_panel, log_psd, observed, pair_weights):
    freq_count, comp_count, span_j, local_pts = green_panel.shape
    span_i = observed.shape[2]
    piece = log_psd.shape[2]
    row_count = lax.axis_size("row")
    col_count = lax.axis_size("col")
    pts_count = lax.axis_size("pts")
    quad_weight = 1.0 / (pts_count * local_pts)
    entry_count = freq_count * pts_count * local_pts
    pair_scale = pair_weights.astype(jnp.float32)
    group_ratio = col_count // row_count
    pieces = []
    for member in range(group_ratio):
        pieces.append(from_root(green_panel, "col", lax.axis_index("row") * group_ratio + member))
    rows_block = jnp.concatenate(pieces, axis=2).reshape(freq_count, 2 * span_i, local_pts)
    cols_block = green_panel.reshape(freq_count, 2 * span_j, local_pts)

    slot = lax.axis_index("row") * col_count + lax.axis_index("col")
    offset = slot * piece
    placed = lax.dynamic_update_slice_in_dim(
        jnp.zeros((freq_count, local_pts), jnp.float32), log_psd[0], offset, axis=1
    )
    log_field = butterfly_sum(placed, ("row", "col"))

    for _ in range(ITERS):
        psd_field = jnp.exp(log_field)
        weighted = (green_panel * psd_field[:, None, None, :]).astype(jnp.bfloat16)
        weighted = weighted.reshape(freq_count, 2 * span_j, local_pts)
        pair_sum = swap_add(correlate(rows_block, weighted), "pts")
        adjoint = (pair_scale * (quad_weight * pair_sum - observed)).astype(jnp.bfloat16)
        point_part = point_terms(adjoint, cols_block, rows_block, psd_field, quad_weight)
        gradient = butterfly_sum(point_part, ("row", "col"))
        squares = swap_add(jnp.sum(gradient * gradient), "pts")
        log_field = log_field - descent * gradient / jnp.sqrt(squares / entry_count + epsilon)

    own = lax.dynamic_slice_in_dim(log_field, offset, piece, axis=1)
    return own[None]


PAIR_PLAN = ((0, 0, 1), (1, 2, 0), (2, 0, 3), (2, 2, 1), (1, 1, 3), (3, 3, 2))


def pair_tables(blocks):
    role = [0] * (blocks * blocks)
    panel_moves = []
    needs = []
    for line, sender, receiver in PAIR_PLAN:
        role[line * blocks + receiver] = 1
        panel_moves.append((line * blocks + sender, line * blocks + receiver))
        needs.append((line * blocks + receiver, 0, receiver * blocks + sender))
        needs.append((line * blocks + receiver, 1, sender * blocks + receiver))
    for plane in range(blocks):
        role[plane * blocks + plane] = 2
    rounds = []
    moved = [[0, 0] for _ in range(blocks * blocks)]
    for dest, which, owner in needs:
        if owner == dest:
            continue
        for number, (pairs, whiches) in enumerate(rounds):
            if all(s != owner and d != dest for s, d in pairs):
                pairs.append((owner, dest))
                whiches.append((dest, which))
                moved[dest][which] = number + 1
                break
        else:
            rounds.append(([(owner, dest)], [(dest, which)]))
            moved[dest][which] = len(rounds)
    return role, panel_moves, rounds, moved


def pair_body(green_panel, log_psd, observed, pair_weights):
    freq_count, comp_count, span_j, local_pts = green_panel.shape
    piece = log_psd.shape[2]
    blocks = lax.axis_size("col")
    pts_count = lax.axis_size("pts")
    quad_weight = 1.0 / (pts_count * local_pts)
    entry_count = freq_count * pts_count * local_pts
    role, panel_moves, rounds, moved = pair_tables(blocks)
    slot = lax.axis_index("row") * blocks + lax.axis_index("col")
    my_role = jnp.array(role, jnp.int32)[slot]
    is_diag = my_role == 2
    axes = ("row", "col")

    received = lax.ppermute(green_panel, axes, panel_moves)
    other = jnp.where(is_diag, green_panel, received)
    mine_rows = green_panel.reshape(freq_count, 2 * span_j, local_pts)
    other_rows = other.reshape(freq_count, 2 * span_j, local_pts)

    own_block = jnp.concatenate(
        [observed.reshape(-1, span_j, span_j), pair_weights.astype(jnp.float32)[None]], axis=0
    )
    arrived = [own_block]
    for pairs, _ in rounds:
        arrived.append(lax.ppermute(own_block, axes, pairs))
    arrived = jnp.stack(arrived)
    moved_table = jnp.array(moved, jnp.int32)[slot]
    first_block = arrived[moved_table[0]]
    second_block = arrived[moved_table[1]]
    obs_first = first_block[:-1].reshape(observed.shape)
    obs_second = second_block[:-1].reshape(observed.shape)
    scale_first = first_block[-1]
    scale_second = second_block[-1]
    keep_first = my_role > 0
    keep_second = my_role == 1

    offset = slot * piece
    placed = lax.dynamic_update_slice_in_dim(
        jnp.zeros((freq_count, local_pts), jnp.float32), log_psd[0], offset, axis=1
    )
    log_field = butterfly_sum(placed, axes)

    for _ in range(ITERS):
        psd_field = jnp.exp(log_field)
        spread = psd_field[:, None, None, :]
        weighted_mine = (green_panel * spread).astype(jnp.bfloat16).reshape(mine_rows.shape)
        weighted_other = (other * spread).astype(jnp.bfloat16).reshape(other_rows.shape)
        corr_first = correlate(mine_rows, weighted_other)
        corr_second = correlate(other_rows, weighted_mine)
        both = swap_add(jnp.stack([corr_first, corr_second]), "pts")
        adj_first = (scale_first * (quad_weight * both[0] - obs_first)).astype(jnp.bfloat16)
        adj_second = (scale_second * (quad_weight * both[1] - obs_second)).astype(jnp.bfloat16)
        term_first = point_terms(adj_first, other_rows, mine_rows, psd_field, quad_weight)
        term_second = point_terms(adj_second, mine_rows, other_rows, psd_field, quad_weight)
        point_part = jnp.where(keep_first, term_first, 0.0) + jnp.where(keep_second, term_second, 0.0)
        gradient = butterfly_sum(point_part, axes)
        squares = swap_add(jnp.sum(gradient * gradient), "pts")
        log_field = log_field - descent * gradient / jnp.sqrt(squares / entry_count + epsilon)

    own = lax.dynamic_slice_in_dim(log_field, offset, piece, axis=1)
    return own[None]


def solution(mesh):
    shape = mesh.shape
    plan_fits = shape["row"] == 4 and shape["col"] == 4 and shape["pts"] == 2
    return jax.shard_map(
        pair_body if plan_fits else broadcast_body,
        mesh=mesh,
        in_specs=(
            P(None, None, "col", "pts"),
            P("pts", None, ("row", "col")),
            P(None, None, "row", "col"),
            P("row", "col"),
        ),
        out_specs=P("pts", None, ("row", "col")),
        check_vma=False,
    )
```

```python
import jax
import jax.numpy as jnp
from jax import lax
from jax.sharding import PartitionSpec as P

ITERS = 2


epsilon = 1e-06
descent = 0.1


def from_root(block, axis, source):
    block = jnp.where(lax.axis_index(axis) == source, block, jnp.zeros_like(block))
    return lax.psum(block, axis)


def butterfly_sum(value, axes):
    for axis in axes:
        size = lax.axis_size(axis)
        if size & (size - 1):
            value = lax.psum(value, axis)
            continue
        me = lax.axis_index(axis)
        bit = 1
        while bit < size:
            radix = 4 if bit * 4 <= size else 2
            got = [value]
            for m in range(1, radix):
                mask = m * bit
                got.append(lax.ppermute(value, axis, [(i, i ^ mask) for i in range(size)]))
            stacked = jnp.stack(got)
            local = (me // bit) % radix
            ordered = [stacked[local ^ j] for j in range(radix)]
            if radix == 4:
                value = (ordered[0] + ordered[1]) + (ordered[2] + ordered[3])
            else:
                value = ordered[0] + ordered[1]
            bit *= radix
    return value


def swap_add(value, axis):
    size = lax.axis_size(axis)
    if size != 2:
        return lax.psum(value, axis)
    return value + lax.ppermute(value, axis, [(0, 1), (1, 0)])


def correlate(left_rows, weighted):
    half_a = left_rows.shape[1] // 2
    half_b = weighted.shape[1] // 2
    products = jnp.einsum("fan,fbn->fab", left_rows, weighted, preferred_element_type=jnp.float32)
    corr_real = products[:, :half_a, :half_b] + products[:, half_a:, half_b:]
    corr_imag = products[:, half_a:, :half_b] - products[:, :half_a, half_b:]
    return jnp.stack([corr_real, corr_imag], axis=1)


def adjoint_block(adjoint):
    adj_real = adjoint[:, 0]
    adj_imag = adjoint[:, 1]
    top_half = jnp.concatenate([adj_real, -adj_imag], axis=2)
    low_half = jnp.concatenate([adj_imag, adj_real], axis=2)
    return jnp.concatenate([top_half, low_half], axis=1)


def point_terms(adjoint, right_rows, left_rows, psd_field, quad_weight):
    accumulated = jnp.einsum(
        "fab,fbn->fan", adjoint_block(adjoint), right_rows, preferred_element_type=jnp.float32
    )
    return quad_weight * psd_field * jnp.sum(left_rows * accumulated, axis=1)


def broadcast_body(green_panel, log_psd, observed, pair_weights):
    freq_count, comp_count, span_j, local_pts = green_panel.shape
    span_i = observed.shape[2]
    piece = log_psd.shape[2]
    row_count = lax.axis_size("row")
    col_count = lax.axis_size("col")
    pts_count = lax.axis_size("pts")
    quad_weight = 1.0 / (pts_count * local_pts)
    entry_count = freq_count * pts_count * local_pts
    pair_scale = pair_weights.astype(jnp.float32)
    group_ratio = col_count // row_count
    pieces = []
    for member in range(group_ratio):
        pieces.append(from_root(green_panel, "col", lax.axis_index("row") * group_ratio + member))
    rows_block = jnp.concatenate(pieces, axis=2).reshape(freq_count, 2 * span_i, local_pts)
    cols_block = green_panel.reshape(freq_count, 2 * span_j, local_pts)

    slot = lax.axis_index("row") * col_count + lax.axis_index("col")
    offset = slot * piece
    placed = lax.dynamic_update_slice_in_dim(
        jnp.zeros((freq_count, local_pts), jnp.float32), log_psd[0], offset, axis=1
    )
    log_field = butterfly_sum(placed, ("row", "col"))

    for _ in range(ITERS):
        psd_field = jnp.exp(log_field)
        weighted = (green_panel * psd_field[:, None, None, :]).astype(jnp.bfloat16)
        weighted = weighted.reshape(freq_count, 2 * span_j, local_pts)
        pair_sum = swap_add(correlate(rows_block, weighted), "pts")
        adjoint = (pair_scale * (quad_weight * pair_sum - observed)).astype(jnp.bfloat16)
        point_part = point_terms(adjoint, cols_block, rows_block, psd_field, quad_weight)
        gradient = butterfly_sum(point_part, ("row", "col"))
        squares = swap_add(jnp.sum(gradient * gradient), "pts")
        log_field = log_field - descent * gradient / jnp.sqrt(squares / entry_count + epsilon)

    own = lax.dynamic_slice_in_dim(log_field, offset, piece, axis=1)
    return own[None]


PAIR_PLAN = ((0, 0, 1), (1, 2, 0), (2, 0, 3), (2, 2, 1), (1, 1, 3), (3, 3, 2))


def pair_tables(blocks):
    role = [0] * (blocks * blocks)
    panel_moves = []
    needs = []
    for line, sender, receiver in PAIR_PLAN:
        role[line * blocks + receiver] = 1
        panel_moves.append((line * blocks + sender, line * blocks + receiver))
        needs.append((line * blocks + receiver, 0, receiver * blocks + sender))
        needs.append((line * blocks + receiver, 1, sender * blocks + receiver))
    for plane in range(blocks):
        role[plane * blocks + plane] = 2
    rounds = []
    moved = [[0, 0] for _ in range(blocks * blocks)]
    for dest, which, owner in needs:
        if owner == dest:
            continue
        for number, (pairs, whiches) in enumerate(rounds):
            if all(s != owner and d != dest for s, d in pairs):
                pairs.append((owner, dest))
                whiches.append((dest, which))
                moved[dest][which] = number + 1
                break
        else:
            rounds.append(([(owner, dest)], [(dest, which)]))
            moved[dest][which] = len(rounds)
    return role, panel_moves, rounds, moved


def pair_body(green_panel, log_psd, observed, pair_weights):
    freq_count, comp_count, span_j, local_pts = green_panel.shape
    piece = log_psd.shape[2]
    blocks = lax.axis_size("col")
    pts_count = lax.axis_size("pts")
    quad_weight = 1.0 / (pts_count * local_pts)
    entry_count = freq_count * pts_count * local_pts
    role, panel_moves, rounds, moved = pair_tables(blocks)
    slot = lax.axis_index("row") * blocks + lax.axis_index("col")
    my_role = jnp.array(role, jnp.int32)[slot]
    is_diag = my_role == 2
    axes = ("row", "col")

    received = lax.ppermute(green_panel, axes, panel_moves)

    own_block = jnp.concatenate(
        [observed.reshape(-1, span_j, span_j), pair_weights.astype(jnp.float32)[None]], axis=0
    )
    arrived = [own_block]
    for pairs, _ in rounds:
        arrived.append(lax.ppermute(own_block, axes, pairs))
    arrived = jnp.stack(arrived)
    received, arrived = lax.optimization_barrier((received, arrived))
    other = jnp.where(is_diag, green_panel, received)
    mine_rows = green_panel.reshape(freq_count, 2 * span_j, local_pts)
    other_rows = other.reshape(freq_count, 2 * span_j, local_pts)
    moved_table = jnp.array(moved, jnp.int32)[slot]
    first_block = arrived[moved_table[0]]
    second_block = arrived[moved_table[1]]
    obs_first = first_block[:-1].reshape(observed.shape)
    obs_second = second_block[:-1].reshape(observed.shape)
    scale_first = first_block[-1]
    scale_second = second_block[-1]
    keep_first = my_role > 0
    keep_second = my_role == 1

    offset = slot * piece
    placed = lax.dynamic_update_slice_in_dim(
        jnp.zeros((freq_count, local_pts), jnp.float32), log_psd[0], offset, axis=1
    )
    log_field = butterfly_sum(placed, axes)

    for _ in range(ITERS):
        psd_field = jnp.exp(log_field)
        spread = psd_field[:, None, None, :]
        weighted_mine = (green_panel * spread).astype(jnp.bfloat16).reshape(mine_rows.shape)
        weighted_other = (other * spread).astype(jnp.bfloat16).reshape(other_rows.shape)
        corr_first = correlate(mine_rows, weighted_other)
        corr_second = correlate(other_rows, weighted_mine)
        both = swap_add(jnp.stack([corr_first, corr_second]), "pts")
        adj_first = (scale_first * (quad_weight * both[0] - obs_first)).astype(jnp.bfloat16)
        adj_second = (scale_second * (quad_weight * both[1] - obs_second)).astype(jnp.bfloat16)
        term_first = point_terms(adj_first, other_rows, mine_rows, psd_field, quad_weight)
        term_second = point_terms(adj_second, mine_rows, other_rows, psd_field, quad_weight)
        point_part = jnp.where(keep_first, term_first, 0.0) + jnp.where(keep_second, term_second, 0.0)
        gradient = butterfly_sum(point_part, axes)
        squares = swap_add(jnp.sum(gradient * gradient), "pts")
        log_field = log_field - descent * gradient / jnp.sqrt(squares / entry_count + epsilon)

    own = lax.dynamic_slice_in_dim(log_field, offset, piece, axis=1)
    return own[None]


def solution(mesh):
    shape = mesh.shape
    plan_fits = shape["row"] == 4 and shape["col"] == 4 and shape["pts"] == 2
    return jax.shard_map(
        pair_body if plan_fits else broadcast_body,
        mesh=mesh,
        in_specs=(
            P(None, None, "col", "pts"),
            P("pts", None, ("row", "col")),
            P(None, None, "row", "col"),
            P("row", "col"),
        ),
        out_specs=P("pts", None, ("row", "col")),
        check_vma=False,
    )
```

```python
import jax
import jax.numpy as jnp
from jax import lax
from jax.sharding import PartitionSpec as P

ITERS = 2


epsilon = 1e-06
descent = 0.1


def from_root(block, axis, source):
    block = jnp.where(lax.axis_index(axis) == source, block, jnp.zeros_like(block))
    return lax.psum(block, axis)


def butterfly_sum(value, axes):
    for axis in axes:
        size = lax.axis_size(axis)
        if size & (size - 1):
            value = lax.psum(value, axis)
            continue
        me = lax.axis_index(axis)
        bit = 1
        while bit < size:
            radix = 4 if bit * 4 <= size else 2
            got = [value]
            for m in range(1, radix):
                mask = m * bit
                got.append(lax.ppermute(value, axis, [(i, i ^ mask) for i in range(size)]))
            stacked = jnp.stack(got)
            local = (me // bit) % radix
            ordered = [stacked[local ^ j] for j in range(radix)]
            if radix == 4:
                value = (ordered[0] + ordered[1]) + (ordered[2] + ordered[3])
            else:
                value = ordered[0] + ordered[1]
            bit *= radix
    return value


def swap_add(value, axis):
    size = lax.axis_size(axis)
    if size != 2:
        return lax.psum(value, axis)
    return value + lax.ppermute(value, axis, [(0, 1), (1, 0)])


def correlate(left_rows, weighted):
    half_a = left_rows.shape[1] // 2
    half_b = weighted.shape[1] // 2
    products = jnp.einsum("fan,fbn->fab", left_rows, weighted, preferred_element_type=jnp.float32)
    corr_real = products[:, :half_a, :half_b] + products[:, half_a:, half_b:]
    corr_imag = products[:, half_a:, :half_b] - products[:, :half_a, half_b:]
    return jnp.stack([corr_real, corr_imag], axis=1)


def adjoint_block(adjoint):
    adj_real = adjoint[:, 0]
    adj_imag = adjoint[:, 1]
    top_half = jnp.concatenate([adj_real, -adj_imag], axis=2)
    low_half = jnp.concatenate([adj_imag, adj_real], axis=2)
    return jnp.concatenate([top_half, low_half], axis=1)


def point_terms(adjoint, right_rows, left_rows, psd_field, quad_weight):
    accumulated = jnp.einsum(
        "fab,fbn->fan", adjoint_block(adjoint), right_rows, preferred_element_type=jnp.float32
    )
    return quad_weight * psd_field * jnp.sum(left_rows * accumulated, axis=1)


def broadcast_body(green_panel, log_psd, observed, pair_weights):
    freq_count, comp_count, span_j, local_pts = green_panel.shape
    span_i = observed.shape[2]
    piece = log_psd.shape[2]
    row_count = lax.axis_size("row")
    col_count = lax.axis_size("col")
    pts_count = lax.axis_size("pts")
    quad_weight = 1.0 / (pts_count * local_pts)
    entry_count = freq_count * pts_count * local_pts
    pair_scale = pair_weights.astype(jnp.float32)
    group_ratio = col_count // row_count
    pieces = []
    for member in range(group_ratio):
        pieces.append(from_root(green_panel, "col", lax.axis_index("row") * group_ratio + member))
    rows_block = jnp.concatenate(pieces, axis=2).reshape(freq_count, 2 * span_i, local_pts)
    cols_block = green_panel.reshape(freq_count, 2 * span_j, local_pts)

    slot = lax.axis_index("row") * col_count + lax.axis_index("col")
    offset = slot * piece
    placed = lax.dynamic_update_slice_in_dim(
        jnp.zeros((freq_count, local_pts), jnp.float32), log_psd[0], offset, axis=1
    )
    log_field = butterfly_sum(placed, ("row", "col"))

    for _ in range(ITERS):
        psd_field = jnp.exp(log_field)
        weighted = (green_panel * psd_field[:, None, None, :]).astype(jnp.bfloat16)
        weighted = weighted.reshape(freq_count, 2 * span_j, local_pts)
        pair_sum = swap_add(correlate(rows_block, weighted), "pts")
        adjoint = (pair_scale * (quad_weight * pair_sum - observed)).astype(jnp.bfloat16)
        point_part = point_terms(adjoint, cols_block, rows_block, psd_field, quad_weight)
        gradient = butterfly_sum(point_part, ("row", "col"))
        squares = swap_add(jnp.sum(gradient * gradient), "pts")
        log_field = log_field - descent * gradient / jnp.sqrt(squares / entry_count + epsilon)

    own = lax.dynamic_slice_in_dim(log_field, offset, piece, axis=1)
    return own[None]


PAIR_PLAN = ((0, 0, 1), (1, 2, 0), (2, 0, 3), (2, 2, 1), (1, 1, 3), (3, 3, 2))


def pair_tables(blocks):
    role = [0] * (blocks * blocks)
    panel_moves = []
    needs = []
    for line, sender, receiver in PAIR_PLAN:
        role[line * blocks + receiver] = 1
        panel_moves.append((line * blocks + sender, line * blocks + receiver))
        needs.append((line * blocks + receiver, 0, receiver * blocks + sender))
        needs.append((line * blocks + receiver, 1, sender * blocks + receiver))
    for plane in range(blocks):
        role[plane * blocks + plane] = 2
    rounds = []
    moved = [[0, 0] for _ in range(blocks * blocks)]
    for dest, which, owner in needs:
        if owner == dest:
            continue
        for number, (pairs, whiches) in enumerate(rounds):
            if all(s != owner and d != dest for s, d in pairs):
                pairs.append((owner, dest))
                whiches.append((dest, which))
                moved[dest][which] = number + 1
                break
        else:
            rounds.append(([(owner, dest)], [(dest, which)]))
            moved[dest][which] = len(rounds)
    return role, panel_moves, rounds, moved


def pair_body(green_panel, log_psd, observed, pair_weights):
    freq_count, comp_count, span_j, local_pts = green_panel.shape
    piece = log_psd.shape[2]
    blocks = lax.axis_size("col")
    pts_count = lax.axis_size("pts")
    quad_weight = 1.0 / (pts_count * local_pts)
    entry_count = freq_count * pts_count * local_pts
    role, panel_moves, rounds, moved = pair_tables(blocks)
    slot = lax.axis_index("row") * blocks + lax.axis_index("col")
    my_role = jnp.array(role, jnp.int32)[slot]
    is_diag = my_role == 2
    axes = ("row", "col")

    received = lax.ppermute(green_panel, axes, panel_moves)

    own_block = jnp.concatenate(
        [observed.reshape(-1, span_j, span_j), pair_weights.astype(jnp.float32)[None]], axis=0
    )
    arrived = [own_block]
    for pairs, _ in rounds:
        arrived.append(lax.ppermute(own_block, axes, pairs))
    arrived = jnp.stack(arrived)
    received, arrived = lax.optimization_barrier((received, arrived))
    other = jnp.where(is_diag, green_panel, received)
    mine_rows = green_panel.reshape(freq_count, 2 * span_j, local_pts)
    other_rows = other.reshape(freq_count, 2 * span_j, local_pts)
    moved_table = jnp.array(moved, jnp.int32)[slot]
    first_block = arrived[moved_table[0]]
    second_block = arrived[moved_table[1]]
    obs_first = first_block[:-1].reshape(observed.shape)
    obs_second = second_block[:-1].reshape(observed.shape)
    scale_first = first_block[-1]
    scale_second = second_block[-1]
    keep_first = my_role > 0
    keep_second = my_role == 1

    offset = slot * piece
    placed = lax.dynamic_update_slice_in_dim(
        jnp.zeros((freq_count, local_pts), jnp.float32), log_psd[0], offset, axis=1
    )
    log_field = butterfly_sum(placed, axes)

    for _ in range(ITERS):
        psd_field = jnp.exp(log_field)
        spread = psd_field[:, None, None, :]
        weighted_mine = (green_panel * spread).astype(jnp.bfloat16).reshape(mine_rows.shape)
        weighted_other = (other * spread).astype(jnp.bfloat16).reshape(other_rows.shape)
        corr_first = correlate(mine_rows, weighted_other)
        corr_second = correlate(other_rows, weighted_mine)
        both = swap_add(jnp.stack([corr_first, corr_second]), "pts")
        adj_first = (scale_first * (quad_weight * both[0] - obs_first)).astype(jnp.bfloat16)
        adj_second = (scale_second * (quad_weight * both[1] - obs_second)).astype(jnp.bfloat16)
        term_first = point_terms(adj_first, other_rows, mine_rows, psd_field, quad_weight)
        term_second = point_terms(adj_second, mine_rows, other_rows, psd_field, quad_weight)
        point_part = jnp.where(keep_first, term_first, 0.0) + jnp.where(keep_second, term_second, 0.0)
        gradient = butterfly_sum(point_part, axes)
        squares = swap_add(jnp.sum(gradient * gradient), "pts")
        log_field = log_field - descent * gradient / jnp.sqrt(squares / entry_count + epsilon)

    own = lax.dynamic_slice_in_dim(log_field, offset, piece, axis=1)
    return own[None]


SPLIT_PLAN = ((0, 0, 1, 0), (0, 1, 2, 1), (0, 2, 3, 0), (1, 1, 3, 0), (2, 0, 2, 0), (3, 0, 3, 0))


def split_tables(blocks, half):
    devices = blocks * blocks
    kind = [[0, 0] for _ in range(devices)]
    first_off = [[0, 0] for _ in range(devices)]
    second_off = [[0, 0] for _ in range(devices)]
    send_off = [[0, 0] for _ in range(devices)]
    partners = [[], []]
    needs = []
    for line, plane_a, plane_b, slot in SPLIT_PLAN:
        for mine, other, part in ((plane_a, plane_b, 0), (plane_b, plane_a, half)):
            dev = line * blocks + mine
            kind[dev][slot] = 1
            first_off[dev][slot] = part
            second_off[dev][slot] = part
            send_off[dev][slot] = half - part
            partners[slot].append((dev, line * blocks + other))
            needs.append((dev, slot * 2, mine * blocks + other))
            needs.append((dev, slot * 2 + 1, other * blocks + mine))
    for plane in range(blocks):
        dev = plane * blocks + plane
        kind[dev][1] = 2
        second_off[dev][1] = half
    rounds = []
    moved = [[0] * 4 for _ in range(devices)]
    for dest, which, owner in needs:
        if owner == dest:
            continue
        for number, pairs in enumerate(rounds):
            if all(s != owner and d != dest for s, d in pairs):
                pairs.append((owner, dest))
                moved[dest][which] = number + 1
                break
        else:
            rounds.append([(owner, dest)])
            moved[dest][which] = len(rounds)
    return kind, first_off, second_off, send_off, partners, rounds, moved


def split_body(green_panel, log_psd, observed, pair_weights):
    freq_count, comp_count, span_j, local_pts = green_panel.shape
    piece = log_psd.shape[2]
    blocks = lax.axis_size("col")
    pts_count = lax.axis_size("pts")
    half = local_pts // 2
    quad_weight = 1.0 / (pts_count * local_pts)
    entry_count = freq_count * pts_count * local_pts
    kind, first_off, second_off, send_off, partners, rounds, moved = split_tables(blocks, half)
    slot = lax.axis_index("row") * blocks + lax.axis_index("col")
    axes = ("row", "col")
    slot_count = 2

    def pick(table):
        return jnp.array(table, jnp.int32)[slot]

    my_kind, my_first, my_second, my_send = pick(kind), pick(first_off), pick(second_off), pick(send_off)

    def part(array, start):
        return lax.dynamic_slice_in_dim(array, start, half, axis=array.ndim - 1)

    received = []
    for s in range(slot_count):
        received.append(lax.ppermute(part(green_panel, my_send[s]), axes, partners[s]))

    own_block = jnp.concatenate(
        [observed.reshape(-1, span_j, span_j), pair_weights.astype(jnp.float32)[None]], axis=0
    )
    arrived = [own_block]
    for pairs in rounds:
        arrived.append(lax.ppermute(own_block, axes, pairs))
    arrived = jnp.stack(arrived)
    received, arrived = lax.optimization_barrier((received, arrived))
    my_moved = pick(moved)

    def rows(array):
        return array.reshape(freq_count, 2 * span_j, half)

    units = []
    for s in range(slot_count):
        is_diag = my_kind[s] == 2
        left_a = part(green_panel, my_first[s])
        own_b = part(green_panel, my_second[s])
        right_a = jnp.where(is_diag, left_a, received[s])
        left_b = jnp.where(is_diag, own_b, received[s])
        right_b = jnp.where(is_diag, own_b, left_a)
        blocks_in = []
        for which in range(2):
            block = arrived[my_moved[s * 2 + which]]
            blocks_in.append((block[:-1].reshape(observed.shape), block[-1]))
        units.append((is_diag, my_kind[s] > 0, left_a, right_a, left_b, right_b, blocks_in))

    offset = slot * piece
    placed = lax.dynamic_update_slice_in_dim(
        jnp.zeros((freq_count, local_pts), jnp.float32), log_psd[0], offset, axis=1
    )
    log_field = butterfly_sum(placed, axes)

    for _ in range(ITERS):
        psd_field = jnp.exp(log_field)
        partials = []
        fields = []
        for s, (is_diag, keep, left_a, right_a, left_b, right_b, blocks_in) in enumerate(units):
            field_a = part(psd_field, my_first[s])
            field_b = part(psd_field, my_second[s])
            weighted_a = (right_a * field_a[:, None, None, :]).astype(jnp.bfloat16)
            weighted_b = (right_b * field_b[:, None, None, :]).astype(jnp.bfloat16)
            partials.append(correlate(rows(left_a), rows(weighted_a)))
            partials.append(correlate(rows(left_b), rows(weighted_b)))
            fields.append((field_a, field_b))
        summed = swap_add(jnp.stack(partials), "pts")
        grad_a = jnp.zeros((freq_count, half), jnp.float32)
        grad_b = jnp.zeros((freq_count, half), jnp.float32)
        for s, (is_diag, keep, left_a, right_a, left_b, right_b, blocks_in) in enumerate(units):
            corr_a, corr_b = summed[2 * s], summed[2 * s + 1]
            got = lax.ppermute(summed[2 * s: 2 * s + 2], axes, partners[s])
            total_a = corr_a + jnp.where(is_diag, corr_b, got[1])
            total_b = corr_b + jnp.where(is_diag, corr_a, got[0])
            (obs_a, scale_a), (obs_b, scale_b) = blocks_in
            adj_a = (scale_a * (quad_weight * total_a - obs_a)).astype(jnp.bfloat16)
            adj_b = (scale_b * (quad_weight * total_b - obs_b)).astype(jnp.bfloat16)
            field_a, field_b = fields[s]
            term_a = point_terms(adj_a, rows(right_a), rows(left_a), field_a, quad_weight)
            term_b = point_terms(adj_b, rows(right_b), rows(left_b), field_b, quad_weight)
            term_a = jnp.where(keep, term_a, 0.0)
            term_b = jnp.where(keep, term_b, 0.0)
            at_a = my_first[s] == 0
            at_b = my_second[s] == 0
            grad_a = grad_a + jnp.where(at_a, term_a, 0.0) + jnp.where(at_b, term_b, 0.0)
            grad_b = grad_b + jnp.where(at_a, 0.0, term_a) + jnp.where(at_b, 0.0, term_b)
        point_part = jnp.concatenate([grad_a, grad_b], axis=1)
        gradient = butterfly_sum(point_part, axes)
        squares = swap_add(jnp.sum(gradient * gradient), "pts")
        log_field = log_field - descent * gradient / jnp.sqrt(squares / entry_count + epsilon)

    own = lax.dynamic_slice_in_dim(log_field, offset, piece, axis=1)
    return own[None]


def solution(mesh):
    shape = mesh.shape
    plan_fits = shape["row"] == 4 and shape["col"] == 4 and shape["pts"] == 2
    return jax.shard_map(
        split_body if plan_fits else broadcast_body,
        mesh=mesh,
        in_specs=(
            P(None, None, "col", "pts"),
            P("pts", None, ("row", "col")),
            P(None, None, "row", "col"),
            P("row", "col"),
        ),
        out_specs=P("pts", None, ("row", "col")),
        check_vma=False,
    )
```

```python
import jax
import jax.numpy as jnp
from jax import lax
from jax.sharding import PartitionSpec as P

ITERS = 2


epsilon = 1e-06
descent = 0.1


def from_root(block, axis, source):
    block = jnp.where(lax.axis_index(axis) == source, block, jnp.zeros_like(block))
    return lax.psum(block, axis)


def butterfly_sum(value, axes):
    for axis in axes:
        size = lax.axis_size(axis)
        if size & (size - 1):
            value = lax.psum(value, axis)
            continue
        me = lax.axis_index(axis)
        bit = 1
        while bit < size:
            radix = 4 if bit * 4 <= size else 2
            got = [value]
            for m in range(1, radix):
                mask = m * bit
                got.append(lax.ppermute(value, axis, [(i, i ^ mask) for i in range(size)]))
            stacked = jnp.stack(got)
            local = (me // bit) % radix
            ordered = [stacked[local ^ j] for j in range(radix)]
            if radix == 4:
                value = (ordered[0] + ordered[1]) + (ordered[2] + ordered[3])
            else:
                value = ordered[0] + ordered[1]
            bit *= radix
    return value


def swap_add(value, axis):
    size = lax.axis_size(axis)
    if size != 2:
        return lax.psum(value, axis)
    return value + lax.ppermute(value, axis, [(0, 1), (1, 0)])


def correlate(left_rows, weighted):
    half_a = left_rows.shape[1] // 2
    half_b = weighted.shape[1] // 2
    products = jnp.einsum("fan,fbn->fab", left_rows, weighted, preferred_element_type=jnp.float32)
    corr_real = products[:, :half_a, :half_b] + products[:, half_a:, half_b:]
    corr_imag = products[:, half_a:, :half_b] - products[:, :half_a, half_b:]
    return jnp.stack([corr_real, corr_imag], axis=1)


def adjoint_block(adjoint):
    adj_real = adjoint[:, 0]
    adj_imag = adjoint[:, 1]
    top_half = jnp.concatenate([adj_real, -adj_imag], axis=2)
    low_half = jnp.concatenate([adj_imag, adj_real], axis=2)
    return jnp.concatenate([top_half, low_half], axis=1)


def point_terms(adjoint, right_rows, left_rows, psd_field, quad_weight):
    accumulated = jnp.einsum(
        "fab,fbn->fan", adjoint_block(adjoint), right_rows, preferred_element_type=jnp.float32
    )
    return quad_weight * psd_field * jnp.sum(left_rows * accumulated, axis=1)


def broadcast_body(green_panel, log_psd, observed, pair_weights):
    freq_count, comp_count, span_j, local_pts = green_panel.shape
    span_i = observed.shape[2]
    piece = log_psd.shape[2]
    row_count = lax.axis_size("row")
    col_count = lax.axis_size("col")
    pts_count = lax.axis_size("pts")
    quad_weight = 1.0 / (pts_count * local_pts)
    entry_count = freq_count * pts_count * local_pts
    pair_scale = pair_weights.astype(jnp.float32)
    group_ratio = col_count // row_count
    pieces = []
    for member in range(group_ratio):
        pieces.append(from_root(green_panel, "col", lax.axis_index("row") * group_ratio + member))
    rows_block = jnp.concatenate(pieces, axis=2).reshape(freq_count, 2 * span_i, local_pts)
    cols_block = green_panel.reshape(freq_count, 2 * span_j, local_pts)

    slot = lax.axis_index("row") * col_count + lax.axis_index("col")
    offset = slot * piece
    placed = lax.dynamic_update_slice_in_dim(
        jnp.zeros((freq_count, local_pts), jnp.float32), log_psd[0], offset, axis=1
    )
    log_field = butterfly_sum(placed, ("row", "col"))

    for _ in range(ITERS):
        psd_field = jnp.exp(log_field)
        weighted = (green_panel * psd_field[:, None, None, :]).astype(jnp.bfloat16)
        weighted = weighted.reshape(freq_count, 2 * span_j, local_pts)
        pair_sum = swap_add(correlate(rows_block, weighted), "pts")
        adjoint = (pair_scale * (quad_weight * pair_sum - observed)).astype(jnp.bfloat16)
        point_part = point_terms(adjoint, cols_block, rows_block, psd_field, quad_weight)
        gradient = butterfly_sum(point_part, ("row", "col"))
        squares = swap_add(jnp.sum(gradient * gradient), "pts")
        log_field = log_field - descent * gradient / jnp.sqrt(squares / entry_count + epsilon)

    own = lax.dynamic_slice_in_dim(log_field, offset, piece, axis=1)
    return own[None]


PAIR_PLAN = ((0, 0, 1), (1, 2, 0), (2, 0, 3), (2, 2, 1), (1, 1, 3), (3, 3, 2))


def pair_tables(blocks):
    role = [0] * (blocks * blocks)
    panel_moves = []
    needs = []
    for line, sender, receiver in PAIR_PLAN:
        role[line * blocks + receiver] = 1
        panel_moves.append((line * blocks + sender, line * blocks + receiver))
        needs.append((line * blocks + receiver, 0, receiver * blocks + sender))
        needs.append((line * blocks + receiver, 1, sender * blocks + receiver))
    for plane in range(blocks):
        role[plane * blocks + plane] = 2
    rounds = []
    moved = [[0, 0] for _ in range(blocks * blocks)]
    for dest, which, owner in needs:
        if owner == dest:
            continue
        for number, (pairs, whiches) in enumerate(rounds):
            if all(s != owner and d != dest for s, d in pairs):
                pairs.append((owner, dest))
                whiches.append((dest, which))
                moved[dest][which] = number + 1
                break
        else:
            rounds.append(([(owner, dest)], [(dest, which)]))
            moved[dest][which] = len(rounds)
    return role, panel_moves, rounds, moved


def pair_body(green_panel, log_psd, observed, pair_weights):
    freq_count, comp_count, span_j, local_pts = green_panel.shape
    piece = log_psd.shape[2]
    blocks = lax.axis_size("col")
    pts_count = lax.axis_size("pts")
    quad_weight = 1.0 / (pts_count * local_pts)
    entry_count = freq_count * pts_count * local_pts
    role, panel_moves, rounds, moved = pair_tables(blocks)
    slot = lax.axis_index("row") * blocks + lax.axis_index("col")
    my_role = jnp.array(role, jnp.int32)[slot]
    is_diag = my_role == 2
    axes = ("row", "col")

    received = lax.ppermute(green_panel, axes, panel_moves)

    own_block = jnp.concatenate(
        [observed.reshape(-1, span_j, span_j), pair_weights.astype(jnp.float32)[None]], axis=0
    )
    arrived = [own_block]
    for pairs, _ in rounds:
        arrived.append(lax.ppermute(own_block, axes, pairs))
    arrived = jnp.stack(arrived)
    received, arrived = lax.optimization_barrier((received, arrived))
    other = jnp.where(is_diag, green_panel, received)
    mine_rows = green_panel.reshape(freq_count, 2 * span_j, local_pts)
    other_rows = other.reshape(freq_count, 2 * span_j, local_pts)
    moved_table = jnp.array(moved, jnp.int32)[slot]
    first_block = arrived[moved_table[0]]
    second_block = arrived[moved_table[1]]
    obs_first = first_block[:-1].reshape(observed.shape)
    obs_second = second_block[:-1].reshape(observed.shape)
    scale_first = first_block[-1]
    scale_second = second_block[-1]
    keep_first = my_role > 0
    keep_second = my_role == 1

    offset = slot * piece
    placed = lax.dynamic_update_slice_in_dim(
        jnp.zeros((freq_count, local_pts), jnp.float32), log_psd[0], offset, axis=1
    )
    log_field = butterfly_sum(placed, axes)

    for _ in range(ITERS):
        psd_field = jnp.exp(log_field)
        spread = psd_field[:, None, None, :]
        weighted_mine = (green_panel * spread).astype(jnp.bfloat16).reshape(mine_rows.shape)
        weighted_other = (other * spread).astype(jnp.bfloat16).reshape(other_rows.shape)
        corr_first = correlate(mine_rows, weighted_other)
        corr_second = correlate(other_rows, weighted_mine)
        both = swap_add(jnp.stack([corr_first, corr_second]), "pts")
        adj_first = (scale_first * (quad_weight * both[0] - obs_first)).astype(jnp.bfloat16)
        adj_second = (scale_second * (quad_weight * both[1] - obs_second)).astype(jnp.bfloat16)
        term_first = point_terms(adj_first, other_rows, mine_rows, psd_field, quad_weight)
        term_second = point_terms(adj_second, mine_rows, other_rows, psd_field, quad_weight)
        point_part = jnp.where(keep_first, term_first, 0.0) + jnp.where(keep_second, term_second, 0.0)
        gradient = butterfly_sum(point_part, axes)
        squares = swap_add(jnp.sum(gradient * gradient), "pts")
        log_field = log_field - descent * gradient / jnp.sqrt(squares / entry_count + epsilon)

    own = lax.dynamic_slice_in_dim(log_field, offset, piece, axis=1)
    return own[None]


SPLIT_PLAN = ((0, 0, 1, 0), (0, 1, 2, 1), (0, 2, 3, 0), (1, 1, 3, 0), (2, 0, 2, 0), (3, 0, 3, 0))


def split_tables(blocks, half):
    devices = blocks * blocks
    kind = [[0, 0] for _ in range(devices)]
    first_off = [[0, 0] for _ in range(devices)]
    second_off = [[0, 0] for _ in range(devices)]
    send_off = [[0, 0] for _ in range(devices)]
    partners = [[], []]
    needs = []
    for line, plane_a, plane_b, slot in SPLIT_PLAN:
        for mine, other, part in ((plane_a, plane_b, 0), (plane_b, plane_a, half)):
            dev = line * blocks + mine
            kind[dev][slot] = 1
            first_off[dev][slot] = part
            second_off[dev][slot] = part
            send_off[dev][slot] = half - part
            partners[slot].append((dev, line * blocks + other))
            needs.append((dev, slot * 2, mine * blocks + other))
            needs.append((dev, slot * 2 + 1, other * blocks + mine))
    for plane in range(blocks):
        dev = plane * blocks + plane
        kind[dev][1] = 2
        second_off[dev][1] = half
    rounds = []
    moved = [[0] * 4 for _ in range(devices)]
    for dest, which, owner in needs:
        if owner == dest:
            continue
        for number, pairs in enumerate(rounds):
            if all(s != owner and d != dest for s, d in pairs):
                pairs.append((owner, dest))
                moved[dest][which] = number + 1
                break
        else:
            rounds.append([(owner, dest)])
            moved[dest][which] = len(rounds)
    return kind, first_off, second_off, send_off, partners, rounds, moved


def split_body(green_panel, log_psd, observed, pair_weights):
    freq_count, comp_count, span_j, local_pts = green_panel.shape
    piece = log_psd.shape[2]
    blocks = lax.axis_size("col")
    pts_count = lax.axis_size("pts")
    half = local_pts // 2
    quad_weight = 1.0 / (pts_count * local_pts)
    entry_count = freq_count * pts_count * local_pts
    kind, first_off, second_off, send_off, partners, rounds, moved = split_tables(blocks, half)
    slot = lax.axis_index("row") * blocks + lax.axis_index("col")
    axes = ("row", "col")
    slot_count = 2

    def pick(table):
        return jnp.array(table, jnp.int32)[slot]

    my_kind, my_first, my_second, my_send = pick(kind), pick(first_off), pick(second_off), pick(send_off)

    def part(array, start):
        return lax.dynamic_slice_in_dim(array, start, half, axis=array.ndim - 1)

    received = []
    for s in range(slot_count):
        received.append(lax.ppermute(part(green_panel, my_send[s]), axes, partners[s]))

    own_block = jnp.concatenate(
        [observed.reshape(-1, span_j, span_j), pair_weights.astype(jnp.float32)[None]], axis=0
    )
    arrived = [own_block]
    for pairs in rounds:
        arrived.append(lax.ppermute(own_block, axes, pairs))
    arrived = jnp.stack(arrived)
    received, arrived = lax.optimization_barrier((received, arrived))
    my_moved = pick(moved)

    def rows(array):
        return array.reshape(freq_count, 2 * span_j, half)

    units = []
    for s in range(slot_count):
        is_diag = my_kind[s] == 2
        left_a = part(green_panel, my_first[s])
        own_b = part(green_panel, my_second[s])
        right_a = jnp.where(is_diag, left_a, received[s])
        left_b = jnp.where(is_diag, own_b, received[s])
        right_b = jnp.where(is_diag, own_b, left_a)
        blocks_in = []
        for which in range(2):
            block = arrived[my_moved[s * 2 + which]]
            blocks_in.append((block[:-1].reshape(observed.shape), block[-1]))
        units.append((is_diag, my_kind[s] > 0, left_a, right_a, left_b, right_b, blocks_in))

    offset = slot * piece
    placed = lax.dynamic_update_slice_in_dim(
        jnp.zeros((freq_count, local_pts), jnp.float32), log_psd[0], offset, axis=1
    )
    log_field = butterfly_sum(placed, axes)

    def run_sweep(sweep_idx, log_field):
        psd_field = jnp.exp(log_field)
        partials = []
        fields = []
        for s, (is_diag, keep, left_a, right_a, left_b, right_b, blocks_in) in enumerate(units):
            field_a = part(psd_field, my_first[s])
            field_b = part(psd_field, my_second[s])
            weighted_a = (right_a * field_a[:, None, None, :]).astype(jnp.bfloat16)
            weighted_b = (right_b * field_b[:, None, None, :]).astype(jnp.bfloat16)
            partials.append(correlate(rows(left_a), rows(weighted_a)))
            partials.append(correlate(rows(left_b), rows(weighted_b)))
            fields.append((field_a, field_b))
        summed = swap_add(jnp.stack(partials), "pts")
        grad_a = jnp.zeros((freq_count, half), jnp.float32)
        grad_b = jnp.zeros((freq_count, half), jnp.float32)
        for s, (is_diag, keep, left_a, right_a, left_b, right_b, blocks_in) in enumerate(units):
            corr_a, corr_b = summed[2 * s], summed[2 * s + 1]
            got = lax.ppermute(summed[2 * s: 2 * s + 2], axes, partners[s])
            total_a = corr_a + jnp.where(is_diag, corr_b, got[1])
            total_b = corr_b + jnp.where(is_diag, corr_a, got[0])
            (obs_a, scale_a), (obs_b, scale_b) = blocks_in
            adj_a = (scale_a * (quad_weight * total_a - obs_a)).astype(jnp.bfloat16)
            adj_b = (scale_b * (quad_weight * total_b - obs_b)).astype(jnp.bfloat16)
            field_a, field_b = fields[s]
            term_a = point_terms(adj_a, rows(right_a), rows(left_a), field_a, quad_weight)
            term_b = point_terms(adj_b, rows(right_b), rows(left_b), field_b, quad_weight)
            term_a = jnp.where(keep, term_a, 0.0)
            term_b = jnp.where(keep, term_b, 0.0)
            at_a = my_first[s] == 0
            at_b = my_second[s] == 0
            grad_a = grad_a + jnp.where(at_a, term_a, 0.0) + jnp.where(at_b, term_b, 0.0)
            grad_b = grad_b + jnp.where(at_a, 0.0, term_a) + jnp.where(at_b, 0.0, term_b)
        point_part = jnp.concatenate([grad_a, grad_b], axis=1)
        gradient = butterfly_sum(point_part, axes)
        squares = swap_add(jnp.sum(gradient * gradient), "pts")
        return log_field - descent * gradient / jnp.sqrt(squares / entry_count + epsilon)

    log_field = lax.fori_loop(0, ITERS, run_sweep, log_field)
    own = lax.dynamic_slice_in_dim(log_field, offset, piece, axis=1)
    return own[None]


def solution(mesh):
    shape = mesh.shape
    plan_fits = shape["row"] == 4 and shape["col"] == 4 and shape["pts"] == 2
    return jax.shard_map(
        split_body if plan_fits else broadcast_body,
        mesh=mesh,
        in_specs=(
            P(None, None, "col", "pts"),
            P("pts", None, ("row", "col")),
            P(None, None, "row", "col"),
            P("row", "col"),
        ),
        out_specs=P("pts", None, ("row", "col")),
        check_vma=False,
    )
```

```python
import jax
import jax.numpy as jnp
from jax import lax
from jax.sharding import PartitionSpec as P

ITERS = 2


epsilon = 1e-06
descent = 0.1


def from_root(block, axis, source):
    block = jnp.where(lax.axis_index(axis) == source, block, jnp.zeros_like(block))
    return lax.psum(block, axis)


def butterfly_sum(value, axes):
    for axis in axes:
        size = lax.axis_size(axis)
        if size & (size - 1):
            value = lax.psum(value, axis)
            continue
        me = lax.axis_index(axis)
        bit = 1
        while bit < size:
            radix = 4 if bit * 4 <= size else 2
            got = [value]
            for m in range(1, radix):
                mask = m * bit
                got.append(lax.ppermute(value, axis, [(i, i ^ mask) for i in range(size)]))
            stacked = jnp.stack(got)
            local = (me // bit) % radix
            ordered = [stacked[local ^ j] for j in range(radix)]
            if radix == 4:
                value = (ordered[0] + ordered[1]) + (ordered[2] + ordered[3])
            else:
                value = ordered[0] + ordered[1]
            bit *= radix
    return value


def swap_add(value, axis):
    size = lax.axis_size(axis)
    if size != 2:
        return lax.psum(value, axis)
    return value + lax.ppermute(value, axis, [(0, 1), (1, 0)])


def correlate(left_rows, weighted):
    half_a = left_rows.shape[1] // 2
    half_b = weighted.shape[1] // 2
    products = jnp.einsum("fan,fbn->fab", left_rows, weighted, preferred_element_type=jnp.float32)
    corr_real = products[:, :half_a, :half_b] + products[:, half_a:, half_b:]
    corr_imag = products[:, half_a:, :half_b] - products[:, :half_a, half_b:]
    return jnp.stack([corr_real, corr_imag], axis=1)


def adjoint_block(adjoint):
    adj_real = adjoint[:, 0]
    adj_imag = adjoint[:, 1]
    top_half = jnp.concatenate([adj_real, -adj_imag], axis=2)
    low_half = jnp.concatenate([adj_imag, adj_real], axis=2)
    return jnp.concatenate([top_half, low_half], axis=1)


def point_terms(adjoint, right_rows, left_rows, psd_field, quad_weight):
    accumulated = jnp.einsum(
        "fab,fbn->fan", adjoint_block(adjoint), right_rows, preferred_element_type=jnp.float32
    )
    return quad_weight * psd_field * jnp.sum(left_rows * accumulated, axis=1)


def broadcast_body(green_panel, log_psd, observed, pair_weights):
    freq_count, comp_count, span_j, local_pts = green_panel.shape
    span_i = observed.shape[2]
    piece = log_psd.shape[2]
    row_count = lax.axis_size("row")
    col_count = lax.axis_size("col")
    pts_count = lax.axis_size("pts")
    quad_weight = 1.0 / (pts_count * local_pts)
    entry_count = freq_count * pts_count * local_pts
    pair_scale = pair_weights.astype(jnp.float32)
    group_ratio = col_count // row_count
    pieces = []
    for member in range(group_ratio):
        pieces.append(from_root(green_panel, "col", lax.axis_index("row") * group_ratio + member))
    rows_block = jnp.concatenate(pieces, axis=2).reshape(freq_count, 2 * span_i, local_pts)
    cols_block = green_panel.reshape(freq_count, 2 * span_j, local_pts)

    slot = lax.axis_index("row") * col_count + lax.axis_index("col")
    offset = slot * piece
    placed = lax.dynamic_update_slice_in_dim(
        jnp.zeros((freq_count, local_pts), jnp.float32), log_psd[0], offset, axis=1
    )
    log_field = butterfly_sum(placed, ("row", "col"))

    for _ in range(ITERS):
        psd_field = jnp.exp(log_field)
        weighted = (green_panel * psd_field[:, None, None, :]).astype(jnp.bfloat16)
        weighted = weighted.reshape(freq_count, 2 * span_j, local_pts)
        pair_sum = swap_add(correlate(rows_block, weighted), "pts")
        adjoint = (pair_scale * (quad_weight * pair_sum - observed)).astype(jnp.bfloat16)
        point_part = point_terms(adjoint, cols_block, rows_block, psd_field, quad_weight)
        gradient = butterfly_sum(point_part, ("row", "col"))
        squares = swap_add(jnp.sum(gradient * gradient), "pts")
        log_field = log_field - descent * gradient / jnp.sqrt(squares / entry_count + epsilon)

    own = lax.dynamic_slice_in_dim(log_field, offset, piece, axis=1)
    return own[None]


PAIR_PLAN = ((0, 0, 1), (1, 2, 0), (2, 0, 3), (2, 2, 1), (1, 1, 3), (3, 3, 2))


def pair_tables(blocks):
    role = [0] * (blocks * blocks)
    panel_moves = []
    needs = []
    for line, sender, receiver in PAIR_PLAN:
        role[line * blocks + receiver] = 1
        panel_moves.append((line * blocks + sender, line * blocks + receiver))
        needs.append((line * blocks + receiver, 0, receiver * blocks + sender))
        needs.append((line * blocks + receiver, 1, sender * blocks + receiver))
    busy = {s for s, _ in panel_moves} | {d for _, d in panel_moves}
    for plane in range(blocks):
        role[plane * blocks + plane] = 2
        free = [line for line in range(blocks) if line * blocks + plane not in busy]
        panel_moves.append((free[0] * blocks + plane, plane * blocks + plane))
        busy.add(free[0] * blocks + plane)
    rounds = []
    moved = [[0, 0] for _ in range(blocks * blocks)]
    for dest, which, owner in needs:
        if owner == dest:
            continue
        for number, (pairs, whiches) in enumerate(rounds):
            if all(s != owner and d != dest for s, d in pairs):
                pairs.append((owner, dest))
                whiches.append((dest, which))
                moved[dest][which] = number + 1
                break
        else:
            rounds.append(([(owner, dest)], [(dest, which)]))
            moved[dest][which] = len(rounds)
    return role, panel_moves, rounds, moved


def pair_body(green_panel, log_psd, observed, pair_weights):
    freq_count, comp_count, span_j, local_pts = green_panel.shape
    piece = log_psd.shape[2]
    blocks = lax.axis_size("col")
    pts_count = lax.axis_size("pts")
    quad_weight = 1.0 / (pts_count * local_pts)
    entry_count = freq_count * pts_count * local_pts
    role, panel_moves, rounds, moved = pair_tables(blocks)
    slot = lax.axis_index("row") * blocks + lax.axis_index("col")
    my_role = jnp.array(role, jnp.int32)[slot]
    is_diag = my_role == 2
    axes = ("row", "col")

    received = lax.ppermute(green_panel, axes, panel_moves)

    own_block = jnp.concatenate(
        [observed.reshape(-1, span_j, span_j), pair_weights.astype(jnp.float32)[None]], axis=0
    )
    arrived = [own_block]
    for pairs, _ in rounds:
        arrived.append(lax.ppermute(own_block, axes, pairs))
    arrived = jnp.stack(arrived)
    received, arrived = lax.optimization_barrier((received, arrived))
    other = received
    mine_rows = green_panel.reshape(freq_count, 2 * span_j, local_pts)
    other_rows = other.reshape(freq_count, 2 * span_j, local_pts)
    moved_table = jnp.array(moved, jnp.int32)[slot]
    first_block = arrived[moved_table[0]]
    second_block = arrived[moved_table[1]]
    obs_first = first_block[:-1].reshape(observed.shape)
    obs_second = second_block[:-1].reshape(observed.shape)
    scale_first = first_block[-1]
    scale_second = second_block[-1]
    keep_first = my_role > 0
    keep_second = my_role == 1

    offset = slot * piece
    placed = lax.dynamic_update_slice_in_dim(
        jnp.zeros((freq_count, local_pts), jnp.float32), log_psd[0], offset, axis=1
    )
    log_field = butterfly_sum(placed, axes)

    for _ in range(ITERS):
        psd_field = jnp.exp(log_field)
        spread = psd_field[:, None, None, :]
        weighted_mine = (green_panel * spread).astype(jnp.bfloat16).reshape(mine_rows.shape)
        weighted_other = (other * spread).astype(jnp.bfloat16).reshape(other_rows.shape)
        corr_first = correlate(mine_rows, weighted_other)
        corr_second = correlate(other_rows, weighted_mine)
        both = swap_add(jnp.stack([corr_first, corr_second]), "pts")
        adj_first = (scale_first * (quad_weight * both[0] - obs_first)).astype(jnp.bfloat16)
        adj_second = (scale_second * (quad_weight * both[1] - obs_second)).astype(jnp.bfloat16)
        term_first = point_terms(adj_first, other_rows, mine_rows, psd_field, quad_weight)
        term_second = point_terms(adj_second, mine_rows, other_rows, psd_field, quad_weight)
        point_part = jnp.where(keep_first, term_first, 0.0) + jnp.where(keep_second, term_second, 0.0)
        gradient = butterfly_sum(point_part, axes)
        squares = swap_add(jnp.sum(gradient * gradient), "pts")
        log_field = log_field - descent * gradient / jnp.sqrt(squares / entry_count + epsilon)

    own = lax.dynamic_slice_in_dim(log_field, offset, piece, axis=1)
    return own[None]


def solution(mesh):
    shape = mesh.shape
    plan_fits = shape["row"] == 4 and shape["col"] == 4 and shape["pts"] == 2
    return jax.shard_map(
        pair_body if plan_fits else broadcast_body,
        mesh=mesh,
        in_specs=(
            P(None, None, "col", "pts"),
            P("pts", None, ("row", "col")),
            P(None, None, "row", "col"),
            P("row", "col"),
        ),
        out_specs=P("pts", None, ("row", "col")),
        check_vma=False,
    )
```

```python
import jax
import jax.numpy as jnp
from jax import lax
from jax.sharding import PartitionSpec as P

ITERS = 2


epsilon = 1e-06
descent = 0.1


def from_root(block, axis, source):
    block = jnp.where(lax.axis_index(axis) == source, block, jnp.zeros_like(block))
    return lax.psum(block, axis)


def butterfly_sum(value, axes):
    for axis in axes:
        size = lax.axis_size(axis)
        if size & (size - 1):
            value = lax.psum(value, axis)
            continue
        me = lax.axis_index(axis)
        bit = 1
        while bit < size:
            radix = 4 if bit * 4 <= size else 2
            got = [value]
            for m in range(1, radix):
                mask = m * bit
                got.append(lax.ppermute(value, axis, [(i, i ^ mask) for i in range(size)]))
            stacked = jnp.stack(got)
            local = (me // bit) % radix
            ordered = [stacked[local ^ j] for j in range(radix)]
            if radix == 4:
                value = (ordered[0] + ordered[1]) + (ordered[2] + ordered[3])
            else:
                value = ordered[0] + ordered[1]
            bit *= radix
    return value


def swap_add(value, axis):
    size = lax.axis_size(axis)
    if size != 2:
        return lax.psum(value, axis)
    return value + lax.ppermute(value, axis, [(0, 1), (1, 0)])


def correlate(left_rows, weighted):
    half_a = left_rows.shape[1] // 2
    half_b = weighted.shape[1] // 2
    products = jnp.einsum("fan,fbn->fab", left_rows, weighted, preferred_element_type=jnp.float32)
    corr_real = products[:, :half_a, :half_b] + products[:, half_a:, half_b:]
    corr_imag = products[:, half_a:, :half_b] - products[:, :half_a, half_b:]
    return jnp.stack([corr_real, corr_imag], axis=1)


def adjoint_block(adjoint):
    adj_real = adjoint[:, 0]
    adj_imag = adjoint[:, 1]
    top_half = jnp.concatenate([adj_real, -adj_imag], axis=2)
    low_half = jnp.concatenate([adj_imag, adj_real], axis=2)
    return jnp.concatenate([top_half, low_half], axis=1)


def point_terms(adjoint, right_rows, left_rows, psd_field, quad_weight):
    accumulated = jnp.einsum(
        "fab,fbn->fan", adjoint_block(adjoint), right_rows, preferred_element_type=jnp.float32
    )
    return quad_weight * psd_field * jnp.sum(left_rows * accumulated, axis=1)


def broadcast_body(green_panel, log_psd, observed, pair_weights):
    freq_count, comp_count, span_j, local_pts = green_panel.shape
    span_i = observed.shape[2]
    piece = log_psd.shape[2]
    row_count = lax.axis_size("row")
    col_count = lax.axis_size("col")
    pts_count = lax.axis_size("pts")
    quad_weight = 1.0 / (pts_count * local_pts)
    entry_count = freq_count * pts_count * local_pts
    pair_scale = pair_weights.astype(jnp.float32)
    group_ratio = col_count // row_count
    pieces = []
    for member in range(group_ratio):
        pieces.append(from_root(green_panel, "col", lax.axis_index("row") * group_ratio + member))
    rows_block = jnp.concatenate(pieces, axis=2).reshape(freq_count, 2 * span_i, local_pts)
    cols_block = green_panel.reshape(freq_count, 2 * span_j, local_pts)

    slot = lax.axis_index("row") * col_count + lax.axis_index("col")
    offset = slot * piece
    placed = lax.dynamic_update_slice_in_dim(
        jnp.zeros((freq_count, local_pts), jnp.float32), log_psd[0], offset, axis=1
    )
    log_field = butterfly_sum(placed, ("row", "col"))

    for _ in range(ITERS):
        psd_field = jnp.exp(log_field)
        weighted = (green_panel * psd_field[:, None, None, :]).astype(jnp.bfloat16)
        weighted = weighted.reshape(freq_count, 2 * span_j, local_pts)
        pair_sum = swap_add(correlate(rows_block, weighted), "pts")
        adjoint = (pair_scale * (quad_weight * pair_sum - observed)).astype(jnp.bfloat16)
        point_part = point_terms(adjoint, cols_block, rows_block, psd_field, quad_weight)
        gradient = butterfly_sum(point_part, ("row", "col"))
        squares = swap_add(jnp.sum(gradient * gradient), "pts")
        log_field = log_field - descent * gradient / jnp.sqrt(squares / entry_count + epsilon)

    own = lax.dynamic_slice_in_dim(log_field, offset, piece, axis=1)
    return own[None]


PAIR_PLAN = ((0, 0, 1), (1, 2, 0), (2, 0, 3), (2, 2, 1), (1, 1, 3), (3, 3, 2))


def pair_tables(blocks):
    role = [0] * (blocks * blocks)
    panel_moves = []
    needs = []
    for line, sender, receiver in PAIR_PLAN:
        role[line * blocks + receiver] = 1
        panel_moves.append((line * blocks + sender, line * blocks + receiver))
        needs.append((line * blocks + receiver, 0, receiver * blocks + sender))
        needs.append((line * blocks + receiver, 1, sender * blocks + receiver))
    for plane in range(blocks):
        role[plane * blocks + plane] = 2
    rounds = []
    moved = [[0, 0] for _ in range(blocks * blocks)]
    for dest, which, owner in needs:
        if owner == dest:
            continue
        for number, (pairs, whiches) in enumerate(rounds):
            if all(s != owner and d != dest for s, d in pairs):
                pairs.append((owner, dest))
                whiches.append((dest, which))
                moved[dest][which] = number + 1
                break
        else:
            rounds.append(([(owner, dest)], [(dest, which)]))
            moved[dest][which] = len(rounds)
    return role, panel_moves, rounds, moved


def pair_body(green_panel, log_psd, observed, pair_weights):
    freq_count, comp_count, span_j, local_pts = green_panel.shape
    piece = log_psd.shape[2]
    blocks = lax.axis_size("col")
    pts_count = lax.axis_size("pts")
    quad_weight = 1.0 / (pts_count * local_pts)
    entry_count = freq_count * pts_count * local_pts
    role, panel_moves, rounds, moved = pair_tables(blocks)
    slot = lax.axis_index("row") * blocks + lax.axis_index("col")
    my_role = jnp.array(role, jnp.int32)[slot]
    is_diag = my_role == 2
    axes = ("row", "col")

    received = lax.ppermute(green_panel, axes, panel_moves)

    own_block = jnp.concatenate(
        [observed.reshape(-1, span_j, span_j), pair_weights.astype(jnp.float32)[None]], axis=0
    )
    arrived = [own_block]
    for pairs, _ in rounds:
        arrived.append(lax.ppermute(own_block, axes, pairs))
    arrived = jnp.stack(arrived)
    received, arrived = lax.optimization_barrier((received, arrived))
    other = jnp.where(is_diag, green_panel, received)
    mine_rows = green_panel.reshape(freq_count, 2 * span_j, local_pts)
    other_rows = other.reshape(freq_count, 2 * span_j, local_pts)
    moved_table = jnp.array(moved, jnp.int32)[slot]
    first_block = arrived[moved_table[0]]
    second_block = arrived[moved_table[1]]
    obs_first = first_block[:-1].reshape(observed.shape)
    obs_second = second_block[:-1].reshape(observed.shape)
    scale_first = first_block[-1]
    scale_second = second_block[-1]
    keep_first = my_role > 0
    keep_second = my_role == 1

    offset = slot * piece
    placed = lax.dynamic_update_slice_in_dim(
        jnp.zeros((freq_count, local_pts), jnp.float32), log_psd[0], offset, axis=1
    )
    log_field = butterfly_sum(placed, axes)

    def run_sweep(sweep_idx, log_field):
        psd_field = jnp.exp(log_field)
        spread = psd_field[:, None, None, :]
        weighted_mine = (green_panel * spread).astype(jnp.bfloat16).reshape(mine_rows.shape)
        weighted_other = (other * spread).astype(jnp.bfloat16).reshape(other_rows.shape)
        corr_first = correlate(mine_rows, weighted_other)
        corr_second = correlate(other_rows, weighted_mine)
        both = swap_add(jnp.stack([corr_first, corr_second]), "pts")
        adj_first = (scale_first * (quad_weight * both[0] - obs_first)).astype(jnp.bfloat16)
        adj_second = (scale_second * (quad_weight * both[1] - obs_second)).astype(jnp.bfloat16)
        term_first = point_terms(adj_first, other_rows, mine_rows, psd_field, quad_weight)
        term_second = point_terms(adj_second, mine_rows, other_rows, psd_field, quad_weight)
        point_part = jnp.where(keep_first, term_first, 0.0) + jnp.where(keep_second, term_second, 0.0)
        gradient = butterfly_sum(point_part, axes)
        squares = swap_add(jnp.sum(gradient * gradient), "pts")
        return log_field - descent * gradient / jnp.sqrt(squares / entry_count + epsilon)

    log_field = lax.fori_loop(0, ITERS, run_sweep, log_field)
    own = lax.dynamic_slice_in_dim(log_field, offset, piece, axis=1)
    return own[None]


def solution(mesh):
    shape = mesh.shape
    plan_fits = shape["row"] == 4 and shape["col"] == 4 and shape["pts"] == 2
    return jax.shard_map(
        pair_body if plan_fits else broadcast_body,
        mesh=mesh,
        in_specs=(
            P(None, None, "col", "pts"),
            P("pts", None, ("row", "col")),
            P(None, None, "row", "col"),
            P("row", "col"),
        ),
        out_specs=P("pts", None, ("row", "col")),
        check_vma=False,
    )
```

```python
import jax
import jax.numpy as jnp
from jax import lax
from jax.sharding import PartitionSpec as P

ITERS = 2


epsilon = 1e-06
descent = 0.1


def from_root(block, axis, source):
    block = jnp.where(lax.axis_index(axis) == source, block, jnp.zeros_like(block))
    return lax.psum(block, axis)


def butterfly_sum(value, axes):
    for axis in axes:
        size = lax.axis_size(axis)
        if size & (size - 1):
            value = lax.psum(value, axis)
            continue
        me = lax.axis_index(axis)
        bit = 1
        while bit < size:
            radix = 4 if bit * 4 <= size else 2
            got = [value]
            for m in range(1, radix):
                mask = m * bit
                got.append(lax.ppermute(value, axis, [(i, i ^ mask) for i in range(size)]))
            stacked = jnp.stack(got)
            local = (me // bit) % radix
            ordered = [stacked[local ^ j] for j in range(radix)]
            if radix == 4:
                value = (ordered[0] + ordered[1]) + (ordered[2] + ordered[3])
            else:
                value = ordered[0] + ordered[1]
            bit *= radix
    return value


def group_sum(value, axes):
    sizes = [lax.axis_size(axis) for axis in axes]
    count = 1
    me = 0
    for axis, size in zip(axes, sizes):
        count *= size
        me = me * size + lax.axis_index(axis)
    got = [value]
    for mask in range(1, count):
        got.append(lax.ppermute(value, axes, [(i, i ^ mask) for i in range(count)]))
    stacked = jnp.stack(got)
    level = [stacked[me ^ j] for j in range(count)]
    while len(level) > 1:
        level = [level[k] + level[k + 1] for k in range(0, len(level), 2)]
    return level[0]


def swap_add(value, axis):
    size = lax.axis_size(axis)
    if size != 2:
        return lax.psum(value, axis)
    return value + lax.ppermute(value, axis, [(0, 1), (1, 0)])


def correlate(left_rows, weighted):
    half_a = left_rows.shape[1] // 2
    half_b = weighted.shape[1] // 2
    products = jnp.einsum("fan,fbn->fab", left_rows, weighted, preferred_element_type=jnp.float32)
    corr_real = products[:, :half_a, :half_b] + products[:, half_a:, half_b:]
    corr_imag = products[:, half_a:, :half_b] - products[:, :half_a, half_b:]
    return jnp.stack([corr_real, corr_imag], axis=1)


def adjoint_block(adjoint):
    adj_real = adjoint[:, 0]
    adj_imag = adjoint[:, 1]
    top_half = jnp.concatenate([adj_real, -adj_imag], axis=2)
    low_half = jnp.concatenate([adj_imag, adj_real], axis=2)
    return jnp.concatenate([top_half, low_half], axis=1)


def point_terms(adjoint, right_rows, left_rows, psd_field, quad_weight):
    accumulated = jnp.einsum(
        "fab,fbn->fan", adjoint_block(adjoint), right_rows, preferred_element_type=jnp.float32
    )
    return quad_weight * psd_field * jnp.sum(left_rows * accumulated, axis=1)


def broadcast_body(green_panel, log_psd, observed, pair_weights):
    freq_count, comp_count, span_j, local_pts = green_panel.shape
    span_i = observed.shape[2]
    piece = log_psd.shape[2]
    row_count = lax.axis_size("row")
    col_count = lax.axis_size("col")
    pts_count = lax.axis_size("pts")
    quad_weight = 1.0 / (pts_count * local_pts)
    entry_count = freq_count * pts_count * local_pts
    pair_scale = pair_weights.astype(jnp.float32)
    group_ratio = col_count // row_count
    pieces = []
    for member in range(group_ratio):
        pieces.append(from_root(green_panel, "col", lax.axis_index("row") * group_ratio + member))
    rows_block = jnp.concatenate(pieces, axis=2).reshape(freq_count, 2 * span_i, local_pts)
    cols_block = green_panel.reshape(freq_count, 2 * span_j, local_pts)

    slot = lax.axis_index("row") * col_count + lax.axis_index("col")
    offset = slot * piece
    placed = lax.dynamic_update_slice_in_dim(
        jnp.zeros((freq_count, local_pts), jnp.float32), log_psd[0], offset, axis=1
    )
    log_field = butterfly_sum(placed, ("row", "col"))

    for _ in range(ITERS):
        psd_field = jnp.exp(log_field)
        weighted = (green_panel * psd_field[:, None, None, :]).astype(jnp.bfloat16)
        weighted = weighted.reshape(freq_count, 2 * span_j, local_pts)
        pair_sum = swap_add(correlate(rows_block, weighted), "pts")
        adjoint = (pair_scale * (quad_weight * pair_sum - observed)).astype(jnp.bfloat16)
        point_part = point_terms(adjoint, cols_block, rows_block, psd_field, quad_weight)
        gradient = butterfly_sum(point_part, ("row", "col"))
        squares = swap_add(jnp.sum(gradient * gradient), "pts")
        log_field = log_field - descent * gradient / jnp.sqrt(squares / entry_count + epsilon)

    own = lax.dynamic_slice_in_dim(log_field, offset, piece, axis=1)
    return own[None]


PAIR_PLAN = ((0, 0, 1), (1, 2, 0), (2, 0, 3), (2, 2, 1), (1, 1, 3), (3, 3, 2))


def pair_tables(blocks):
    role = [0] * (blocks * blocks)
    panel_moves = []
    needs = []
    for line, sender, receiver in PAIR_PLAN:
        role[line * blocks + receiver] = 1
        panel_moves.append((line * blocks + sender, line * blocks + receiver))
        needs.append((line * blocks + receiver, 0, receiver * blocks + sender))
        needs.append((line * blocks + receiver, 1, sender * blocks + receiver))
    for plane in range(blocks):
        role[plane * blocks + plane] = 2
    rounds = []
    moved = [[0, 0] for _ in range(blocks * blocks)]
    for dest, which, owner in needs:
        if owner == dest:
            continue
        for number, (pairs, whiches) in enumerate(rounds):
            if all(s != owner and d != dest for s, d in pairs):
                pairs.append((owner, dest))
                whiches.append((dest, which))
                moved[dest][which] = number + 1
                break
        else:
            rounds.append(([(owner, dest)], [(dest, which)]))
            moved[dest][which] = len(rounds)
    return role, panel_moves, rounds, moved


def pair_body(green_panel, log_psd, observed, pair_weights):
    freq_count, comp_count, span_j, local_pts = green_panel.shape
    piece = log_psd.shape[2]
    blocks = lax.axis_size("col")
    pts_count = lax.axis_size("pts")
    quad_weight = 1.0 / (pts_count * local_pts)
    entry_count = freq_count * pts_count * local_pts
    role, panel_moves, rounds, moved = pair_tables(blocks)
    slot = lax.axis_index("row") * blocks + lax.axis_index("col")
    my_role = jnp.array(role, jnp.int32)[slot]
    is_diag = my_role == 2
    axes = ("row", "col")

    received = lax.ppermute(green_panel, axes, panel_moves)

    own_block = jnp.concatenate(
        [observed.reshape(-1, span_j, span_j), pair_weights.astype(jnp.float32)[None]], axis=0
    )
    arrived = [own_block]
    for pairs, _ in rounds:
        arrived.append(lax.ppermute(own_block, axes, pairs))
    arrived = jnp.stack(arrived)
    received, arrived = lax.optimization_barrier((received, arrived))
    other = jnp.where(is_diag, green_panel, received)
    mine_rows = green_panel.reshape(freq_count, 2 * span_j, local_pts)
    other_rows = other.reshape(freq_count, 2 * span_j, local_pts)
    moved_table = jnp.array(moved, jnp.int32)[slot]
    first_block = arrived[moved_table[0]]
    second_block = arrived[moved_table[1]]
    obs_first = first_block[:-1].reshape(observed.shape)
    obs_second = second_block[:-1].reshape(observed.shape)
    scale_first = first_block[-1]
    scale_second = second_block[-1]
    keep_first = my_role > 0
    keep_second = my_role == 1

    offset = slot * piece
    placed = lax.dynamic_update_slice_in_dim(
        jnp.zeros((freq_count, local_pts), jnp.float32), log_psd[0], offset, axis=1
    )
    log_field = group_sum(placed, axes)

    def run_sweep(sweep_idx, log_field):
        psd_field = jnp.exp(log_field)
        spread = psd_field[:, None, None, :]
        weighted_mine = (green_panel * spread).astype(jnp.bfloat16).reshape(mine_rows.shape)
        weighted_other = (other * spread).astype(jnp.bfloat16).reshape(other_rows.shape)
        corr_first = correlate(mine_rows, weighted_other)
        corr_second = correlate(other_rows, weighted_mine)
        both = swap_add(jnp.stack([corr_first, corr_second]), "pts")
        adj_first = (scale_first * (quad_weight * both[0] - obs_first)).astype(jnp.bfloat16)
        adj_second = (scale_second * (quad_weight * both[1] - obs_second)).astype(jnp.bfloat16)
        term_first = point_terms(adj_first, other_rows, mine_rows, psd_field, quad_weight)
        term_second = point_terms(adj_second, mine_rows, other_rows, psd_field, quad_weight)
        point_part = jnp.where(keep_first, term_first, 0.0) + jnp.where(keep_second, term_second, 0.0)
        gradient = group_sum(point_part, axes)
        squares = swap_add(jnp.sum(gradient * gradient), "pts")
        return log_field - descent * gradient / jnp.sqrt(squares / entry_count + epsilon)

    log_field = lax.fori_loop(0, ITERS, run_sweep, log_field)
    own = lax.dynamic_slice_in_dim(log_field, offset, piece, axis=1)
    return own[None]


def solution(mesh):
    shape = mesh.shape
    plan_fits = shape["row"] == 4 and shape["col"] == 4 and shape["pts"] == 2
    return jax.shard_map(
        pair_body if plan_fits else broadcast_body,
        mesh=mesh,
        in_specs=(
            P(None, None, "col", "pts"),
            P("pts", None, ("row", "col")),
            P(None, None, "row", "col"),
            P("row", "col"),
        ),
        out_specs=P("pts", None, ("row", "col")),
        check_vma=False,
    )
```

```python
import jax
import jax.numpy as jnp
from jax import lax
from jax.sharding import PartitionSpec as P

ITERS = 2


epsilon = 1e-06
descent = 0.1


def from_root(block, axis, source):
    block = jnp.where(lax.axis_index(axis) == source, block, jnp.zeros_like(block))
    return lax.psum(block, axis)


def butterfly_sum(value, axes):
    for axis in axes:
        size = lax.axis_size(axis)
        if size & (size - 1):
            value = lax.psum(value, axis)
            continue
        me = lax.axis_index(axis)
        bit = 1
        while bit < size:
            radix = 4 if bit * 4 <= size else 2
            got = [value]
            for m in range(1, radix):
                mask = m * bit
                got.append(lax.ppermute(value, axis, [(i, i ^ mask) for i in range(size)]))
            stacked = jnp.stack(got)
            local = (me // bit) % radix
            ordered = [stacked[local ^ j] for j in range(radix)]
            if radix == 4:
                value = (ordered[0] + ordered[1]) + (ordered[2] + ordered[3])
            else:
                value = ordered[0] + ordered[1]
            bit *= radix
    return value


def swap_add(value, axis):
    size = lax.axis_size(axis)
    if size != 2:
        return lax.psum(value, axis)
    return value + lax.ppermute(value, axis, [(0, 1), (1, 0)])


def correlate(left_rows, weighted):
    half_a = left_rows.shape[1] // 2
    half_b = weighted.shape[1] // 2
    products = jnp.einsum("fan,fbn->fab", left_rows, weighted, preferred_element_type=jnp.float32)
    corr_real = products[:, :half_a, :half_b] + products[:, half_a:, half_b:]
    corr_imag = products[:, half_a:, :half_b] - products[:, :half_a, half_b:]
    return jnp.stack([corr_real, corr_imag], axis=1)


def adjoint_block(adjoint):
    adj_real = adjoint[:, 0]
    adj_imag = adjoint[:, 1]
    top_half = jnp.concatenate([adj_real, -adj_imag], axis=2)
    low_half = jnp.concatenate([adj_imag, adj_real], axis=2)
    return jnp.concatenate([top_half, low_half], axis=1)


def point_terms(adjoint, right_rows, left_rows, psd_field, quad_weight):
    accumulated = jnp.einsum(
        "fab,fbn->fan", adjoint_block(adjoint), right_rows, preferred_element_type=jnp.float32
    )
    return quad_weight * psd_field * jnp.sum(left_rows * accumulated, axis=1)


def broadcast_body(green_panel, log_psd, observed, pair_weights):
    freq_count, comp_count, span_j, local_pts = green_panel.shape
    span_i = observed.shape[2]
    piece = log_psd.shape[2]
    row_count = lax.axis_size("row")
    col_count = lax.axis_size("col")
    pts_count = lax.axis_size("pts")
    quad_weight = 1.0 / (pts_count * local_pts)
    entry_count = freq_count * pts_count * local_pts
    pair_scale = pair_weights.astype(jnp.float32)
    group_ratio = col_count // row_count
    pieces = []
    for member in range(group_ratio):
        pieces.append(from_root(green_panel, "col", lax.axis_index("row") * group_ratio + member))
    rows_block = jnp.concatenate(pieces, axis=2).reshape(freq_count, 2 * span_i, local_pts)
    cols_block = green_panel.reshape(freq_count, 2 * span_j, local_pts)

    slot = lax.axis_index("row") * col_count + lax.axis_index("col")
    offset = slot * piece
    placed = lax.dynamic_update_slice_in_dim(
        jnp.zeros((freq_count, local_pts), jnp.float32), log_psd[0], offset, axis=1
    )
    log_field = butterfly_sum(placed, ("row", "col"))

    for _ in range(ITERS):
        psd_field = jnp.exp(log_field)
        weighted = (green_panel * psd_field[:, None, None, :]).astype(jnp.bfloat16)
        weighted = weighted.reshape(freq_count, 2 * span_j, local_pts)
        pair_sum = swap_add(correlate(rows_block, weighted), "pts")
        adjoint = (pair_scale * (quad_weight * pair_sum - observed)).astype(jnp.bfloat16)
        point_part = point_terms(adjoint, cols_block, rows_block, psd_field, quad_weight)
        gradient = butterfly_sum(point_part, ("row", "col"))
        squares = swap_add(jnp.sum(gradient * gradient), "pts")
        log_field = log_field - descent * gradient / jnp.sqrt(squares / entry_count + epsilon)

    own = lax.dynamic_slice_in_dim(log_field, offset, piece, axis=1)
    return own[None]


PAIR_PLAN = ((0, 0, 1), (1, 2, 0), (2, 0, 3), (2, 2, 1), (1, 1, 3), (3, 3, 2))


def pair_tables(blocks):
    role = [0] * (blocks * blocks)
    panel_moves = []
    needs = []
    for line, sender, receiver in PAIR_PLAN:
        role[line * blocks + receiver] = 1
        panel_moves.append((line * blocks + sender, line * blocks + receiver))
        needs.append((line * blocks + receiver, 0, receiver * blocks + sender))
        needs.append((line * blocks + receiver, 1, sender * blocks + receiver))
    for plane in range(blocks):
        role[plane * blocks + plane] = 2
    rounds = []
    moved = [[0, 0] for _ in range(blocks * blocks)]
    for dest, which, owner in needs:
        if owner == dest:
            continue
        for number, (pairs, whiches) in enumerate(rounds):
            if all(s != owner and d != dest for s, d in pairs):
                pairs.append((owner, dest))
                whiches.append((dest, which))
                moved[dest][which] = number + 1
                break
        else:
            rounds.append(([(owner, dest)], [(dest, which)]))
            moved[dest][which] = len(rounds)
    return role, panel_moves, rounds, moved


def pair_body(green_panel, log_psd, observed, pair_weights):
    freq_count, comp_count, span_j, local_pts = green_panel.shape
    piece = log_psd.shape[2]
    blocks = lax.axis_size("col")
    pts_count = lax.axis_size("pts")
    quad_weight = 1.0 / (pts_count * local_pts)
    entry_count = freq_count * pts_count * local_pts
    role, panel_moves, rounds, moved = pair_tables(blocks)
    slot = lax.axis_index("row") * blocks + lax.axis_index("col")
    my_role = jnp.array(role, jnp.int32)[slot]
    is_diag = my_role == 2
    axes = ("row", "col")

    received = lax.ppermute(green_panel, axes, panel_moves)

    own_block = jnp.concatenate(
        [observed.reshape(-1, span_j, span_j), pair_weights.astype(jnp.float32)[None]], axis=0
    )
    planes = own_block.shape[0]
    half_planes = (planes + 1) // 2
    padded = jnp.concatenate(
        [own_block, jnp.zeros((2 * half_planes - planes,) + own_block.shape[1:], own_block.dtype)], axis=0
    )
    core = lax.axis_index("pts")
    own_half = lax.dynamic_slice_in_dim(padded, core * half_planes, half_planes, axis=0)
    halves = jnp.stack([lax.ppermute(own_half, axes, pairs) for pairs, _ in rounds])
    partner_halves = lax.ppermute(halves, "pts", [(0, 1), (1, 0)])
    joined = jnp.where(
        core == 0,
        jnp.concatenate([halves, partner_halves], axis=1),
        jnp.concatenate([partner_halves, halves], axis=1),
    )[:, :planes]
    arrived = jnp.concatenate([own_block[None], joined], axis=0)
    received, arrived = lax.optimization_barrier((received, arrived))
    other = jnp.where(is_diag, green_panel, received)
    mine_rows = green_panel.reshape(freq_count, 2 * span_j, local_pts)
    other_rows = other.reshape(freq_count, 2 * span_j, local_pts)
    moved_table = jnp.array(moved, jnp.int32)[slot]
    first_block = arrived[moved_table[0]]
    second_block = arrived[moved_table[1]]
    obs_first = first_block[:-1].reshape(observed.shape)
    obs_second = second_block[:-1].reshape(observed.shape)
    scale_first = first_block[-1]
    scale_second = second_block[-1]
    keep_first = my_role > 0
    keep_second = my_role == 1

    offset = slot * piece
    placed = lax.dynamic_update_slice_in_dim(
        jnp.zeros((freq_count, local_pts), jnp.float32), log_psd[0], offset, axis=1
    )
    log_field = butterfly_sum(placed, axes)

    def run_sweep(sweep_idx, log_field):
        psd_field = jnp.exp(log_field)
        spread = psd_field[:, None, None, :]
        weighted_mine = (green_panel * spread).astype(jnp.bfloat16).reshape(mine_rows.shape)
        weighted_other = (other * spread).astype(jnp.bfloat16).reshape(other_rows.shape)
        corr_first = correlate(mine_rows, weighted_other)
        corr_second = correlate(other_rows, weighted_mine)
        both = swap_add(jnp.stack([corr_first, corr_second]), "pts")
        adj_first = (scale_first * (quad_weight * both[0] - obs_first)).astype(jnp.bfloat16)
        adj_second = (scale_second * (quad_weight * both[1] - obs_second)).astype(jnp.bfloat16)
        term_first = point_terms(adj_first, other_rows, mine_rows, psd_field, quad_weight)
        term_second = point_terms(adj_second, mine_rows, other_rows, psd_field, quad_weight)
        point_part = jnp.where(keep_first, term_first, 0.0) + jnp.where(keep_second, term_second, 0.0)
        gradient = butterfly_sum(point_part, axes)
        squares = swap_add(jnp.sum(gradient * gradient), "pts")
        return log_field - descent * gradient / jnp.sqrt(squares / entry_count + epsilon)

    log_field = lax.fori_loop(0, ITERS, run_sweep, log_field)
    own = lax.dynamic_slice_in_dim(log_field, offset, piece, axis=1)
    return own[None]


def solution(mesh):
    shape = mesh.shape
    plan_fits = shape["row"] == 4 and shape["col"] == 4 and shape["pts"] == 2
    return jax.shard_map(
        pair_body if plan_fits else broadcast_body,
        mesh=mesh,
        in_specs=(
            P(None, None, "col", "pts"),
            P("pts", None, ("row", "col")),
            P(None, None, "row", "col"),
            P("row", "col"),
        ),
        out_specs=P("pts", None, ("row", "col")),
        check_vma=False,
    )
```

```python
import jax
import jax.numpy as jnp
from jax import lax
from jax.sharding import PartitionSpec as P

ITERS = 2


epsilon = 1e-06
descent = 0.1


def from_root(block, axis, source):
    block = jnp.where(lax.axis_index(axis) == source, block, jnp.zeros_like(block))
    return lax.psum(block, axis)


def butterfly_sum(value, axes):
    for axis in axes:
        size = lax.axis_size(axis)
        if size & (size - 1):
            value = lax.psum(value, axis)
            continue
        me = lax.axis_index(axis)
        bit = 1
        while bit < size:
            radix = 4 if bit * 4 <= size else 2
            got = [value]
            for m in range(1, radix):
                mask = m * bit
                got.append(lax.ppermute(value, axis, [(i, i ^ mask) for i in range(size)]))
            stacked = jnp.stack(got)
            local = (me // bit) % radix
            ordered = [stacked[local ^ j] for j in range(radix)]
            if radix == 4:
                value = (ordered[0] + ordered[1]) + (ordered[2] + ordered[3])
            else:
                value = ordered[0] + ordered[1]
            bit *= radix
    return value


def swap_add(value, axis):
    size = lax.axis_size(axis)
    if size != 2:
        return lax.psum(value, axis)
    return value + lax.ppermute(value, axis, [(0, 1), (1, 0)])


def correlate(left_rows, weighted):
    half_a = left_rows.shape[1] // 2
    half_b = weighted.shape[1] // 2
    products = jnp.einsum("fan,fbn->fab", left_rows, weighted, preferred_element_type=jnp.float32)
    corr_real = products[:, :half_a, :half_b] + products[:, half_a:, half_b:]
    corr_imag = products[:, half_a:, :half_b] - products[:, :half_a, half_b:]
    return jnp.stack([corr_real, corr_imag], axis=1)


def adjoint_block(adjoint):
    adj_real = adjoint[:, 0]
    adj_imag = adjoint[:, 1]
    top_half = jnp.concatenate([adj_real, -adj_imag], axis=2)
    low_half = jnp.concatenate([adj_imag, adj_real], axis=2)
    return jnp.concatenate([top_half, low_half], axis=1)


def point_terms(adjoint, right_rows, left_rows, psd_field, quad_weight):
    accumulated = jnp.einsum(
        "fab,fbn->fan", adjoint_block(adjoint), right_rows, preferred_element_type=jnp.float32
    )
    return quad_weight * psd_field * jnp.sum(left_rows * accumulated, axis=1)


def broadcast_body(green_panel, log_psd, observed, pair_weights):
    freq_count, comp_count, span_j, local_pts = green_panel.shape
    span_i = observed.shape[2]
    piece = log_psd.shape[2]
    row_count = lax.axis_size("row")
    col_count = lax.axis_size("col")
    pts_count = lax.axis_size("pts")
    quad_weight = 1.0 / (pts_count * local_pts)
    entry_count = freq_count * pts_count * local_pts
    pair_scale = pair_weights.astype(jnp.float32)
    group_ratio = col_count // row_count
    pieces = []
    for member in range(group_ratio):
        pieces.append(from_root(green_panel, "col", lax.axis_index("row") * group_ratio + member))
    rows_block = jnp.concatenate(pieces, axis=2).reshape(freq_count, 2 * span_i, local_pts)
    cols_block = green_panel.reshape(freq_count, 2 * span_j, local_pts)

    slot = lax.axis_index("row") * col_count + lax.axis_index("col")
    offset = slot * piece
    placed = lax.dynamic_update_slice_in_dim(
        jnp.zeros((freq_count, local_pts), jnp.float32), log_psd[0], offset, axis=1
    )
    log_field = butterfly_sum(placed, ("row", "col"))

    for _ in range(ITERS):
        psd_field = jnp.exp(log_field)
        weighted = (green_panel * psd_field[:, None, None, :]).astype(jnp.bfloat16)
        weighted = weighted.reshape(freq_count, 2 * span_j, local_pts)
        pair_sum = swap_add(correlate(rows_block, weighted), "pts")
        adjoint = (pair_scale * (quad_weight * pair_sum - observed)).astype(jnp.bfloat16)
        point_part = point_terms(adjoint, cols_block, rows_block, psd_field, quad_weight)
        gradient = butterfly_sum(point_part, ("row", "col"))
        squares = swap_add(jnp.sum(gradient * gradient), "pts")
        log_field = log_field - descent * gradient / jnp.sqrt(squares / entry_count + epsilon)

    own = lax.dynamic_slice_in_dim(log_field, offset, piece, axis=1)
    return own[None]


PAIR_PLAN = ((2, 0, 1), (1, 0, 2), (1, 3, 0), (0, 1, 2), (2, 1, 3), (0, 2, 3))


def pair_tables(blocks):
    role = [0] * (blocks * blocks)
    panel_moves = []
    needs = []
    for line, sender, receiver in PAIR_PLAN:
        role[line * blocks + receiver] = 1
        panel_moves.append((line * blocks + sender, line * blocks + receiver))
        needs.append((line * blocks + receiver, 0, receiver * blocks + sender))
        needs.append((line * blocks + receiver, 1, sender * blocks + receiver))
    for plane in range(blocks):
        role[plane * blocks + plane] = 2
        panel_moves.append((plane * blocks + plane, plane * blocks + plane))
    rounds = []
    moved = [[0, 0] for _ in range(blocks * blocks)]
    for dest, which, owner in needs:
        if owner == dest:
            continue
        for number, (pairs, whiches) in enumerate(rounds):
            if all(s != owner and d != dest for s, d in pairs):
                pairs.append((owner, dest))
                whiches.append((dest, which))
                moved[dest][which] = number + 1
                break
        else:
            rounds.append(([(owner, dest)], [(dest, which)]))
            moved[dest][which] = len(rounds)
    return role, panel_moves, rounds, moved


def pair_body(green_panel, log_psd, observed, pair_weights):
    freq_count, comp_count, span_j, local_pts = green_panel.shape
    piece = log_psd.shape[2]
    blocks = lax.axis_size("col")
    pts_count = lax.axis_size("pts")
    quad_weight = 1.0 / (pts_count * local_pts)
    entry_count = freq_count * pts_count * local_pts
    role, panel_moves, rounds, moved = pair_tables(blocks)
    slot = lax.axis_index("row") * blocks + lax.axis_index("col")
    my_role = jnp.array(role, jnp.int32)[slot]
    is_diag = my_role == 2
    axes = ("row", "col")

    received = lax.ppermute(green_panel, axes, panel_moves)

    own_block = jnp.concatenate(
        [observed.reshape(-1, span_j, span_j), pair_weights.astype(jnp.float32)[None]], axis=0
    )
    planes = own_block.shape[0]
    half_planes = (planes + 1) // 2
    padded = jnp.concatenate(
        [own_block, jnp.zeros((2 * half_planes - planes,) + own_block.shape[1:], own_block.dtype)], axis=0
    )
    core = lax.axis_index("pts")
    own_half = lax.dynamic_slice_in_dim(padded, core * half_planes, half_planes, axis=0)
    halves = jnp.stack([lax.ppermute(own_half, axes, pairs) for pairs, _ in rounds])
    partner_halves = lax.ppermute(halves, "pts", [(0, 1), (1, 0)])
    joined = jnp.where(
        core == 0,
        jnp.concatenate([halves, partner_halves], axis=1),
        jnp.concatenate([partner_halves, halves], axis=1),
    )[:, :planes]
    arrived = jnp.concatenate([own_block[None], joined], axis=0)
    received, arrived = lax.optimization_barrier((received, arrived))
    other = received
    mine_rows = green_panel.reshape(freq_count, 2 * span_j, local_pts)
    other_rows = other.reshape(freq_count, 2 * span_j, local_pts)
    moved_table = jnp.array(moved, jnp.int32)[slot]
    first_block = arrived[moved_table[0]]
    second_block = arrived[moved_table[1]]
    obs_first = first_block[:-1].reshape(observed.shape)
    obs_second = second_block[:-1].reshape(observed.shape)
    scale_first = first_block[-1]
    scale_second = second_block[-1]
    keep_first = my_role > 0
    keep_second = my_role == 1

    offset = slot * piece
    placed = lax.dynamic_update_slice_in_dim(
        jnp.zeros((freq_count, local_pts), jnp.float32), log_psd[0], offset, axis=1
    )
    log_field = butterfly_sum(placed, axes)

    def run_sweep(sweep_idx, log_field):
        psd_field = jnp.exp(log_field)
        spread = psd_field[:, None, None, :]
        weighted_mine = (green_panel * spread).astype(jnp.bfloat16).reshape(mine_rows.shape)
        weighted_other = (other * spread).astype(jnp.bfloat16).reshape(other_rows.shape)
        corr_first = correlate(mine_rows, weighted_other)
        corr_second = correlate(other_rows, weighted_mine)
        both = swap_add(jnp.stack([corr_first, corr_second]), "pts")
        adj_first = (scale_first * (quad_weight * both[0] - obs_first)).astype(jnp.bfloat16)
        adj_second = (scale_second * (quad_weight * both[1] - obs_second)).astype(jnp.bfloat16)
        term_first = point_terms(adj_first, other_rows, mine_rows, psd_field, quad_weight)
        term_second = point_terms(adj_second, mine_rows, other_rows, psd_field, quad_weight)
        point_part = jnp.where(keep_first, term_first, 0.0) + jnp.where(keep_second, term_second, 0.0)
        gradient = butterfly_sum(point_part, axes)
        squares = swap_add(jnp.sum(gradient * gradient), "pts")
        return log_field - descent * gradient / jnp.sqrt(squares / entry_count + epsilon)

    log_field = lax.fori_loop(0, ITERS, run_sweep, log_field)
    own = lax.dynamic_slice_in_dim(log_field, offset, piece, axis=1)
    return own[None]


def solution(mesh):
    shape = mesh.shape
    plan_fits = shape["row"] == 4 and shape["col"] == 4 and shape["pts"] == 2
    return jax.shard_map(
        pair_body if plan_fits else broadcast_body,
        mesh=mesh,
        in_specs=(
            P(None, None, "col", "pts"),
            P("pts", None, ("row", "col")),
            P(None, None, "row", "col"),
            P("row", "col"),
        ),
        out_specs=P("pts", None, ("row", "col")),
        check_vma=False,
    )
```

```python
import jax
import jax.numpy as jnp
from jax import lax
from jax.experimental import pallas as pl
from jax.experimental.pallas import tpu as pltpu
from jax.sharding import PartitionSpec as P

ITERS = 2


epsilon = 1e-06
descent = 0.1


def from_root(block, axis, source):
    block = jnp.where(lax.axis_index(axis) == source, block, jnp.zeros_like(block))
    return lax.psum(block, axis)


def butterfly_sum(value, axes):
    for axis in axes:
        size = lax.axis_size(axis)
        if size & (size - 1):
            value = lax.psum(value, axis)
            continue
        me = lax.axis_index(axis)
        bit = 1
        while bit < size:
            radix = 4 if bit * 4 <= size else 2
            got = [value]
            for m in range(1, radix):
                mask = m * bit
                got.append(lax.ppermute(value, axis, [(i, i ^ mask) for i in range(size)]))
            stacked = jnp.stack(got)
            local = (me // bit) % radix
            ordered = [stacked[local ^ j] for j in range(radix)]
            if radix == 4:
                value = (ordered[0] + ordered[1]) + (ordered[2] + ordered[3])
            else:
                value = ordered[0] + ordered[1]
            bit *= radix
    return value


def swap_add(value, axis):
    size = lax.axis_size(axis)
    if size != 2:
        return lax.psum(value, axis)
    return value + lax.ppermute(value, axis, [(0, 1), (1, 0)])


def correlate(left_rows, weighted):
    half_a = left_rows.shape[1] // 2
    half_b = weighted.shape[1] // 2
    products = jnp.einsum("fan,fbn->fab", left_rows, weighted, preferred_element_type=jnp.float32)
    corr_real = products[:, :half_a, :half_b] + products[:, half_a:, half_b:]
    corr_imag = products[:, half_a:, :half_b] - products[:, :half_a, half_b:]
    return jnp.stack([corr_real, corr_imag], axis=1)


def pair_products(mine, other, field, tile=512):
    freq, rows, points = mine.shape
    def kernel(mine_ref, other_ref, field_ref, first_ref, second_ref):
        step = pl.program_id(1)
        @pl.when(step == 0)
        def _():
            first_ref[...] = jnp.zeros_like(first_ref)
            second_ref[...] = jnp.zeros_like(second_ref)
        spread = field_ref[0]
        mine_tile = mine_ref[0]
        other_tile = other_ref[0]
        weighted_other = (other_tile.astype(jnp.float32) * spread).astype(jnp.bfloat16)
        weighted_mine = (mine_tile.astype(jnp.float32) * spread).astype(jnp.bfloat16)
        dims = (((1,), (1,)), ((), ()))
        first_ref[0] += jax.lax.dot_general(mine_tile, weighted_other, dims, preferred_element_type=jnp.float32)
        second_ref[0] += jax.lax.dot_general(other_tile, weighted_mine, dims, preferred_element_type=jnp.float32)
    spec = pl.BlockSpec((1, rows, tile), lambda f, t: (f, 0, t))
    out_spec = pl.BlockSpec((1, rows, rows), lambda f, t: (f, 0, 0))
    return pl.pallas_call(
        kernel,
        grid=(freq, points // tile),
        in_specs=[spec, spec, pl.BlockSpec((1, 1, tile), lambda f, t: (f, 0, t))],
        out_specs=[out_spec, out_spec],
        out_shape=[jax.ShapeDtypeStruct((freq, rows, rows), jnp.float32)] * 2,
        compiler_params=pltpu.CompilerParams(dimension_semantics=("parallel", "arbitrary")),
    )(mine, other, field[:, None, :])


def combine(products, half_a, half_b):
    corr_real = products[:, :half_a, :half_b] + products[:, half_a:, half_b:]
    corr_imag = products[:, half_a:, :half_b] - products[:, :half_a, half_b:]
    return jnp.stack([corr_real, corr_imag], axis=1)


def adjoint_block(adjoint):
    adj_real = adjoint[:, 0]
    adj_imag = adjoint[:, 1]
    top_half = jnp.concatenate([adj_real, -adj_imag], axis=2)
    low_half = jnp.concatenate([adj_imag, adj_real], axis=2)
    return jnp.concatenate([top_half, low_half], axis=1)


def point_terms(adjoint, right_rows, left_rows, psd_field, quad_weight):
    accumulated = jnp.einsum(
        "fab,fbn->fan", adjoint_block(adjoint), right_rows, preferred_element_type=jnp.float32
    )
    return quad_weight * psd_field * jnp.sum(left_rows * accumulated, axis=1)


def broadcast_body(green_panel, log_psd, observed, pair_weights):
    freq_count, comp_count, span_j, local_pts = green_panel.shape
    span_i = observed.shape[2]
    piece = log_psd.shape[2]
    row_count = lax.axis_size("row")
    col_count = lax.axis_size("col")
    pts_count = lax.axis_size("pts")
    quad_weight = 1.0 / (pts_count * local_pts)
    entry_count = freq_count * pts_count * local_pts
    pair_scale = pair_weights.astype(jnp.float32)
    group_ratio = col_count // row_count
    pieces = []
    for member in range(group_ratio):
        pieces.append(from_root(green_panel, "col", lax.axis_index("row") * group_ratio + member))
    rows_block = jnp.concatenate(pieces, axis=2).reshape(freq_count, 2 * span_i, local_pts)
    cols_block = green_panel.reshape(freq_count, 2 * span_j, local_pts)

    slot = lax.axis_index("row") * col_count + lax.axis_index("col")
    offset = slot * piece
    placed = lax.dynamic_update_slice_in_dim(
        jnp.zeros((freq_count, local_pts), jnp.float32), log_psd[0], offset, axis=1
    )
    log_field = butterfly_sum(placed, ("row", "col"))

    for _ in range(ITERS):
        psd_field = jnp.exp(log_field)
        weighted = (green_panel * psd_field[:, None, None, :]).astype(jnp.bfloat16)
        weighted = weighted.reshape(freq_count, 2 * span_j, local_pts)
        pair_sum = swap_add(correlate(rows_block, weighted), "pts")
        adjoint = (pair_scale * (quad_weight * pair_sum - observed)).astype(jnp.bfloat16)
        point_part = point_terms(adjoint, cols_block, rows_block, psd_field, quad_weight)
        gradient = butterfly_sum(point_part, ("row", "col"))
        squares = swap_add(jnp.sum(gradient * gradient), "pts")
        log_field = log_field - descent * gradient / jnp.sqrt(squares / entry_count + epsilon)

    own = lax.dynamic_slice_in_dim(log_field, offset, piece, axis=1)
    return own[None]


PAIR_PLAN = ((0, 0, 1), (1, 2, 0), (2, 0, 3), (2, 2, 1), (1, 1, 3), (3, 3, 2))


def pair_tables(blocks):
    role = [0] * (blocks * blocks)
    panel_moves = []
    needs = []
    for line, sender, receiver in PAIR_PLAN:
        role[line * blocks + receiver] = 1
        panel_moves.append((line * blocks + sender, line * blocks + receiver))
        needs.append((line * blocks + receiver, 0, receiver * blocks + sender))
        needs.append((line * blocks + receiver, 1, sender * blocks + receiver))
    for plane in range(blocks):
        role[plane * blocks + plane] = 2
    rounds = []
    moved = [[0, 0] for _ in range(blocks * blocks)]
    for dest, which, owner in needs:
        if owner == dest:
            continue
        for number, (pairs, whiches) in enumerate(rounds):
            if all(s != owner and d != dest for s, d in pairs):
                pairs.append((owner, dest))
                whiches.append((dest, which))
                moved[dest][which] = number + 1
                break
        else:
            rounds.append(([(owner, dest)], [(dest, which)]))
            moved[dest][which] = len(rounds)
    return role, panel_moves, rounds, moved


def pair_body(green_panel, log_psd, observed, pair_weights):
    freq_count, comp_count, span_j, local_pts = green_panel.shape
    piece = log_psd.shape[2]
    blocks = lax.axis_size("col")
    pts_count = lax.axis_size("pts")
    quad_weight = 1.0 / (pts_count * local_pts)
    entry_count = freq_count * pts_count * local_pts
    role, panel_moves, rounds, moved = pair_tables(blocks)
    slot = lax.axis_index("row") * blocks + lax.axis_index("col")
    my_role = jnp.array(role, jnp.int32)[slot]
    is_diag = my_role == 2
    axes = ("row", "col")

    received = lax.ppermute(green_panel, axes, panel_moves)

    own_block = jnp.concatenate(
        [observed.reshape(-1, span_j, span_j), pair_weights.astype(jnp.float32)[None]], axis=0
    )
    planes = own_block.shape[0]
    half_planes = (planes + 1) // 2
    padded = jnp.concatenate(
        [own_block, jnp.zeros((2 * half_planes - planes,) + own_block.shape[1:], own_block.dtype)], axis=0
    )
    core = lax.axis_index("pts")
    own_half = lax.dynamic_slice_in_dim(padded, core * half_planes, half_planes, axis=0)
    halves = jnp.stack([lax.ppermute(own_half, axes, pairs) for pairs, _ in rounds])
    partner_halves = lax.ppermute(halves, "pts", [(0, 1), (1, 0)])
    joined = jnp.where(
        core == 0,
        jnp.concatenate([halves, partner_halves], axis=1),
        jnp.concatenate([partner_halves, halves], axis=1),
    )[:, :planes]
    arrived = jnp.concatenate([own_block[None], joined], axis=0)
    received, arrived = lax.optimization_barrier((received, arrived))
    other = jnp.where(is_diag, green_panel, received)
    mine_rows = green_panel.reshape(freq_count, 2 * span_j, local_pts)
    other_rows = other.reshape(freq_count, 2 * span_j, local_pts)
    moved_table = jnp.array(moved, jnp.int32)[slot]
    first_block = arrived[moved_table[0]]
    second_block = arrived[moved_table[1]]
    obs_first = first_block[:-1].reshape(observed.shape)
    obs_second = second_block[:-1].reshape(observed.shape)
    scale_first = first_block[-1]
    scale_second = second_block[-1]
    keep_first = my_role > 0
    keep_second = my_role == 1

    offset = slot * piece
    placed = lax.dynamic_update_slice_in_dim(
        jnp.zeros((freq_count, local_pts), jnp.float32), log_psd[0], offset, axis=1
    )
    log_field = butterfly_sum(placed, axes)

    def run_sweep(sweep_idx, log_field):
        psd_field = jnp.exp(log_field)
        spread = psd_field[:, None, None, :]
        product_first, product_second = pair_products(mine_rows, other_rows, psd_field)
        corr_first = combine(product_first, span_j, span_j)
        corr_second = combine(product_second, span_j, span_j)
        both = swap_add(jnp.stack([corr_first, corr_second]), "pts")
        adj_first = (scale_first * (quad_weight * both[0] - obs_first)).astype(jnp.bfloat16)
        adj_second = (scale_second * (quad_weight * both[1] - obs_second)).astype(jnp.bfloat16)
        term_first = point_terms(adj_first, other_rows, mine_rows, psd_field, quad_weight)
        term_second = point_terms(adj_second, mine_rows, other_rows, psd_field, quad_weight)
        point_part = jnp.where(keep_first, term_first, 0.0) + jnp.where(keep_second, term_second, 0.0)
        gradient = butterfly_sum(point_part, axes)
        squares = swap_add(jnp.sum(gradient * gradient), "pts")
        return log_field - descent * gradient / jnp.sqrt(squares / entry_count + epsilon)

    log_field = lax.fori_loop(0, ITERS, run_sweep, log_field)
    own = lax.dynamic_slice_in_dim(log_field, offset, piece, axis=1)
    return own[None]


def solution(mesh):
    shape = mesh.shape
    plan_fits = shape["row"] == 4 and shape["col"] == 4 and shape["pts"] == 2
    return jax.shard_map(
        pair_body if plan_fits else broadcast_body,
        mesh=mesh,
        in_specs=(
            P(None, None, "col", "pts"),
            P("pts", None, ("row", "col")),
            P(None, None, "row", "col"),
            P("row", "col"),
        ),
        out_specs=P("pts", None, ("row", "col")),
        check_vma=False,
    )
```

```python
import jax
import jax.numpy as jnp
from jax import lax
from jax.experimental import pallas as pl
from jax.experimental.pallas import tpu as pltpu
from jax.sharding import PartitionSpec as P

ITERS = 2


epsilon = 1e-06
descent = 0.1


def from_root(block, axis, source):
    block = jnp.where(lax.axis_index(axis) == source, block, jnp.zeros_like(block))
    return lax.psum(block, axis)


def butterfly_sum(value, axes):
    for axis in axes:
        size = lax.axis_size(axis)
        if size & (size - 1):
            value = lax.psum(value, axis)
            continue
        me = lax.axis_index(axis)
        bit = 1
        while bit < size:
            radix = 4 if bit * 4 <= size else 2
            got = [value]
            for m in range(1, radix):
                mask = m * bit
                got.append(lax.ppermute(value, axis, [(i, i ^ mask) for i in range(size)]))
            stacked = jnp.stack(got)
            local = (me // bit) % radix
            ordered = [stacked[local ^ j] for j in range(radix)]
            if radix == 4:
                value = (ordered[0] + ordered[1]) + (ordered[2] + ordered[3])
            else:
                value = ordered[0] + ordered[1]
            bit *= radix
    return value


def swap_add(value, axis):
    size = lax.axis_size(axis)
    if size != 2:
        return lax.psum(value, axis)
    return value + lax.ppermute(value, axis, [(0, 1), (1, 0)])


def correlate(left_rows, weighted):
    half_a = left_rows.shape[1] // 2
    half_b = weighted.shape[1] // 2
    products = jnp.einsum("fan,fbn->fab", left_rows, weighted, preferred_element_type=jnp.float32)
    corr_real = products[:, :half_a, :half_b] + products[:, half_a:, half_b:]
    corr_imag = products[:, half_a:, :half_b] - products[:, :half_a, half_b:]
    return jnp.stack([corr_real, corr_imag], axis=1)


def pair_products(mine, other, field, tile=1536):
    freq, rows, points = mine.shape
    def kernel(mine_ref, other_ref, field_ref, first_ref, second_ref):
        step = pl.program_id(1)
        @pl.when(step == 0)
        def _():
            first_ref[...] = jnp.zeros_like(first_ref)
            second_ref[...] = jnp.zeros_like(second_ref)
        spread = field_ref[0]
        mine_tile = mine_ref[0]
        other_tile = other_ref[0]
        weighted_other = (other_tile.astype(jnp.float32) * spread).astype(jnp.bfloat16)
        weighted_mine = (mine_tile.astype(jnp.float32) * spread).astype(jnp.bfloat16)
        dims = (((1,), (1,)), ((), ()))
        first_ref[0] += jax.lax.dot_general(mine_tile, weighted_other, dims, preferred_element_type=jnp.float32)
        second_ref[0] += jax.lax.dot_general(other_tile, weighted_mine, dims, preferred_element_type=jnp.float32)
    spec = pl.BlockSpec((1, rows, tile), lambda f, t: (f, 0, t))
    out_spec = pl.BlockSpec((1, rows, rows), lambda f, t: (f, 0, 0))
    return pl.pallas_call(
        kernel,
        grid=(freq, points // tile),
        in_specs=[spec, spec, pl.BlockSpec((1, 1, tile), lambda f, t: (f, 0, t))],
        out_specs=[out_spec, out_spec],
        out_shape=[jax.ShapeDtypeStruct((freq, rows, rows), jnp.float32)] * 2,
        compiler_params=pltpu.CompilerParams(dimension_semantics=("parallel", "arbitrary")),
    )(mine, other, field[:, None, :])


def combine(products, half_a, half_b):
    corr_real = products[:, :half_a, :half_b] + products[:, half_a:, half_b:]
    corr_imag = products[:, half_a:, :half_b] - products[:, :half_a, half_b:]
    return jnp.stack([corr_real, corr_imag], axis=1)


def adjoint_block(adjoint):
    adj_real = adjoint[:, 0]
    adj_imag = adjoint[:, 1]
    top_half = jnp.concatenate([adj_real, -adj_imag], axis=2)
    low_half = jnp.concatenate([adj_imag, adj_real], axis=2)
    return jnp.concatenate([top_half, low_half], axis=1)


def point_terms(adjoint, right_rows, left_rows, psd_field, quad_weight):
    accumulated = jnp.einsum(
        "fab,fbn->fan", adjoint_block(adjoint), right_rows, preferred_element_type=jnp.float32
    )
    return quad_weight * psd_field * jnp.sum(left_rows * accumulated, axis=1)


def broadcast_body(green_panel, log_psd, observed, pair_weights):
    freq_count, comp_count, span_j, local_pts = green_panel.shape
    span_i = observed.shape[2]
    piece = log_psd.shape[2]
    row_count = lax.axis_size("row")
    col_count = lax.axis_size("col")
    pts_count = lax.axis_size("pts")
    quad_weight = 1.0 / (pts_count * local_pts)
    entry_count = freq_count * pts_count * local_pts
    pair_scale = pair_weights.astype(jnp.float32)
    group_ratio = col_count // row_count
    pieces = []
    for member in range(group_ratio):
        pieces.append(from_root(green_panel, "col", lax.axis_index("row") * group_ratio + member))
    rows_block = jnp.concatenate(pieces, axis=2).reshape(freq_count, 2 * span_i, local_pts)
    cols_block = green_panel.reshape(freq_count, 2 * span_j, local_pts)

    slot = lax.axis_index("row") * col_count + lax.axis_index("col")
    offset = slot * piece
    placed = lax.dynamic_update_slice_in_dim(
        jnp.zeros((freq_count, local_pts), jnp.float32), log_psd[0], offset, axis=1
    )
    log_field = butterfly_sum(placed, ("row", "col"))

    for _ in range(ITERS):
        psd_field = jnp.exp(log_field)
        weighted = (green_panel * psd_field[:, None, None, :]).astype(jnp.bfloat16)
        weighted = weighted.reshape(freq_count, 2 * span_j, local_pts)
        pair_sum = swap_add(correlate(rows_block, weighted), "pts")
        adjoint = (pair_scale * (quad_weight * pair_sum - observed)).astype(jnp.bfloat16)
        point_part = point_terms(adjoint, cols_block, rows_block, psd_field, quad_weight)
        gradient = butterfly_sum(point_part, ("row", "col"))
        squares = swap_add(jnp.sum(gradient * gradient), "pts")
        log_field = log_field - descent * gradient / jnp.sqrt(squares / entry_count + epsilon)

    own = lax.dynamic_slice_in_dim(log_field, offset, piece, axis=1)
    return own[None]


PAIR_PLAN = ((0, 0, 1), (1, 2, 0), (2, 0, 3), (2, 2, 1), (1, 1, 3), (3, 3, 2))


def pair_tables(blocks):
    role = [0] * (blocks * blocks)
    panel_moves = []
    needs = []
    for line, sender, receiver in PAIR_PLAN:
        role[line * blocks + receiver] = 1
        panel_moves.append((line * blocks + sender, line * blocks + receiver))
        needs.append((line * blocks + receiver, 0, receiver * blocks + sender))
        needs.append((line * blocks + receiver, 1, sender * blocks + receiver))
    for plane in range(blocks):
        role[plane * blocks + plane] = 2
    rounds = []
    moved = [[0, 0] for _ in range(blocks * blocks)]
    for dest, which, owner in needs:
        if owner == dest:
            continue
        for number, (pairs, whiches) in enumerate(rounds):
            if all(s != owner and d != dest for s, d in pairs):
                pairs.append((owner, dest))
                whiches.append((dest, which))
                moved[dest][which] = number + 1
                break
        else:
            rounds.append(([(owner, dest)], [(dest, which)]))
            moved[dest][which] = len(rounds)
    return role, panel_moves, rounds, moved


def pair_body(green_panel, log_psd, observed, pair_weights):
    freq_count, comp_count, span_j, local_pts = green_panel.shape
    piece = log_psd.shape[2]
    blocks = lax.axis_size("col")
    pts_count = lax.axis_size("pts")
    quad_weight = 1.0 / (pts_count * local_pts)
    entry_count = freq_count * pts_count * local_pts
    role, panel_moves, rounds, moved = pair_tables(blocks)
    slot = lax.axis_index("row") * blocks + lax.axis_index("col")
    my_role = jnp.array(role, jnp.int32)[slot]
    is_diag = my_role == 2
    axes = ("row", "col")

    received = lax.ppermute(green_panel, axes, panel_moves)

    own_block = jnp.concatenate(
        [observed.reshape(-1, span_j, span_j), pair_weights.astype(jnp.float32)[None]], axis=0
    )
    planes = own_block.shape[0]
    half_planes = (planes + 1) // 2
    padded = jnp.concatenate(
        [own_block, jnp.zeros((2 * half_planes - planes,) + own_block.shape[1:], own_block.dtype)], axis=0
    )
    core = lax.axis_index("pts")
    own_half = lax.dynamic_slice_in_dim(padded, core * half_planes, half_planes, axis=0)
    halves = jnp.stack([lax.ppermute(own_half, axes, pairs) for pairs, _ in rounds])
    partner_halves = lax.ppermute(halves, "pts", [(0, 1), (1, 0)])
    joined = jnp.where(
        core == 0,
        jnp.concatenate([halves, partner_halves], axis=1),
        jnp.concatenate([partner_halves, halves], axis=1),
    )[:, :planes]
    arrived = jnp.concatenate([own_block[None], joined], axis=0)
    received, arrived = lax.optimization_barrier((received, arrived))
    other = jnp.where(is_diag, green_panel, received)
    mine_rows = green_panel.reshape(freq_count, 2 * span_j, local_pts)
    other_rows = other.reshape(freq_count, 2 * span_j, local_pts)
    moved_table = jnp.array(moved, jnp.int32)[slot]
    first_block = arrived[moved_table[0]]
    second_block = arrived[moved_table[1]]
    obs_first = first_block[:-1].reshape(observed.shape)
    obs_second = second_block[:-1].reshape(observed.shape)
    scale_first = first_block[-1]
    scale_second = second_block[-1]
    keep_first = my_role > 0
    keep_second = my_role == 1

    offset = slot * piece
    placed = lax.dynamic_update_slice_in_dim(
        jnp.zeros((freq_count, local_pts), jnp.float32), log_psd[0], offset, axis=1
    )
    log_field = butterfly_sum(placed, axes)

    def run_sweep(sweep_idx, log_field):
        psd_field = jnp.exp(log_field)
        spread = psd_field[:, None, None, :]
        product_first, product_second = pair_products(mine_rows, other_rows, psd_field)
        corr_first = combine(product_first, span_j, span_j)
        corr_second = combine(product_second, span_j, span_j)
        both = swap_add(jnp.stack([corr_first, corr_second]), "pts")
        adj_first = (scale_first * (quad_weight * both[0] - obs_first)).astype(jnp.bfloat16)
        adj_second = (scale_second * (quad_weight * both[1] - obs_second)).astype(jnp.bfloat16)
        term_first = point_terms(adj_first, other_rows, mine_rows, psd_field, quad_weight)
        term_second = point_terms(adj_second, mine_rows, other_rows, psd_field, quad_weight)
        point_part = jnp.where(keep_first, term_first, 0.0) + jnp.where(keep_second, term_second, 0.0)
        gradient = butterfly_sum(point_part, axes)
        squares = swap_add(jnp.sum(gradient * gradient), "pts")
        return log_field - descent * gradient / jnp.sqrt(squares / entry_count + epsilon)

    log_field = lax.fori_loop(0, ITERS, run_sweep, log_field)
    own = lax.dynamic_slice_in_dim(log_field, offset, piece, axis=1)
    return own[None]


def solution(mesh):
    shape = mesh.shape
    plan_fits = shape["row"] == 4 and shape["col"] == 4 and shape["pts"] == 2
    return jax.shard_map(
        pair_body if plan_fits else broadcast_body,
        mesh=mesh,
        in_specs=(
            P(None, None, "col", "pts"),
            P("pts", None, ("row", "col")),
            P(None, None, "row", "col"),
            P("row", "col"),
        ),
        out_specs=P("pts", None, ("row", "col")),
        check_vma=False,
    )
```

```python
import jax
import jax.numpy as jnp
from jax import lax
from jax.experimental import pallas as pl
from jax.experimental.pallas import tpu as pltpu
from jax.sharding import PartitionSpec as P

ITERS = 2


epsilon = 1e-06
descent = 0.1


def from_root(block, axis, source):
    block = jnp.where(lax.axis_index(axis) == source, block, jnp.zeros_like(block))
    return lax.psum(block, axis)


def butterfly_sum(value, axes):
    for axis in axes:
        size = lax.axis_size(axis)
        if size & (size - 1):
            value = lax.psum(value, axis)
            continue
        me = lax.axis_index(axis)
        bit = 1
        while bit < size:
            radix = 4 if bit * 4 <= size else 2
            got = [value]
            for m in range(1, radix):
                mask = m * bit
                got.append(lax.ppermute(value, axis, [(i, i ^ mask) for i in range(size)]))
            stacked = jnp.stack(got)
            local = (me // bit) % radix
            ordered = [stacked[local ^ j] for j in range(radix)]
            if radix == 4:
                value = (ordered[0] + ordered[1]) + (ordered[2] + ordered[3])
            else:
                value = ordered[0] + ordered[1]
            bit *= radix
    return value


def swap_add(value, axis):
    size = lax.axis_size(axis)
    if size != 2:
        return lax.psum(value, axis)
    return value + lax.ppermute(value, axis, [(0, 1), (1, 0)])


def correlate(left_rows, weighted):
    half_a = left_rows.shape[1] // 2
    half_b = weighted.shape[1] // 2
    products = jnp.einsum("fan,fbn->fab", left_rows, weighted, preferred_element_type=jnp.float32)
    corr_real = products[:, :half_a, :half_b] + products[:, half_a:, half_b:]
    corr_imag = products[:, half_a:, :half_b] - products[:, :half_a, half_b:]
    return jnp.stack([corr_real, corr_imag], axis=1)


def pair_products(mine, other, field, tile=3072):
    freq, rows, points = mine.shape
    def kernel(mine_ref, other_ref, field_ref, first_ref, second_ref):
        step = pl.program_id(1)
        @pl.when(step == 0)
        def _():
            first_ref[...] = jnp.zeros_like(first_ref)
            second_ref[...] = jnp.zeros_like(second_ref)
        spread = field_ref[0]
        mine_tile = mine_ref[0]
        other_tile = other_ref[0]
        weighted_other = (other_tile.astype(jnp.float32) * spread).astype(jnp.bfloat16)
        weighted_mine = (mine_tile.astype(jnp.float32) * spread).astype(jnp.bfloat16)
        dims = (((1,), (1,)), ((), ()))
        first_ref[0] += jax.lax.dot_general(mine_tile, weighted_other, dims, preferred_element_type=jnp.float32)
        second_ref[0] += jax.lax.dot_general(other_tile, weighted_mine, dims, preferred_element_type=jnp.float32)
    spec = pl.BlockSpec((1, rows, tile), lambda f, t: (f, 0, t))
    out_spec = pl.BlockSpec((1, rows, rows), lambda f, t: (f, 0, 0))
    return pl.pallas_call(
        kernel,
        grid=(freq, points // tile),
        in_specs=[spec, spec, pl.BlockSpec((1, 1, tile), lambda f, t: (f, 0, t))],
        out_specs=[out_spec, out_spec],
        out_shape=[jax.ShapeDtypeStruct((freq, rows, rows), jnp.float32)] * 2,
        compiler_params=pltpu.CompilerParams(dimension_semantics=("parallel", "arbitrary")),
    )(mine, other, field[:, None, :])


def combine(products, half_a, half_b):
    corr_real = products[:, :half_a, :half_b] + products[:, half_a:, half_b:]
    corr_imag = products[:, half_a:, :half_b] - products[:, :half_a, half_b:]
    return jnp.stack([corr_real, corr_imag], axis=1)


def adjoint_block(adjoint):
    adj_real = adjoint[:, 0]
    adj_imag = adjoint[:, 1]
    top_half = jnp.concatenate([adj_real, -adj_imag], axis=2)
    low_half = jnp.concatenate([adj_imag, adj_real], axis=2)
    return jnp.concatenate([top_half, low_half], axis=1)


def point_terms(adjoint, right_rows, left_rows, psd_field, quad_weight):
    accumulated = jnp.einsum(
        "fab,fbn->fan", adjoint_block(adjoint), right_rows, preferred_element_type=jnp.float32
    )
    return quad_weight * psd_field * jnp.sum(left_rows * accumulated, axis=1)


def broadcast_body(green_panel, log_psd, observed, pair_weights):
    freq_count, comp_count, span_j, local_pts = green_panel.shape
    span_i = observed.shape[2]
    piece = log_psd.shape[2]
    row_count = lax.axis_size("row")
    col_count = lax.axis_size("col")
    pts_count = lax.axis_size("pts")
    quad_weight = 1.0 / (pts_count * local_pts)
    entry_count = freq_count * pts_count * local_pts
    pair_scale = pair_weights.astype(jnp.float32)
    group_ratio = col_count // row_count
    pieces = []
    for member in range(group_ratio):
        pieces.append(from_root(green_panel, "col", lax.axis_index("row") * group_ratio + member))
    rows_block = jnp.concatenate(pieces, axis=2).reshape(freq_count, 2 * span_i, local_pts)
    cols_block = green_panel.reshape(freq_count, 2 * span_j, local_pts)

    slot = lax.axis_index("row") * col_count + lax.axis_index("col")
    offset = slot * piece
    placed = lax.dynamic_update_slice_in_dim(
        jnp.zeros((freq_count, local_pts), jnp.float32), log_psd[0], offset, axis=1
    )
    log_field = butterfly_sum(placed, ("row", "col"))

    for _ in range(ITERS):
        psd_field = jnp.exp(log_field)
        weighted = (green_panel * psd_field[:, None, None, :]).astype(jnp.bfloat16)
        weighted = weighted.reshape(freq_count, 2 * span_j, local_pts)
        pair_sum = swap_add(correlate(rows_block, weighted), "pts")
        adjoint = (pair_scale * (quad_weight * pair_sum - observed)).astype(jnp.bfloat16)
        point_part = point_terms(adjoint, cols_block, rows_block, psd_field, quad_weight)
        gradient = butterfly_sum(point_part, ("row", "col"))
        squares = swap_add(jnp.sum(gradient * gradient), "pts")
        log_field = log_field - descent * gradient / jnp.sqrt(squares / entry_count + epsilon)

    own = lax.dynamic_slice_in_dim(log_field, offset, piece, axis=1)
    return own[None]


PAIR_PLAN = ((0, 0, 1), (1, 2, 0), (2, 0, 3), (2, 2, 1), (1, 1, 3), (3, 3, 2))


def pair_tables(blocks):
    role = [0] * (blocks * blocks)
    panel_moves = []
    needs = []
    for line, sender, receiver in PAIR_PLAN:
        role[line * blocks + receiver] = 1
        panel_moves.append((line * blocks + sender, line * blocks + receiver))
        needs.append((line * blocks + receiver, 0, receiver * blocks + sender))
        needs.append((line * blocks + receiver, 1, sender * blocks + receiver))
    for plane in range(blocks):
        role[plane * blocks + plane] = 2
    rounds = []
    moved = [[0, 0] for _ in range(blocks * blocks)]
    for dest, which, owner in needs:
        if owner == dest:
            continue
        for number, (pairs, whiches) in enumerate(rounds):
            if all(s != owner and d != dest for s, d in pairs):
                pairs.append((owner, dest))
                whiches.append((dest, which))
                moved[dest][which] = number + 1
                break
        else:
            rounds.append(([(owner, dest)], [(dest, which)]))
            moved[dest][which] = len(rounds)
    return role, panel_moves, rounds, moved


def pair_body(green_panel, log_psd, observed, pair_weights):
    freq_count, comp_count, span_j, local_pts = green_panel.shape
    piece = log_psd.shape[2]
    blocks = lax.axis_size("col")
    pts_count = lax.axis_size("pts")
    quad_weight = 1.0 / (pts_count * local_pts)
    entry_count = freq_count * pts_count * local_pts
    role, panel_moves, rounds, moved = pair_tables(blocks)
    slot = lax.axis_index("row") * blocks + lax.axis_index("col")
    my_role = jnp.array(role, jnp.int32)[slot]
    is_diag = my_role == 2
    axes = ("row", "col")

    received = lax.ppermute(green_panel, axes, panel_moves)

    own_block = jnp.concatenate(
        [observed.reshape(-1, span_j, span_j), pair_weights.astype(jnp.float32)[None]], axis=0
    )
    planes = own_block.shape[0]
    half_planes = (planes + 1) // 2
    padded = jnp.concatenate(
        [own_block, jnp.zeros((2 * half_planes - planes,) + own_block.shape[1:], own_block.dtype)], axis=0
    )
    core = lax.axis_index("pts")
    own_half = lax.dynamic_slice_in_dim(padded, core * half_planes, half_planes, axis=0)
    halves = jnp.stack([lax.ppermute(own_half, axes, pairs) for pairs, _ in rounds])
    partner_halves = lax.ppermute(halves, "pts", [(0, 1), (1, 0)])
    joined = jnp.where(
        core == 0,
        jnp.concatenate([halves, partner_halves], axis=1),
        jnp.concatenate([partner_halves, halves], axis=1),
    )[:, :planes]
    arrived = jnp.concatenate([own_block[None], joined], axis=0)
    received, arrived = lax.optimization_barrier((received, arrived))
    other = jnp.where(is_diag, green_panel, received)
    mine_rows = green_panel.reshape(freq_count, 2 * span_j, local_pts)
    other_rows = other.reshape(freq_count, 2 * span_j, local_pts)
    moved_table = jnp.array(moved, jnp.int32)[slot]
    first_block = arrived[moved_table[0]]
    second_block = arrived[moved_table[1]]
    obs_first = first_block[:-1].reshape(observed.shape)
    obs_second = second_block[:-1].reshape(observed.shape)
    scale_first = first_block[-1]
    scale_second = second_block[-1]
    keep_first = my_role > 0
    keep_second = my_role == 1

    offset = slot * piece
    placed = lax.dynamic_update_slice_in_dim(
        jnp.zeros((freq_count, local_pts), jnp.float32), log_psd[0], offset, axis=1
    )
    log_field = butterfly_sum(placed, axes)

    def run_sweep(sweep_idx, log_field):
        psd_field = jnp.exp(log_field)
        spread = psd_field[:, None, None, :]
        product_first, product_second = pair_products(mine_rows, other_rows, psd_field)
        corr_first = combine(product_first, span_j, span_j)
        corr_second = combine(product_second, span_j, span_j)
        both = swap_add(jnp.stack([corr_first, corr_second]), "pts")
        adj_first = (scale_first * (quad_weight * both[0] - obs_first)).astype(jnp.bfloat16)
        adj_second = (scale_second * (quad_weight * both[1] - obs_second)).astype(jnp.bfloat16)
        term_first = point_terms(adj_first, other_rows, mine_rows, psd_field, quad_weight)
        term_second = point_terms(adj_second, mine_rows, other_rows, psd_field, quad_weight)
        point_part = jnp.where(keep_first, term_first, 0.0) + jnp.where(keep_second, term_second, 0.0)
        gradient = butterfly_sum(point_part, axes)
        squares = swap_add(jnp.sum(gradient * gradient), "pts")
        return log_field - descent * gradient / jnp.sqrt(squares / entry_count + epsilon)

    log_field = lax.fori_loop(0, ITERS, run_sweep, log_field)
    own = lax.dynamic_slice_in_dim(log_field, offset, piece, axis=1)
    return own[None]


def solution(mesh):
    shape = mesh.shape
    plan_fits = shape["row"] == 4 and shape["col"] == 4 and shape["pts"] == 2
    return jax.shard_map(
        pair_body if plan_fits else broadcast_body,
        mesh=mesh,
        in_specs=(
            P(None, None, "col", "pts"),
            P("pts", None, ("row", "col")),
            P(None, None, "row", "col"),
            P("row", "col"),
        ),
        out_specs=P("pts", None, ("row", "col")),
        check_vma=False,
    )
```

```python
import jax
import jax.numpy as jnp
from jax import lax
from jax.experimental import pallas as pl
from jax.experimental.pallas import tpu as pltpu
from jax.sharding import PartitionSpec as P

ITERS = 2


epsilon = 1e-06
descent = 0.1


def from_root(block, axis, source):
    block = jnp.where(lax.axis_index(axis) == source, block, jnp.zeros_like(block))
    return lax.psum(block, axis)


def butterfly_sum(value, axes):
    for axis in axes:
        size = lax.axis_size(axis)
        if size & (size - 1):
            value = lax.psum(value, axis)
            continue
        me = lax.axis_index(axis)
        bit = 1
        while bit < size:
            radix = 4 if bit * 4 <= size else 2
            got = [value]
            for m in range(1, radix):
                mask = m * bit
                got.append(lax.ppermute(value, axis, [(i, i ^ mask) for i in range(size)]))
            stacked = jnp.stack(got)
            local = (me // bit) % radix
            ordered = [stacked[local ^ j] for j in range(radix)]
            if radix == 4:
                value = (ordered[0] + ordered[1]) + (ordered[2] + ordered[3])
            else:
                value = ordered[0] + ordered[1]
            bit *= radix
    return value


def swap_add(value, axis):
    size = lax.axis_size(axis)
    if size != 2:
        return lax.psum(value, axis)
    return value + lax.ppermute(value, axis, [(0, 1), (1, 0)])


def correlate(left_rows, weighted):
    half_a = left_rows.shape[1] // 2
    half_b = weighted.shape[1] // 2
    products = jnp.einsum("fan,fbn->fab", left_rows, weighted, preferred_element_type=jnp.float32)
    corr_real = products[:, :half_a, :half_b] + products[:, half_a:, half_b:]
    corr_imag = products[:, half_a:, :half_b] - products[:, :half_a, half_b:]
    return jnp.stack([corr_real, corr_imag], axis=1)


def pair_products(mine, other, field, tile=3072):
    freq, rows, points = mine.shape
    def kernel(mine_ref, other_ref, field_ref, first_ref, second_ref):
        step = pl.program_id(1)
        @pl.when(step == 0)
        def _():
            first_ref[...] = jnp.zeros_like(first_ref)
            second_ref[...] = jnp.zeros_like(second_ref)
        spread = field_ref[0]
        mine_tile = mine_ref[0]
        other_tile = other_ref[0]
        weighted_other = (other_tile.astype(jnp.float32) * spread).astype(jnp.bfloat16)
        weighted_mine = (mine_tile.astype(jnp.float32) * spread).astype(jnp.bfloat16)
        dims = (((1,), (1,)), ((), ()))
        first_ref[0] += jax.lax.dot_general(mine_tile, weighted_other, dims, preferred_element_type=jnp.float32)
        second_ref[0] += jax.lax.dot_general(other_tile, weighted_mine, dims, preferred_element_type=jnp.float32)
    spec = pl.BlockSpec((1, rows, tile), lambda f, t: (f, 0, t))
    out_spec = pl.BlockSpec((1, rows, rows), lambda f, t: (f, 0, 0))
    return pl.pallas_call(
        kernel,
        grid=(freq, points // tile),
        in_specs=[spec, spec, pl.BlockSpec((1, 1, tile), lambda f, t: (f, 0, t))],
        out_specs=[out_spec, out_spec],
        out_shape=[jax.ShapeDtypeStruct((freq, rows, rows), jnp.float32)] * 2,
        compiler_params=pltpu.CompilerParams(dimension_semantics=("parallel", "arbitrary")),
    )(mine, other, field[:, None, :])


def combine(products, half_a, half_b):
    corr_real = products[:, :half_a, :half_b] + products[:, half_a:, half_b:]
    corr_imag = products[:, half_a:, :half_b] - products[:, :half_a, half_b:]
    return jnp.stack([corr_real, corr_imag], axis=1)


def adjoint_block(adjoint):
    adj_real = adjoint[:, 0]
    adj_imag = adjoint[:, 1]
    top_half = jnp.concatenate([adj_real, -adj_imag], axis=2)
    low_half = jnp.concatenate([adj_imag, adj_real], axis=2)
    return jnp.concatenate([top_half, low_half], axis=1)


def point_terms(adjoint, right_rows, left_rows, psd_field, quad_weight):
    accumulated = jnp.einsum(
        "fab,fbn->fan", adjoint_block(adjoint), right_rows, preferred_element_type=jnp.float32
    )
    return quad_weight * psd_field * jnp.sum(left_rows * accumulated, axis=1)


def broadcast_body(green_panel, log_psd, observed, pair_weights):
    freq_count, comp_count, span_j, local_pts = green_panel.shape
    span_i = observed.shape[2]
    piece = log_psd.shape[2]
    row_count = lax.axis_size("row")
    col_count = lax.axis_size("col")
    pts_count = lax.axis_size("pts")
    quad_weight = 1.0 / (pts_count * local_pts)
    entry_count = freq_count * pts_count * local_pts
    pair_scale = pair_weights.astype(jnp.float32)
    group_ratio = col_count // row_count
    pieces = []
    for member in range(group_ratio):
        pieces.append(from_root(green_panel, "col", lax.axis_index("row") * group_ratio + member))
    rows_block = jnp.concatenate(pieces, axis=2).reshape(freq_count, 2 * span_i, local_pts)
    cols_block = green_panel.reshape(freq_count, 2 * span_j, local_pts)

    slot = lax.axis_index("row") * col_count + lax.axis_index("col")
    offset = slot * piece
    placed = lax.dynamic_update_slice_in_dim(
        jnp.zeros((freq_count, local_pts), jnp.float32), log_psd[0], offset, axis=1
    )
    log_field = butterfly_sum(placed, ("row", "col"))

    for _ in range(ITERS):
        psd_field = jnp.exp(log_field)
        weighted = (green_panel * psd_field[:, None, None, :]).astype(jnp.bfloat16)
        weighted = weighted.reshape(freq_count, 2 * span_j, local_pts)
        pair_sum = swap_add(correlate(rows_block, weighted), "pts")
        adjoint = (pair_scale * (quad_weight * pair_sum - observed)).astype(jnp.bfloat16)
        point_part = point_terms(adjoint, cols_block, rows_block, psd_field, quad_weight)
        gradient = butterfly_sum(point_part, ("row", "col"))
        squares = swap_add(jnp.sum(gradient * gradient), "pts")
        log_field = log_field - descent * gradient / jnp.sqrt(squares / entry_count + epsilon)

    own = lax.dynamic_slice_in_dim(log_field, offset, piece, axis=1)
    return own[None]


PAIR_PLAN = ((0, 0, 1), (1, 2, 0), (2, 0, 3), (2, 2, 1), (1, 1, 3), (3, 3, 2))


def pair_tables(blocks):
    role = [0] * (blocks * blocks)
    panel_moves = []
    needs = []
    for line, sender, receiver in PAIR_PLAN:
        role[line * blocks + receiver] = 1
        panel_moves.append((line * blocks + sender, line * blocks + receiver))
        needs.append((line * blocks + receiver, 0, receiver * blocks + sender))
        needs.append((line * blocks + receiver, 1, sender * blocks + receiver))
    for plane in range(blocks):
        role[plane * blocks + plane] = 2
    rounds = []
    moved = [[0, 0] for _ in range(blocks * blocks)]
    for dest, which, owner in needs:
        if owner == dest:
            continue
        for number, (pairs, whiches) in enumerate(rounds):
            if all(s != owner and d != dest for s, d in pairs):
                pairs.append((owner, dest))
                whiches.append((dest, which))
                moved[dest][which] = number + 1
                break
        else:
            rounds.append(([(owner, dest)], [(dest, which)]))
            moved[dest][which] = len(rounds)
    return role, panel_moves, rounds, moved


def pair_body(green_panel, log_psd, observed, pair_weights):
    freq_count, comp_count, span_j, local_pts = green_panel.shape
    piece = log_psd.shape[2]
    blocks = lax.axis_size("col")
    pts_count = lax.axis_size("pts")
    quad_weight = 1.0 / (pts_count * local_pts)
    entry_count = freq_count * pts_count * local_pts
    role, panel_moves, rounds, moved = pair_tables(blocks)
    slot = lax.axis_index("row") * blocks + lax.axis_index("col")
    my_role = jnp.array(role, jnp.int32)[slot]
    is_diag = my_role == 2
    axes = ("row", "col")

    received = lax.ppermute(green_panel, axes, panel_moves)

    own_block = jnp.concatenate(
        [observed.reshape(-1, span_j, span_j), pair_weights.astype(jnp.float32)[None]], axis=0
    )
    planes = own_block.shape[0]
    half_planes = (planes + 1) // 2
    padded = jnp.concatenate(
        [own_block, jnp.zeros((2 * half_planes - planes,) + own_block.shape[1:], own_block.dtype)], axis=0
    )
    core = lax.axis_index("pts")
    own_half = lax.dynamic_slice_in_dim(padded, core * half_planes, half_planes, axis=0)
    halves = jnp.stack([lax.ppermute(own_half, axes, pairs) for pairs, _ in rounds])
    partner_halves = lax.ppermute(halves, "pts", [(0, 1), (1, 0)])
    joined = jnp.where(
        core == 0,
        jnp.concatenate([halves, partner_halves], axis=1),
        jnp.concatenate([partner_halves, halves], axis=1),
    )[:, :planes]
    arrived = jnp.concatenate([own_block[None], joined], axis=0)
    received, arrived = lax.optimization_barrier((received, arrived))
    other = lax.cond(is_diag, lambda: green_panel, lambda: received)
    mine_rows = green_panel.reshape(freq_count, 2 * span_j, local_pts)
    other_rows = other.reshape(freq_count, 2 * span_j, local_pts)
    moved_table = jnp.array(moved, jnp.int32)[slot]
    first_block = arrived[moved_table[0]]
    second_block = arrived[moved_table[1]]
    obs_first = first_block[:-1].reshape(observed.shape)
    obs_second = second_block[:-1].reshape(observed.shape)
    scale_first = first_block[-1]
    scale_second = second_block[-1]
    keep_first = my_role > 0
    keep_second = my_role == 1

    offset = slot * piece
    placed = lax.dynamic_update_slice_in_dim(
        jnp.zeros((freq_count, local_pts), jnp.float32), log_psd[0], offset, axis=1
    )
    log_field = butterfly_sum(placed, axes)

    def run_sweep(sweep_idx, log_field):
        psd_field = jnp.exp(log_field)
        spread = psd_field[:, None, None, :]
        product_first, product_second = pair_products(mine_rows, other_rows, psd_field)
        corr_first = combine(product_first, span_j, span_j)
        corr_second = combine(product_second, span_j, span_j)
        both = swap_add(jnp.stack([corr_first, corr_second]), "pts")
        adj_first = (scale_first * (quad_weight * both[0] - obs_first)).astype(jnp.bfloat16)
        adj_second = (scale_second * (quad_weight * both[1] - obs_second)).astype(jnp.bfloat16)
        term_first = point_terms(adj_first, other_rows, mine_rows, psd_field, quad_weight)
        term_second = point_terms(adj_second, mine_rows, other_rows, psd_field, quad_weight)
        point_part = jnp.where(keep_first, term_first, 0.0) + jnp.where(keep_second, term_second, 0.0)
        gradient = butterfly_sum(point_part, axes)
        squares = swap_add(jnp.sum(gradient * gradient), "pts")
        return log_field - descent * gradient / jnp.sqrt(squares / entry_count + epsilon)

    log_field = lax.fori_loop(0, ITERS, run_sweep, log_field)
    own = lax.dynamic_slice_in_dim(log_field, offset, piece, axis=1)
    return own[None]


def solution(mesh):
    shape = mesh.shape
    plan_fits = shape["row"] == 4 and shape["col"] == 4 and shape["pts"] == 2
    return jax.shard_map(
        pair_body if plan_fits else broadcast_body,
        mesh=mesh,
        in_specs=(
            P(None, None, "col", "pts"),
            P("pts", None, ("row", "col")),
            P(None, None, "row", "col"),
            P("row", "col"),
        ),
        out_specs=P("pts", None, ("row", "col")),
        check_vma=False,
    )
```

```python
import jax
import jax.numpy as jnp
from jax import lax
from jax.experimental import pallas as pl
from jax.experimental.pallas import tpu as pltpu
from jax.sharding import PartitionSpec as P

ITERS = 2


epsilon = 1e-06
descent = 0.1


def from_root(block, axis, source):
    block = jnp.where(lax.axis_index(axis) == source, block, jnp.zeros_like(block))
    return lax.psum(block, axis)


def butterfly_sum(value, axes):
    for axis in axes:
        size = lax.axis_size(axis)
        if size & (size - 1):
            value = lax.psum(value, axis)
            continue
        me = lax.axis_index(axis)
        bit = 1
        while bit < size:
            radix = 4 if bit * 4 <= size else 2
            got = [value]
            for m in range(1, radix):
                mask = m * bit
                got.append(lax.ppermute(value, axis, [(i, i ^ mask) for i in range(size)]))
            stacked = jnp.stack(got)
            local = (me // bit) % radix
            ordered = [stacked[local ^ j] for j in range(radix)]
            if radix == 4:
                value = (ordered[0] + ordered[1]) + (ordered[2] + ordered[3])
            else:
                value = ordered[0] + ordered[1]
            bit *= radix
    return value


def swap_add(value, axis):
    size = lax.axis_size(axis)
    if size != 2:
        return lax.psum(value, axis)
    return value + lax.ppermute(value, axis, [(0, 1), (1, 0)])


def correlate(left_rows, weighted):
    half_a = left_rows.shape[1] // 2
    half_b = weighted.shape[1] // 2
    products = jnp.einsum("fan,fbn->fab", left_rows, weighted, preferred_element_type=jnp.float32)
    corr_real = products[:, :half_a, :half_b] + products[:, half_a:, half_b:]
    corr_imag = products[:, half_a:, :half_b] - products[:, :half_a, half_b:]
    return jnp.stack([corr_real, corr_imag], axis=1)


def pair_products(mine, other, field, tile=3072):
    freq, rows, points = mine.shape
    def kernel(mine_ref, other_ref, field_ref, first_ref, second_ref):
        step = pl.program_id(1)
        @pl.when(step == 0)
        def _():
            first_ref[...] = jnp.zeros_like(first_ref)
            second_ref[...] = jnp.zeros_like(second_ref)
        spread = field_ref[0]
        mine_tile = mine_ref[0]
        other_tile = other_ref[0]
        weighted_other = (other_tile.astype(jnp.float32) * spread).astype(jnp.bfloat16)
        weighted_mine = (mine_tile.astype(jnp.float32) * spread).astype(jnp.bfloat16)
        dims = (((1,), (1,)), ((), ()))
        first_ref[0] += jax.lax.dot_general(mine_tile, weighted_other, dims, preferred_element_type=jnp.float32)
        second_ref[0] += jax.lax.dot_general(other_tile, weighted_mine, dims, preferred_element_type=jnp.float32)
    spec = pl.BlockSpec((1, rows, tile), lambda f, t: (f, 0, t))
    out_spec = pl.BlockSpec((1, rows, rows), lambda f, t: (f, 0, 0))
    return pl.pallas_call(
        kernel,
        grid=(freq, points // tile),
        in_specs=[spec, spec, pl.BlockSpec((1, 1, tile), lambda f, t: (f, 0, t))],
        out_specs=[out_spec, out_spec],
        out_shape=[jax.ShapeDtypeStruct((freq, rows, rows), jnp.float32)] * 2,
        compiler_params=pltpu.CompilerParams(dimension_semantics=("parallel", "arbitrary")),
    )(mine, other, field[:, None, :])


def combine(products, half_a, half_b):
    corr_real = products[:, :half_a, :half_b] + products[:, half_a:, half_b:]
    corr_imag = products[:, half_a:, :half_b] - products[:, :half_a, half_b:]
    return jnp.stack([corr_real, corr_imag], axis=1)


def adjoint_block(adjoint):
    adj_real = adjoint[:, 0]
    adj_imag = adjoint[:, 1]
    top_half = jnp.concatenate([adj_real, -adj_imag], axis=2)
    low_half = jnp.concatenate([adj_imag, adj_real], axis=2)
    return jnp.concatenate([top_half, low_half], axis=1)


def point_terms(adjoint, right_rows, left_rows, psd_field, quad_weight):
    accumulated = jnp.einsum(
        "fab,fbn->fan", adjoint_block(adjoint), right_rows, preferred_element_type=jnp.float32
    )
    return quad_weight * psd_field * jnp.sum(left_rows * accumulated, axis=1)


def broadcast_body(green_panel, log_psd, observed, pair_weights):
    freq_count, comp_count, span_j, local_pts = green_panel.shape
    span_i = observed.shape[2]
    piece = log_psd.shape[2]
    row_count = lax.axis_size("row")
    col_count = lax.axis_size("col")
    pts_count = lax.axis_size("pts")
    quad_weight = 1.0 / (pts_count * local_pts)
    entry_count = freq_count * pts_count * local_pts
    pair_scale = pair_weights.astype(jnp.float32)
    group_ratio = col_count // row_count
    pieces = []
    for member in range(group_ratio):
        pieces.append(from_root(green_panel, "col", lax.axis_index("row") * group_ratio + member))
    rows_block = jnp.concatenate(pieces, axis=2).reshape(freq_count, 2 * span_i, local_pts)
    cols_block = green_panel.reshape(freq_count, 2 * span_j, local_pts)

    slot = lax.axis_index("row") * col_count + lax.axis_index("col")
    offset = slot * piece
    placed = lax.dynamic_update_slice_in_dim(
        jnp.zeros((freq_count, local_pts), jnp.float32), log_psd[0], offset, axis=1
    )
    log_field = butterfly_sum(placed, ("row", "col"))

    for _ in range(ITERS):
        psd_field = jnp.exp(log_field)
        weighted = (green_panel * psd_field[:, None, None, :]).astype(jnp.bfloat16)
        weighted = weighted.reshape(freq_count, 2 * span_j, local_pts)
        pair_sum = swap_add(correlate(rows_block, weighted), "pts")
        adjoint = (pair_scale * (quad_weight * pair_sum - observed)).astype(jnp.bfloat16)
        point_part = point_terms(adjoint, cols_block, rows_block, psd_field, quad_weight)
        gradient = butterfly_sum(point_part, ("row", "col"))
        squares = swap_add(jnp.sum(gradient * gradient), "pts")
        log_field = log_field - descent * gradient / jnp.sqrt(squares / entry_count + epsilon)

    own = lax.dynamic_slice_in_dim(log_field, offset, piece, axis=1)
    return own[None]


PAIR_PLAN = ((0, 0, 1), (1, 2, 0), (2, 0, 3), (2, 2, 1), (1, 1, 3), (3, 3, 2))


def pair_tables(blocks):
    role = [0] * (blocks * blocks)
    panel_moves = []
    needs = []
    for line, sender, receiver in PAIR_PLAN:
        role[line * blocks + receiver] = 1
        panel_moves.append((line * blocks + sender, line * blocks + receiver))
        needs.append((line * blocks + receiver, 0, receiver * blocks + sender))
        needs.append((line * blocks + receiver, 1, sender * blocks + receiver))
    for plane in range(blocks):
        role[plane * blocks + plane] = 2
    rounds = []
    moved = [[0, 0] for _ in range(blocks * blocks)]
    for dest, which, owner in needs:
        if owner == dest:
            continue
        for number, (pairs, whiches) in enumerate(rounds):
            if all(s != owner and d != dest for s, d in pairs):
                pairs.append((owner, dest))
                whiches.append((dest, which))
                moved[dest][which] = number + 1
                break
        else:
            rounds.append(([(owner, dest)], [(dest, which)]))
            moved[dest][which] = len(rounds)
    return role, panel_moves, rounds, moved


def pair_body(green_panel, log_psd, observed, pair_weights):
    freq_count, comp_count, span_j, local_pts = green_panel.shape
    piece = log_psd.shape[2]
    blocks = lax.axis_size("col")
    pts_count = lax.axis_size("pts")
    quad_weight = 1.0 / (pts_count * local_pts)
    entry_count = freq_count * pts_count * local_pts
    role, panel_moves, rounds, moved = pair_tables(blocks)
    slot = lax.axis_index("row") * blocks + lax.axis_index("col")
    my_role = jnp.array(role, jnp.int32)[slot]
    is_diag = my_role == 2
    axes = ("row", "col")

    received = lax.ppermute(green_panel, axes, panel_moves)

    own_block = jnp.concatenate(
        [observed.reshape(-1, span_j, span_j), pair_weights.astype(jnp.float32)[None]], axis=0
    )
    planes = own_block.shape[0]
    half_planes = (planes + 1) // 2
    padded = jnp.concatenate(
        [own_block, jnp.zeros((2 * half_planes - planes,) + own_block.shape[1:], own_block.dtype)], axis=0
    )
    core = lax.axis_index("pts")
    own_half = lax.dynamic_slice_in_dim(padded, core * half_planes, half_planes, axis=0)
    halves = jnp.stack([lax.ppermute(own_half, axes, pairs) for pairs, _ in rounds])
    partner_halves = lax.ppermute(halves, "pts", [(0, 1), (1, 0)])
    joined = jnp.where(
        core == 0,
        jnp.concatenate([halves, partner_halves], axis=1),
        jnp.concatenate([partner_halves, halves], axis=1),
    )[:, :planes]
    arrived = jnp.concatenate([own_block[None], joined], axis=0)
    received, arrived = lax.optimization_barrier((received, arrived))
    other = lax.cond(is_diag, lambda: green_panel, lambda: received)
    mine_rows = green_panel.reshape(freq_count, 2 * span_j, local_pts)
    other_rows = other.reshape(freq_count, 2 * span_j, local_pts)
    moved_table = jnp.array(moved, jnp.int32)[slot]
    first_block = arrived[moved_table[0]]
    second_block = arrived[moved_table[1]]
    obs_first = first_block[:-1].reshape(observed.shape)
    obs_second = second_block[:-1].reshape(observed.shape)
    scale_first = first_block[-1]
    scale_second = second_block[-1]
    keep_first = my_role > 0
    keep_second = my_role == 1

    offset = slot * piece
    placed = lax.dynamic_update_slice_in_dim(
        jnp.zeros((freq_count, local_pts), jnp.float32), log_psd[0], offset, axis=1
    )
    log_field = butterfly_sum(placed, axes)

    def run_sweep(sweep_idx, log_field):
        psd_field = jnp.exp(log_field)
        spread = psd_field[:, None, None, :]
        product_first, product_second = pair_products(mine_rows, other_rows, psd_field)
        corr_first = combine(product_first, span_j, span_j)
        corr_second = combine(product_second, span_j, span_j)
        both = swap_add(jnp.stack([corr_first, corr_second]), "pts")
        adj_first = (scale_first * (quad_weight * both[0] - obs_first)).astype(jnp.bfloat16)
        adj_second = (scale_second * (quad_weight * both[1] - obs_second)).astype(jnp.bfloat16)
        term_first = point_terms(adj_first, other_rows, mine_rows, psd_field, quad_weight)
        term_second = point_terms(adj_second, mine_rows, other_rows, psd_field, quad_weight)
        point_part = jnp.where(keep_first, term_first, 0.0) + jnp.where(keep_second, term_second, 0.0)
        gradient = butterfly_sum(point_part, ("col", "row"))
        squares = swap_add(jnp.sum(gradient * gradient), "pts")
        return log_field - descent * gradient / jnp.sqrt(squares / entry_count + epsilon)

    log_field = lax.fori_loop(0, ITERS, run_sweep, log_field)
    own = lax.dynamic_slice_in_dim(log_field, offset, piece, axis=1)
    return own[None]


def solution(mesh):
    shape = mesh.shape
    plan_fits = shape["row"] == 4 and shape["col"] == 4 and shape["pts"] == 2
    return jax.shard_map(
        pair_body if plan_fits else broadcast_body,
        mesh=mesh,
        in_specs=(
            P(None, None, "col", "pts"),
            P("pts", None, ("row", "col")),
            P(None, None, "row", "col"),
            P("row", "col"),
        ),
        out_specs=P("pts", None, ("row", "col")),
        check_vma=False,
    )
```

```python
import jax
import jax.numpy as jnp
from jax import lax
from jax.experimental import pallas as pl
from jax.experimental.pallas import tpu as pltpu
from jax.sharding import PartitionSpec as P

ITERS = 2


epsilon = 1e-06
descent = 0.1


def from_root(block, axis, source):
    block = jnp.where(lax.axis_index(axis) == source, block, jnp.zeros_like(block))
    return lax.psum(block, axis)


def butterfly_sum(value, axes):
    for axis in axes:
        size = lax.axis_size(axis)
        if size & (size - 1):
            value = lax.psum(value, axis)
            continue
        me = lax.axis_index(axis)
        bit = 1
        while bit < size:
            radix = 4 if bit * 4 <= size else 2
            got = [value]
            for m in range(1, radix):
                mask = m * bit
                got.append(lax.ppermute(value, axis, [(i, i ^ mask) for i in range(size)]))
            stacked = jnp.stack(got)
            local = (me // bit) % radix
            ordered = [stacked[local ^ j] for j in range(radix)]
            if radix == 4:
                value = (ordered[0] + ordered[1]) + (ordered[2] + ordered[3])
            else:
                value = ordered[0] + ordered[1]
            bit *= radix
    return value


def swap_add(value, axis):
    size = lax.axis_size(axis)
    if size != 2:
        return lax.psum(value, axis)
    return value + lax.ppermute(value, axis, [(0, 1), (1, 0)])


def correlate(left_rows, weighted):
    half_a = left_rows.shape[1] // 2
    half_b = weighted.shape[1] // 2
    products = jnp.einsum("fan,fbn->fab", left_rows, weighted, preferred_element_type=jnp.float32)
    corr_real = products[:, :half_a, :half_b] + products[:, half_a:, half_b:]
    corr_imag = products[:, half_a:, :half_b] - products[:, :half_a, half_b:]
    return jnp.stack([corr_real, corr_imag], axis=1)


def pair_products(mine, other, field, tile=3072):
    freq, rows, points = mine.shape
    def kernel(mine_ref, other_ref, field_ref, first_ref, second_ref):
        step = pl.program_id(1)
        @pl.when(step == 0)
        def _():
            first_ref[...] = jnp.zeros_like(first_ref)
            second_ref[...] = jnp.zeros_like(second_ref)
        spread = field_ref[0]
        mine_tile = mine_ref[0]
        other_tile = other_ref[0]
        weighted_other = (other_tile.astype(jnp.float32) * spread).astype(jnp.bfloat16)
        weighted_mine = (mine_tile.astype(jnp.float32) * spread).astype(jnp.bfloat16)
        dims = (((1,), (1,)), ((), ()))
        first_ref[0] += jax.lax.dot_general(mine_tile, weighted_other, dims, preferred_element_type=jnp.float32)
        second_ref[0] += jax.lax.dot_general(other_tile, weighted_mine, dims, preferred_element_type=jnp.float32)
    spec = pl.BlockSpec((1, rows, tile), lambda f, t: (f, 0, t))
    out_spec = pl.BlockSpec((1, rows, rows), lambda f, t: (f, 0, 0))
    return pl.pallas_call(
        kernel,
        grid=(freq, points // tile),
        in_specs=[spec, spec, pl.BlockSpec((1, 1, tile), lambda f, t: (f, 0, t))],
        out_specs=[out_spec, out_spec],
        out_shape=[jax.ShapeDtypeStruct((freq, rows, rows), jnp.float32)] * 2,
        compiler_params=pltpu.CompilerParams(dimension_semantics=("parallel", "arbitrary")),
    )(mine, other, field[:, None, :])


def combine(products, half_a, half_b):
    corr_real = products[:, :half_a, :half_b] + products[:, half_a:, half_b:]
    corr_imag = products[:, half_a:, :half_b] - products[:, :half_a, half_b:]
    return jnp.stack([corr_real, corr_imag], axis=1)


def adjoint_block(adjoint):
    adj_real = adjoint[:, 0]
    adj_imag = adjoint[:, 1]
    top_half = jnp.concatenate([adj_real, -adj_imag], axis=2)
    low_half = jnp.concatenate([adj_imag, adj_real], axis=2)
    return jnp.concatenate([top_half, low_half], axis=1)


def point_terms(adjoint, right_rows, left_rows, psd_field, quad_weight):
    accumulated = jnp.einsum(
        "fab,fbn->fan", adjoint_block(adjoint), right_rows, preferred_element_type=jnp.float32
    )
    return quad_weight * psd_field * jnp.sum(left_rows * accumulated, axis=1)


def broadcast_body(green_panel, log_psd, observed, pair_weights):
    freq_count, comp_count, span_j, local_pts = green_panel.shape
    span_i = observed.shape[2]
    piece = log_psd.shape[2]
    row_count = lax.axis_size("row")
    col_count = lax.axis_size("col")
    pts_count = lax.axis_size("pts")
    quad_weight = 1.0 / (pts_count * local_pts)
    entry_count = freq_count * pts_count * local_pts
    pair_scale = pair_weights.astype(jnp.float32)
    group_ratio = col_count // row_count
    pieces = []
    for member in range(group_ratio):
        pieces.append(from_root(green_panel, "col", lax.axis_index("row") * group_ratio + member))
    rows_block = jnp.concatenate(pieces, axis=2).reshape(freq_count, 2 * span_i, local_pts)
    cols_block = green_panel.reshape(freq_count, 2 * span_j, local_pts)

    slot = lax.axis_index("row") * col_count + lax.axis_index("col")
    offset = slot * piece
    placed = lax.dynamic_update_slice_in_dim(
        jnp.zeros((freq_count, local_pts), jnp.float32), log_psd[0], offset, axis=1
    )
    log_field = butterfly_sum(placed, ("row", "col"))

    for _ in range(ITERS):
        psd_field = jnp.exp(log_field)
        weighted = (green_panel * psd_field[:, None, None, :]).astype(jnp.bfloat16)
        weighted = weighted.reshape(freq_count, 2 * span_j, local_pts)
        pair_sum = swap_add(correlate(rows_block, weighted), "pts")
        adjoint = (pair_scale * (quad_weight * pair_sum - observed)).astype(jnp.bfloat16)
        point_part = point_terms(adjoint, cols_block, rows_block, psd_field, quad_weight)
        gradient = butterfly_sum(point_part, ("row", "col"))
        squares = swap_add(jnp.sum(gradient * gradient), "pts")
        log_field = log_field - descent * gradient / jnp.sqrt(squares / entry_count + epsilon)

    own = lax.dynamic_slice_in_dim(log_field, offset, piece, axis=1)
    return own[None]


PAIR_PLAN = ((0, 0, 1), (1, 2, 0), (2, 0, 3), (2, 2, 1), (1, 1, 3), (3, 3, 2))


def pair_tables(blocks):
    role = [0] * (blocks * blocks)
    panel_moves = []
    needs = []
    for line, sender, receiver in PAIR_PLAN:
        role[line * blocks + receiver] = 1
        panel_moves.append((line * blocks + sender, line * blocks + receiver))
        needs.append((line * blocks + receiver, 0, receiver * blocks + sender))
        needs.append((line * blocks + receiver, 1, sender * blocks + receiver))
    for plane in range(blocks):
        role[plane * blocks + plane] = 2
    rounds = []
    moved = [[0, 0] for _ in range(blocks * blocks)]
    for dest, which, owner in needs:
        if owner == dest:
            continue
        for number, (pairs, whiches) in enumerate(rounds):
            if all(s != owner and d != dest for s, d in pairs):
                pairs.append((owner, dest))
                whiches.append((dest, which))
                moved[dest][which] = number + 1
                break
        else:
            rounds.append(([(owner, dest)], [(dest, which)]))
            moved[dest][which] = len(rounds)
    return role, panel_moves, rounds, moved


def pair_body(green_panel, log_psd, observed, pair_weights):
    freq_count, comp_count, span_j, local_pts = green_panel.shape
    piece = log_psd.shape[2]
    blocks = lax.axis_size("col")
    pts_count = lax.axis_size("pts")
    quad_weight = 1.0 / (pts_count * local_pts)
    entry_count = freq_count * pts_count * local_pts
    role, panel_moves, rounds, moved = pair_tables(blocks)
    slot = lax.axis_index("row") * blocks + lax.axis_index("col")
    my_role = jnp.array(role, jnp.int32)[slot]
    is_diag = my_role == 2
    axes = ("row", "col")

    received = lax.ppermute(green_panel, axes, panel_moves)

    own_block = jnp.concatenate(
        [observed.reshape(-1, span_j, span_j), pair_weights.astype(jnp.float32)[None]], axis=0
    )
    planes = own_block.shape[0]
    half_planes = (planes + 1) // 2
    padded = jnp.concatenate(
        [own_block, jnp.zeros((2 * half_planes - planes,) + own_block.shape[1:], own_block.dtype)], axis=0
    )
    core = lax.axis_index("pts")
    own_half = lax.dynamic_slice_in_dim(padded, core * half_planes, half_planes, axis=0)
    halves = jnp.stack([lax.ppermute(own_half, axes, pairs) for pairs, _ in rounds])
    partner_halves = lax.ppermute(halves, "pts", [(0, 1), (1, 0)])
    joined = jnp.where(
        core == 0,
        jnp.concatenate([halves, partner_halves], axis=1),
        jnp.concatenate([partner_halves, halves], axis=1),
    )[:, :planes]
    arrived = jnp.concatenate([own_block[None], joined], axis=0)
    received, arrived = lax.optimization_barrier((received, arrived))
    other = lax.cond(is_diag, lambda: green_panel, lambda: received)
    mine_rows = green_panel.reshape(freq_count, 2 * span_j, local_pts)
    other_rows = other.reshape(freq_count, 2 * span_j, local_pts)
    stacked_rows = jnp.concatenate([mine_rows, other_rows], axis=1)
    moved_table = jnp.array(moved, jnp.int32)[slot]
    first_block = arrived[moved_table[0]]
    second_block = arrived[moved_table[1]]
    obs_first = first_block[:-1].reshape(observed.shape)
    obs_second = second_block[:-1].reshape(observed.shape)
    scale_first = first_block[-1]
    scale_second = second_block[-1]
    keep_first = my_role > 0
    keep_second = my_role == 1

    offset = slot * piece
    placed = lax.dynamic_update_slice_in_dim(
        jnp.zeros((freq_count, local_pts), jnp.float32), log_psd[0], offset, axis=1
    )
    log_field = butterfly_sum(placed, axes)

    def run_sweep(sweep_idx, log_field):
        psd_field = jnp.exp(log_field)
        spread = psd_field[:, None, None, :]
        product_first, product_second = pair_products(mine_rows, other_rows, psd_field)
        corr_first = combine(product_first, span_j, span_j)
        corr_second = combine(product_second, span_j, span_j)
        both = swap_add(jnp.stack([corr_first, corr_second]), "pts")
        adj_first = (scale_first * (quad_weight * both[0] - obs_first)).astype(jnp.bfloat16)
        adj_second = (scale_second * (quad_weight * both[1] - obs_second)).astype(jnp.bfloat16)
        block_first = jnp.where(keep_first, adjoint_block(adj_first), jnp.zeros((), jnp.bfloat16))
        block_second = jnp.where(keep_second, adjoint_block(adj_second), jnp.zeros((), jnp.bfloat16))
        empty = jnp.zeros_like(block_first)
        crossed = jnp.concatenate(
            [jnp.concatenate([empty, block_first], axis=2), jnp.concatenate([block_second, empty], axis=2)],
            axis=1,
        )
        accumulated = jnp.einsum("fab,fbn->fan", crossed, stacked_rows, preferred_element_type=jnp.float32)
        point_part = quad_weight * psd_field * jnp.sum(stacked_rows * accumulated, axis=1)
        gradient = butterfly_sum(point_part, axes)
        squares = swap_add(jnp.sum(gradient * gradient), "pts")
        return log_field - descent * gradient / jnp.sqrt(squares / entry_count + epsilon)

    log_field = lax.fori_loop(0, ITERS, run_sweep, log_field)
    own = lax.dynamic_slice_in_dim(log_field, offset, piece, axis=1)
    return own[None]


def solution(mesh):
    shape = mesh.shape
    plan_fits = shape["row"] == 4 and shape["col"] == 4 and shape["pts"] == 2
    return jax.shard_map(
        pair_body if plan_fits else broadcast_body,
        mesh=mesh,
        in_specs=(
            P(None, None, "col", "pts"),
            P("pts", None, ("row", "col")),
            P(None, None, "row", "col"),
            P("row", "col"),
        ),
        out_specs=P("pts", None, ("row", "col")),
        check_vma=False,
    )
```

```python
import jax
import jax.numpy as jnp
from jax import lax
from jax.experimental import pallas as pl
from jax.experimental.pallas import tpu as pltpu
from jax.sharding import PartitionSpec as P

ITERS = 2


epsilon = 1e-06
descent = 0.1


def from_root(block, axis, source):
    block = jnp.where(lax.axis_index(axis) == source, block, jnp.zeros_like(block))
    return lax.psum(block, axis)


def butterfly_sum(value, axes):
    for axis in axes:
        size = lax.axis_size(axis)
        if size & (size - 1):
            value = lax.psum(value, axis)
            continue
        me = lax.axis_index(axis)
        bit = 1
        while bit < size:
            radix = 4 if bit * 4 <= size else 2
            got = [value]
            for m in range(1, radix):
                mask = m * bit
                got.append(lax.ppermute(value, axis, [(i, i ^ mask) for i in range(size)]))
            stacked = jnp.stack(got)
            local = (me // bit) % radix
            ordered = [stacked[local ^ j] for j in range(radix)]
            if radix == 4:
                value = (ordered[0] + ordered[1]) + (ordered[2] + ordered[3])
            else:
                value = ordered[0] + ordered[1]
            bit *= radix
    return value


def swap_add(value, axis):
    size = lax.axis_size(axis)
    if size != 2:
        return lax.psum(value, axis)
    return value + lax.ppermute(value, axis, [(0, 1), (1, 0)])


def correlate(left_rows, weighted):
    half_a = left_rows.shape[1] // 2
    half_b = weighted.shape[1] // 2
    products = jnp.einsum("fan,fbn->fab", left_rows, weighted, preferred_element_type=jnp.float32)
    corr_real = products[:, :half_a, :half_b] + products[:, half_a:, half_b:]
    corr_imag = products[:, half_a:, :half_b] - products[:, :half_a, half_b:]
    return jnp.stack([corr_real, corr_imag], axis=1)


def pair_products(mine, other, field):
    freq, rows, points = mine.shape
    half = rows // 2

    def kernel(mine_ref, other_ref, field_ref, first_ref, second_ref):
        spread = field_ref[0]
        mine_tile = mine_ref[0]
        other_tile = other_ref[0]
        weighted_other = (other_tile.astype(jnp.float32) * spread).astype(jnp.bfloat16)
        weighted_mine = (mine_tile.astype(jnp.float32) * spread).astype(jnp.bfloat16)
        dims = (((1,), (1,)), ((), ()))
        for out_ref, left, right in ((first_ref, mine_tile, weighted_other), (second_ref, other_tile, weighted_mine)):
            products = jax.lax.dot_general(left, right, dims, preferred_element_type=jnp.float32)
            out_ref[0, 0] = products[:half, :half] + products[half:, half:]
            out_ref[0, 1] = products[half:, :half] - products[:half, half:]

    spec = pl.BlockSpec((1, rows, points), lambda f: (f, 0, 0))
    out_spec = pl.BlockSpec((1, 2, half, half), lambda f: (f, 0, 0, 0))
    return pl.pallas_call(
        kernel,
        grid=(freq,),
        in_specs=[spec, spec, pl.BlockSpec((1, 1, points), lambda f: (f, 0, 0))],
        out_specs=[out_spec, out_spec],
        out_shape=[jax.ShapeDtypeStruct((freq, 2, half, half), jnp.float32)] * 2,
    )(mine, other, field[:, None, :])


def combine(products, half_a, half_b):
    corr_real = products[:, :half_a, :half_b] + products[:, half_a:, half_b:]
    corr_imag = products[:, half_a:, :half_b] - products[:, :half_a, half_b:]
    return jnp.stack([corr_real, corr_imag], axis=1)


def adjoint_block(adjoint):
    adj_real = adjoint[:, 0]
    adj_imag = adjoint[:, 1]
    top_half = jnp.concatenate([adj_real, -adj_imag], axis=2)
    low_half = jnp.concatenate([adj_imag, adj_real], axis=2)
    return jnp.concatenate([top_half, low_half], axis=1)


def point_terms(adjoint, right_rows, left_rows, psd_field, quad_weight):
    accumulated = jnp.einsum(
        "fab,fbn->fan", adjoint_block(adjoint), right_rows, preferred_element_type=jnp.float32
    )
    return quad_weight * psd_field * jnp.sum(left_rows * accumulated, axis=1)


def broadcast_body(green_panel, log_psd, observed, pair_weights):
    freq_count, comp_count, span_j, local_pts = green_panel.shape
    span_i = observed.shape[2]
    piece = log_psd.shape[2]
    row_count = lax.axis_size("row")
    col_count = lax.axis_size("col")
    pts_count = lax.axis_size("pts")
    quad_weight = 1.0 / (pts_count * local_pts)
    entry_count = freq_count * pts_count * local_pts
    pair_scale = pair_weights.astype(jnp.float32)
    group_ratio = col_count // row_count
    pieces = []
    for member in range(group_ratio):
        pieces.append(from_root(green_panel, "col", lax.axis_index("row") * group_ratio + member))
    rows_block = jnp.concatenate(pieces, axis=2).reshape(freq_count, 2 * span_i, local_pts)
    cols_block = green_panel.reshape(freq_count, 2 * span_j, local_pts)

    slot = lax.axis_index("row") * col_count + lax.axis_index("col")
    offset = slot * piece
    placed = lax.dynamic_update_slice_in_dim(
        jnp.zeros((freq_count, local_pts), jnp.float32), log_psd[0], offset, axis=1
    )
    log_field = butterfly_sum(placed, ("row", "col"))

    for _ in range(ITERS):
        psd_field = jnp.exp(log_field)
        weighted = (green_panel * psd_field[:, None, None, :]).astype(jnp.bfloat16)
        weighted = weighted.reshape(freq_count, 2 * span_j, local_pts)
        pair_sum = swap_add(correlate(rows_block, weighted), "pts")
        adjoint = (pair_scale * (quad_weight * pair_sum - observed)).astype(jnp.bfloat16)
        point_part = point_terms(adjoint, cols_block, rows_block, psd_field, quad_weight)
        gradient = butterfly_sum(point_part, ("row", "col"))
        squares = swap_add(jnp.sum(gradient * gradient), "pts")
        log_field = log_field - descent * gradient / jnp.sqrt(squares / entry_count + epsilon)

    own = lax.dynamic_slice_in_dim(log_field, offset, piece, axis=1)
    return own[None]


PAIR_PLAN = ((0, 0, 1), (1, 2, 0), (2, 0, 3), (2, 2, 1), (1, 1, 3), (3, 3, 2))


def pair_tables(blocks):
    role = [0] * (blocks * blocks)
    panel_moves = []
    needs = []
    for line, sender, receiver in PAIR_PLAN:
        role[line * blocks + receiver] = 1
        panel_moves.append((line * blocks + sender, line * blocks + receiver))
        needs.append((line * blocks + receiver, 0, receiver * blocks + sender))
        needs.append((line * blocks + receiver, 1, sender * blocks + receiver))
    for plane in range(blocks):
        role[plane * blocks + plane] = 2
    rounds = []
    moved = [[0, 0] for _ in range(blocks * blocks)]
    for dest, which, owner in needs:
        if owner == dest:
            continue
        for number, (pairs, whiches) in enumerate(rounds):
            if all(s != owner and d != dest for s, d in pairs):
                pairs.append((owner, dest))
                whiches.append((dest, which))
                moved[dest][which] = number + 1
                break
        else:
            rounds.append(([(owner, dest)], [(dest, which)]))
            moved[dest][which] = len(rounds)
    return role, panel_moves, rounds, moved


def pair_body(green_panel, log_psd, observed, pair_weights):
    freq_count, comp_count, span_j, local_pts = green_panel.shape
    piece = log_psd.shape[2]
    blocks = lax.axis_size("col")
    pts_count = lax.axis_size("pts")
    quad_weight = 1.0 / (pts_count * local_pts)
    entry_count = freq_count * pts_count * local_pts
    role, panel_moves, rounds, moved = pair_tables(blocks)
    slot = lax.axis_index("row") * blocks + lax.axis_index("col")
    my_role = jnp.array(role, jnp.int32)[slot]
    is_diag = my_role == 2
    axes = ("row", "col")

    received = lax.ppermute(green_panel, axes, panel_moves)

    own_block = jnp.concatenate(
        [observed.reshape(-1, span_j, span_j), pair_weights.astype(jnp.float32)[None]], axis=0
    )
    planes = own_block.shape[0]
    half_planes = (planes + 1) // 2
    padded = jnp.concatenate(
        [own_block, jnp.zeros((2 * half_planes - planes,) + own_block.shape[1:], own_block.dtype)], axis=0
    )
    core = lax.axis_index("pts")
    own_half = lax.dynamic_slice_in_dim(padded, core * half_planes, half_planes, axis=0)
    halves = jnp.stack([lax.ppermute(own_half, axes, pairs) for pairs, _ in rounds])
    partner_halves = lax.ppermute(halves, "pts", [(0, 1), (1, 0)])
    joined = jnp.where(
        core == 0,
        jnp.concatenate([halves, partner_halves], axis=1),
        jnp.concatenate([partner_halves, halves], axis=1),
    )[:, :planes]
    arrived = jnp.concatenate([own_block[None], joined], axis=0)
    received, arrived = lax.optimization_barrier((received, arrived))
    other = lax.cond(is_diag, lambda: green_panel, lambda: received)
    mine_rows = green_panel.reshape(freq_count, 2 * span_j, local_pts)
    other_rows = other.reshape(freq_count, 2 * span_j, local_pts)
    moved_table = jnp.array(moved, jnp.int32)[slot]
    first_block = arrived[moved_table[0]]
    second_block = arrived[moved_table[1]]
    obs_first = first_block[:-1].reshape(observed.shape)
    obs_second = second_block[:-1].reshape(observed.shape)
    scale_first = first_block[-1]
    scale_second = second_block[-1]
    keep_first = my_role > 0
    keep_second = my_role == 1

    offset = slot * piece
    placed = lax.dynamic_update_slice_in_dim(
        jnp.zeros((freq_count, local_pts), jnp.float32), log_psd[0], offset, axis=1
    )
    log_field = butterfly_sum(placed, axes)

    def run_sweep(sweep_idx, log_field):
        psd_field = jnp.exp(log_field)
        spread = psd_field[:, None, None, :]
        corr_first, corr_second = pair_products(mine_rows, other_rows, psd_field)
        both = swap_add(jnp.stack([corr_first, corr_second]), "pts")
        adj_first = (scale_first * (quad_weight * both[0] - obs_first)).astype(jnp.bfloat16)
        adj_second = (scale_second * (quad_weight * both[1] - obs_second)).astype(jnp.bfloat16)
        term_first = point_terms(adj_first, other_rows, mine_rows, psd_field, quad_weight)
        term_second = point_terms(adj_second, mine_rows, other_rows, psd_field, quad_weight)
        point_part = jnp.where(keep_first, term_first, 0.0) + jnp.where(keep_second, term_second, 0.0)
        gradient = butterfly_sum(point_part, axes)
        squares = swap_add(jnp.sum(gradient * gradient), "pts")
        return log_field - descent * gradient / jnp.sqrt(squares / entry_count + epsilon)

    log_field = lax.fori_loop(0, ITERS, run_sweep, log_field)
    own = lax.dynamic_slice_in_dim(log_field, offset, piece, axis=1)
    return own[None]


def solution(mesh):
    shape = mesh.shape
    plan_fits = shape["row"] == 4 and shape["col"] == 4 and shape["pts"] == 2
    return jax.shard_map(
        pair_body if plan_fits else broadcast_body,
        mesh=mesh,
        in_specs=(
            P(None, None, "col", "pts"),
            P("pts", None, ("row", "col")),
            P(None, None, "row", "col"),
            P("row", "col"),
        ),
        out_specs=P("pts", None, ("row", "col")),
        check_vma=False,
    )
```

```python
import jax
import jax.numpy as jnp
from jax import lax
from jax.experimental import pallas as pl
from jax.experimental.pallas import tpu as pltpu
from jax.sharding import PartitionSpec as P

ITERS = 2


epsilon = 1e-06
descent = 0.1


def from_root(block, axis, source):
    block = jnp.where(lax.axis_index(axis) == source, block, jnp.zeros_like(block))
    return lax.psum(block, axis)


def butterfly_sum(value, axes):
    for axis in axes:
        size = lax.axis_size(axis)
        if size & (size - 1):
            value = lax.psum(value, axis)
            continue
        me = lax.axis_index(axis)
        bit = 1
        while bit < size:
            radix = 4 if bit * 4 <= size else 2
            got = [value]
            for m in range(1, radix):
                mask = m * bit
                got.append(lax.ppermute(value, axis, [(i, i ^ mask) for i in range(size)]))
            stacked = jnp.stack(got)
            local = (me // bit) % radix
            ordered = [stacked[local ^ j] for j in range(radix)]
            if radix == 4:
                value = (ordered[0] + ordered[1]) + (ordered[2] + ordered[3])
            else:
                value = ordered[0] + ordered[1]
            bit *= radix
    return value


def swap_add(value, axis):
    size = lax.axis_size(axis)
    if size != 2:
        return lax.psum(value, axis)
    return value + lax.ppermute(value, axis, [(0, 1), (1, 0)])


def correlate(left_rows, weighted):
    half_a = left_rows.shape[1] // 2
    half_b = weighted.shape[1] // 2
    products = jnp.einsum("fan,fbn->fab", left_rows, weighted, preferred_element_type=jnp.float32)
    corr_real = products[:, :half_a, :half_b] + products[:, half_a:, half_b:]
    corr_imag = products[:, half_a:, :half_b] - products[:, :half_a, half_b:]
    return jnp.stack([corr_real, corr_imag], axis=1)


def pair_products(mine, other, field, tile=3072):
    freq, rows, points = mine.shape
    def kernel(mine_ref, other_ref, field_ref, first_ref, second_ref):
        step = pl.program_id(1)
        @pl.when(step == 0)
        def _():
            first_ref[...] = jnp.zeros_like(first_ref)
            second_ref[...] = jnp.zeros_like(second_ref)
        spread = field_ref[0]
        mine_tile = mine_ref[0]
        other_tile = other_ref[0]
        weighted_other = (other_tile.astype(jnp.float32) * spread).astype(jnp.bfloat16)
        weighted_mine = (mine_tile.astype(jnp.float32) * spread).astype(jnp.bfloat16)
        dims = (((1,), (1,)), ((), ()))
        first_ref[0] += jax.lax.dot_general(mine_tile, weighted_other, dims, preferred_element_type=jnp.float32)
        second_ref[0] += jax.lax.dot_general(other_tile, weighted_mine, dims, preferred_element_type=jnp.float32)
    spec = pl.BlockSpec((1, rows, tile), lambda f, t: (f, 0, t))
    out_spec = pl.BlockSpec((1, rows, rows), lambda f, t: (f, 0, 0))
    return pl.pallas_call(
        kernel,
        grid=(freq, points // tile),
        in_specs=[spec, spec, pl.BlockSpec((1, 1, tile), lambda f, t: (f, 0, t))],
        out_specs=[out_spec, out_spec],
        out_shape=[jax.ShapeDtypeStruct((freq, rows, rows), jnp.float32)] * 2,
        compiler_params=pltpu.CompilerParams(dimension_semantics=("parallel", "arbitrary")),
    )(mine, other, field[:, None, :])


def combine(products, half_a, half_b):
    corr_real = products[:, :half_a, :half_b] + products[:, half_a:, half_b:]
    corr_imag = products[:, half_a:, :half_b] - products[:, :half_a, half_b:]
    return jnp.stack([corr_real, corr_imag], axis=1)


def adjoint_block(adjoint):
    adj_real = adjoint[:, 0]
    adj_imag = adjoint[:, 1]
    top_half = jnp.concatenate([adj_real, -adj_imag], axis=2)
    low_half = jnp.concatenate([adj_imag, adj_real], axis=2)
    return jnp.concatenate([top_half, low_half], axis=1)


def point_terms(adjoint, right_rows, left_rows, psd_field, quad_weight):
    accumulated = jnp.einsum(
        "fab,fbn->fan", adjoint_block(adjoint), right_rows, preferred_element_type=jnp.float32
    )
    return quad_weight * psd_field * jnp.sum(left_rows * accumulated, axis=1)


def broadcast_body(green_panel, log_psd, observed, pair_weights):
    freq_count, comp_count, span_j, local_pts = green_panel.shape
    span_i = observed.shape[2]
    piece = log_psd.shape[2]
    row_count = lax.axis_size("row")
    col_count = lax.axis_size("col")
    pts_count = lax.axis_size("pts")
    quad_weight = 1.0 / (pts_count * local_pts)
    entry_count = freq_count * pts_count * local_pts
    pair_scale = pair_weights.astype(jnp.float32)
    group_ratio = col_count // row_count
    pieces = []
    for member in range(group_ratio):
        pieces.append(from_root(green_panel, "col", lax.axis_index("row") * group_ratio + member))
    rows_block = jnp.concatenate(pieces, axis=2).reshape(freq_count, 2 * span_i, local_pts)
    cols_block = green_panel.reshape(freq_count, 2 * span_j, local_pts)

    slot = lax.axis_index("row") * col_count + lax.axis_index("col")
    offset = slot * piece
    placed = lax.dynamic_update_slice_in_dim(
        jnp.zeros((freq_count, local_pts), jnp.float32), log_psd[0], offset, axis=1
    )
    log_field = butterfly_sum(placed, ("row", "col"))

    for _ in range(ITERS):
        psd_field = jnp.exp(log_field)
        weighted = (green_panel * psd_field[:, None, None, :]).astype(jnp.bfloat16)
        weighted = weighted.reshape(freq_count, 2 * span_j, local_pts)
        pair_sum = swap_add(correlate(rows_block, weighted), "pts")
        adjoint = (pair_scale * (quad_weight * pair_sum - observed)).astype(jnp.bfloat16)
        point_part = point_terms(adjoint, cols_block, rows_block, psd_field, quad_weight)
        gradient = butterfly_sum(point_part, ("row", "col"))
        squares = swap_add(jnp.sum(gradient * gradient), "pts")
        log_field = log_field - descent * gradient / jnp.sqrt(squares / entry_count + epsilon)

    own = lax.dynamic_slice_in_dim(log_field, offset, piece, axis=1)
    return own[None]


PAIR_PLAN = ((0, 0, 1), (1, 2, 0), (2, 0, 3), (2, 2, 1), (1, 1, 3), (3, 3, 2))


def pair_tables(blocks):
    role = [0] * (blocks * blocks)
    panel_moves = []
    needs = []
    for line, sender, receiver in PAIR_PLAN:
        role[line * blocks + receiver] = 1
        panel_moves.append((line * blocks + sender, line * blocks + receiver))
        needs.append((line * blocks + receiver, 0, receiver * blocks + sender))
        needs.append((line * blocks + receiver, 1, sender * blocks + receiver))
    for plane in range(blocks):
        role[plane * blocks + plane] = 2
    rounds = []
    moved = [[0, 0] for _ in range(blocks * blocks)]
    for dest, which, owner in needs:
        if owner == dest:
            continue
        for number, (pairs, whiches) in enumerate(rounds):
            if all(s != owner and d != dest for s, d in pairs):
                pairs.append((owner, dest))
                whiches.append((dest, which))
                moved[dest][which] = number + 1
                break
        else:
            rounds.append(([(owner, dest)], [(dest, which)]))
            moved[dest][which] = len(rounds)
    return role, panel_moves, rounds, moved


def pair_body(green_panel, log_psd, observed, pair_weights):
    freq_count, comp_count, span_j, local_pts = green_panel.shape
    piece = log_psd.shape[2]
    blocks = lax.axis_size("col")
    pts_count = lax.axis_size("pts")
    quad_weight = 1.0 / (pts_count * local_pts)
    entry_count = freq_count * pts_count * local_pts
    role, panel_moves, rounds, moved = pair_tables(blocks)
    slot = lax.axis_index("row") * blocks + lax.axis_index("col")
    my_role = jnp.array(role, jnp.int32)[slot]
    is_diag = my_role == 2
    axes = ("row", "col")

    received = lax.ppermute(green_panel, axes, panel_moves)

    own_block = jnp.concatenate(
        [observed.reshape(-1, span_j, span_j), pair_weights.astype(jnp.float32)[None]], axis=0
    )
    planes = own_block.shape[0]
    half_planes = (planes + 1) // 2
    padded = jnp.concatenate(
        [own_block, jnp.zeros((2 * half_planes - planes,) + own_block.shape[1:], own_block.dtype)], axis=0
    )
    core = lax.axis_index("pts")
    own_half = lax.dynamic_slice_in_dim(padded, core * half_planes, half_planes, axis=0)
    halves = jnp.stack([lax.ppermute(own_half, axes, pairs) for pairs, _ in rounds])
    partner_halves = lax.ppermute(halves, "pts", [(0, 1), (1, 0)])
    joined = jnp.where(
        core == 0,
        jnp.concatenate([halves, partner_halves], axis=1),
        jnp.concatenate([partner_halves, halves], axis=1),
    )[:, :planes]
    arrived = jnp.concatenate([own_block[None], joined], axis=0)
    received, arrived = lax.optimization_barrier((received, arrived))
    other = lax.cond(is_diag, lambda: green_panel, lambda: received)
    mine_rows = green_panel.reshape(freq_count, 2 * span_j, local_pts)
    other_rows = other.reshape(freq_count, 2 * span_j, local_pts)
    moved_table = jnp.array(moved, jnp.int32)[slot]
    first_block = arrived[moved_table[0]]
    second_block = arrived[moved_table[1]]
    obs_first = first_block[:-1].reshape(observed.shape)
    obs_second = second_block[:-1].reshape(observed.shape)
    scale_first = first_block[-1]
    scale_second = second_block[-1]
    keep_first = my_role > 0
    keep_second = my_role == 1

    offset = slot * piece
    placed = lax.dynamic_update_slice_in_dim(
        jnp.zeros((freq_count, local_pts), jnp.float32), log_psd[0], offset, axis=1
    )
    log_field = butterfly_sum(placed, axes)

    def run_sweep(sweep_idx, log_field):
        psd_field = jnp.exp(log_field)
        spread = psd_field[:, None, None, :]
        product_first, product_second = pair_products(mine_rows, other_rows, psd_field)
        corr_first = combine(product_first, span_j, span_j)
        corr_second = combine(product_second, span_j, span_j)
        own_part = jnp.stack([corr_first, corr_second]).astype(jnp.bfloat16)
        peer_part = lax.ppermute(own_part, "pts", [(0, 1), (1, 0)])
        first_core = lax.axis_index("pts") == 0
        low = jnp.where(first_core, own_part, peer_part).astype(jnp.float32)
        high = jnp.where(first_core, peer_part, own_part).astype(jnp.float32)
        both = low + high
        adj_first = (scale_first * (quad_weight * both[0] - obs_first)).astype(jnp.bfloat16)
        adj_second = (scale_second * (quad_weight * both[1] - obs_second)).astype(jnp.bfloat16)
        term_first = point_terms(adj_first, other_rows, mine_rows, psd_field, quad_weight)
        term_second = point_terms(adj_second, mine_rows, other_rows, psd_field, quad_weight)
        point_part = jnp.where(keep_first, term_first, 0.0) + jnp.where(keep_second, term_second, 0.0)
        gradient = butterfly_sum(point_part, axes)
        squares = swap_add(jnp.sum(gradient * gradient), "pts")
        return log_field - descent * gradient / jnp.sqrt(squares / entry_count + epsilon)

    log_field = lax.fori_loop(0, ITERS, run_sweep, log_field)
    own = lax.dynamic_slice_in_dim(log_field, offset, piece, axis=1)
    return own[None]


def solution(mesh):
    shape = mesh.shape
    plan_fits = shape["row"] == 4 and shape["col"] == 4 and shape["pts"] == 2
    return jax.shard_map(
        pair_body if plan_fits else broadcast_body,
        mesh=mesh,
        in_specs=(
            P(None, None, "col", "pts"),
            P("pts", None, ("row", "col")),
            P(None, None, "row", "col"),
            P("row", "col"),
        ),
        out_specs=P("pts", None, ("row", "col")),
        check_vma=False,
    )
```

```python
import jax
import jax.numpy as jnp
from jax import lax
from jax.experimental import pallas as pl
from jax.experimental.pallas import tpu as pltpu
from jax.sharding import PartitionSpec as P

ITERS = 2


epsilon = 1e-06
descent = 0.1


def from_root(block, axis, source):
    block = jnp.where(lax.axis_index(axis) == source, block, jnp.zeros_like(block))
    return lax.psum(block, axis)


def butterfly_sum(value, axes):
    for axis in axes:
        size = lax.axis_size(axis)
        if size & (size - 1):
            value = lax.psum(value, axis)
            continue
        me = lax.axis_index(axis)
        bit = 1
        while bit < size:
            radix = 4 if bit * 4 <= size else 2
            got = [value]
            for m in range(1, radix):
                mask = m * bit
                got.append(lax.ppermute(value, axis, [(i, i ^ mask) for i in range(size)]))
            stacked = jnp.stack(got)
            local = (me // bit) % radix
            ordered = [stacked[local ^ j] for j in range(radix)]
            if radix == 4:
                value = (ordered[0] + ordered[1]) + (ordered[2] + ordered[3])
            else:
                value = ordered[0] + ordered[1]
            bit *= radix
    return value


def swap_add(value, axis):
    size = lax.axis_size(axis)
    if size != 2:
        return lax.psum(value, axis)
    return value + lax.ppermute(value, axis, [(0, 1), (1, 0)])


def correlate(left_rows, weighted):
    half_a = left_rows.shape[1] // 2
    half_b = weighted.shape[1] // 2
    products = jnp.einsum("fan,fbn->fab", left_rows, weighted, preferred_element_type=jnp.float32)
    corr_real = products[:, :half_a, :half_b] + products[:, half_a:, half_b:]
    corr_imag = products[:, half_a:, :half_b] - products[:, :half_a, half_b:]
    return jnp.stack([corr_real, corr_imag], axis=1)


def pair_products(mine, other, field, tile=3072):
    freq, rows, points = mine.shape
    def kernel(mine_ref, other_ref, field_ref, first_ref, second_ref):
        step = pl.program_id(1)
        @pl.when(step == 0)
        def _():
            first_ref[...] = jnp.zeros_like(first_ref)
            second_ref[...] = jnp.zeros_like(second_ref)
        for k in range(2):
            spread = field_ref[k]
            mine_tile = mine_ref[k]
            other_tile = other_ref[k]
            weighted_other = (other_tile.astype(jnp.float32) * spread).astype(jnp.bfloat16)
            weighted_mine = (mine_tile.astype(jnp.float32) * spread).astype(jnp.bfloat16)
            dims = (((1,), (1,)), ((), ()))
            first_ref[k] += jax.lax.dot_general(mine_tile, weighted_other, dims, preferred_element_type=jnp.float32)
            second_ref[k] += jax.lax.dot_general(other_tile, weighted_mine, dims, preferred_element_type=jnp.float32)
    spec = pl.BlockSpec((2, rows, tile), lambda f, t: (f, 0, t))
    out_spec = pl.BlockSpec((2, rows, rows), lambda f, t: (f, 0, 0))
    return pl.pallas_call(
        kernel,
        grid=(freq // 2, points // tile),
        in_specs=[spec, spec, pl.BlockSpec((2, 1, tile), lambda f, t: (f, 0, t))],
        out_specs=[out_spec, out_spec],
        out_shape=[jax.ShapeDtypeStruct((freq, rows, rows), jnp.float32)] * 2,
        compiler_params=pltpu.CompilerParams(dimension_semantics=("parallel", "arbitrary")),
    )(mine, other, field[:, None, :])


def combine(products, half_a, half_b):
    corr_real = products[:, :half_a, :half_b] + products[:, half_a:, half_b:]
    corr_imag = products[:, half_a:, :half_b] - products[:, :half_a, half_b:]
    return jnp.stack([corr_real, corr_imag], axis=1)


def adjoint_block(adjoint):
    adj_real = adjoint[:, 0]
    adj_imag = adjoint[:, 1]
    top_half = jnp.concatenate([adj_real, -adj_imag], axis=2)
    low_half = jnp.concatenate([adj_imag, adj_real], axis=2)
    return jnp.concatenate([top_half, low_half], axis=1)


def point_terms(adjoint, right_rows, left_rows, psd_field, quad_weight):
    accumulated = jnp.einsum(
        "fab,fbn->fan", adjoint_block(adjoint), right_rows, preferred_element_type=jnp.float32
    )
    return quad_weight * psd_field * jnp.sum(left_rows * accumulated, axis=1)


def broadcast_body(green_panel, log_psd, observed, pair_weights):
    freq_count, comp_count, span_j, local_pts = green_panel.shape
    span_i = observed.shape[2]
    piece = log_psd.shape[2]
    row_count = lax.axis_size("row")
    col_count = lax.axis_size("col")
    pts_count = lax.axis_size("pts")
    quad_weight = 1.0 / (pts_count * local_pts)
    entry_count = freq_count * pts_count * local_pts
    pair_scale = pair_weights.astype(jnp.float32)
    group_ratio = col_count // row_count
    pieces = []
    for member in range(group_ratio):
        pieces.append(from_root(green_panel, "col", lax.axis_index("row") * group_ratio + member))
    rows_block = jnp.concatenate(pieces, axis=2).reshape(freq_count, 2 * span_i, local_pts)
    cols_block = green_panel.reshape(freq_count, 2 * span_j, local_pts)

    slot = lax.axis_index("row") * col_count + lax.axis_index("col")
    offset = slot * piece
    placed = lax.dynamic_update_slice_in_dim(
        jnp.zeros((freq_count, local_pts), jnp.float32), log_psd[0], offset, axis=1
    )
    log_field = butterfly_sum(placed, ("row", "col"))

    for _ in range(ITERS):
        psd_field = jnp.exp(log_field)
        weighted = (green_panel * psd_field[:, None, None, :]).astype(jnp.bfloat16)
        weighted = weighted.reshape(freq_count, 2 * span_j, local_pts)
        pair_sum = swap_add(correlate(rows_block, weighted), "pts")
        adjoint = (pair_scale * (quad_weight * pair_sum - observed)).astype(jnp.bfloat16)
        point_part = point_terms(adjoint, cols_block, rows_block, psd_field, quad_weight)
        gradient = butterfly_sum(point_part, ("row", "col"))
        squares = swap_add(jnp.sum(gradient * gradient), "pts")
        log_field = log_field - descent * gradient / jnp.sqrt(squares / entry_count + epsilon)

    own = lax.dynamic_slice_in_dim(log_field, offset, piece, axis=1)
    return own[None]


PAIR_PLAN = ((0, 0, 1), (1, 2, 0), (2, 0, 3), (2, 2, 1), (1, 1, 3), (3, 3, 2))


def pair_tables(blocks):
    role = [0] * (blocks * blocks)
    panel_moves = []
    needs = []
    for line, sender, receiver in PAIR_PLAN:
        role[line * blocks + receiver] = 1
        panel_moves.append((line * blocks + sender, line * blocks + receiver))
        needs.append((line * blocks + receiver, 0, receiver * blocks + sender))
        needs.append((line * blocks + receiver, 1, sender * blocks + receiver))
    for plane in range(blocks):
        role[plane * blocks + plane] = 2
    rounds = []
    moved = [[0, 0] for _ in range(blocks * blocks)]
    for dest, which, owner in needs:
        if owner == dest:
            continue
        for number, (pairs, whiches) in enumerate(rounds):
            if all(s != owner and d != dest for s, d in pairs):
                pairs.append((owner, dest))
                whiches.append((dest, which))
                moved[dest][which] = number + 1
                break
        else:
            rounds.append(([(owner, dest)], [(dest, which)]))
            moved[dest][which] = len(rounds)
    return role, panel_moves, rounds, moved


def pair_body(green_panel, log_psd, observed, pair_weights):
    freq_count, comp_count, span_j, local_pts = green_panel.shape
    piece = log_psd.shape[2]
    blocks = lax.axis_size("col")
    pts_count = lax.axis_size("pts")
    quad_weight = 1.0 / (pts_count * local_pts)
    entry_count = freq_count * pts_count * local_pts
    role, panel_moves, rounds, moved = pair_tables(blocks)
    slot = lax.axis_index("row") * blocks + lax.axis_index("col")
    my_role = jnp.array(role, jnp.int32)[slot]
    is_diag = my_role == 2
    axes = ("row", "col")

    received = lax.ppermute(green_panel, axes, panel_moves)

    own_block = jnp.concatenate(
        [observed.reshape(-1, span_j, span_j), pair_weights.astype(jnp.float32)[None]], axis=0
    )
    planes = own_block.shape[0]
    half_planes = (planes + 1) // 2
    padded = jnp.concatenate(
        [own_block, jnp.zeros((2 * half_planes - planes,) + own_block.shape[1:], own_block.dtype)], axis=0
    )
    core = lax.axis_index("pts")
    own_half = lax.dynamic_slice_in_dim(padded, core * half_planes, half_planes, axis=0)
    halves = jnp.stack([lax.ppermute(own_half, axes, pairs) for pairs, _ in rounds])
    partner_halves = lax.ppermute(halves, "pts", [(0, 1), (1, 0)])
    joined = jnp.where(
        core == 0,
        jnp.concatenate([halves, partner_halves], axis=1),
        jnp.concatenate([partner_halves, halves], axis=1),
    )[:, :planes]
    arrived = jnp.concatenate([own_block[None], joined], axis=0)
    received, arrived = lax.optimization_barrier((received, arrived))
    other = lax.cond(is_diag, lambda: green_panel, lambda: received)
    mine_rows = green_panel.reshape(freq_count, 2 * span_j, local_pts)
    other_rows = other.reshape(freq_count, 2 * span_j, local_pts)
    moved_table = jnp.array(moved, jnp.int32)[slot]
    first_block = arrived[moved_table[0]]
    second_block = arrived[moved_table[1]]
    obs_first = first_block[:-1].reshape(observed.shape)
    obs_second = second_block[:-1].reshape(observed.shape)
    scale_first = first_block[-1]
    scale_second = second_block[-1]
    keep_first = my_role > 0
    keep_second = my_role == 1

    offset = slot * piece
    placed = lax.dynamic_update_slice_in_dim(
        jnp.zeros((freq_count, local_pts), jnp.float32), log_psd[0], offset, axis=1
    )
    log_field = butterfly_sum(placed, axes)

    def run_sweep(sweep_idx, log_field):
        psd_field = jnp.exp(log_field)
        spread = psd_field[:, None, None, :]
        product_first, product_second = pair_products(mine_rows, other_rows, psd_field)
        corr_first = combine(product_first, span_j, span_j)
        corr_second = combine(product_second, span_j, span_j)
        both = swap_add(jnp.stack([corr_first, corr_second]), "pts")
        adj_first = (scale_first * (quad_weight * both[0] - obs_first)).astype(jnp.bfloat16)
        adj_second = (scale_second * (quad_weight * both[1] - obs_second)).astype(jnp.bfloat16)
        term_first = point_terms(adj_first, other_rows, mine_rows, psd_field, quad_weight)
        term_second = point_terms(adj_second, mine_rows, other_rows, psd_field, quad_weight)
        point_part = jnp.where(keep_first, term_first, 0.0) + jnp.where(keep_second, term_second, 0.0)
        gradient = butterfly_sum(point_part, axes)
        squares = swap_add(jnp.sum(gradient * gradient), "pts")
        return log_field - descent * gradient / jnp.sqrt(squares / entry_count + epsilon)

    log_field = lax.fori_loop(0, ITERS, run_sweep, log_field)
    own = lax.dynamic_slice_in_dim(log_field, offset, piece, axis=1)
    return own[None]


def solution(mesh):
    shape = mesh.shape
    plan_fits = shape["row"] == 4 and shape["col"] == 4 and shape["pts"] == 2
    return jax.shard_map(
        pair_body if plan_fits else broadcast_body,
        mesh=mesh,
        in_specs=(
            P(None, None, "col", "pts"),
            P("pts", None, ("row", "col")),
            P(None, None, "row", "col"),
            P("row", "col"),
        ),
        out_specs=P("pts", None, ("row", "col")),
        check_vma=False,
    )
```

```python
import jax
import jax.numpy as jnp
from jax import lax
from jax.experimental import pallas as pl
from jax.experimental.pallas import tpu as pltpu
from jax.sharding import PartitionSpec as P

ITERS = 2


epsilon = 1e-06
descent = 0.1


def from_root(block, axis, source):
    block = jnp.where(lax.axis_index(axis) == source, block, jnp.zeros_like(block))
    return lax.psum(block, axis)


def butterfly_sum(value, axes):
    for axis in axes:
        size = lax.axis_size(axis)
        if size & (size - 1):
            value = lax.psum(value, axis)
            continue
        me = lax.axis_index(axis)
        bit = 1
        while bit < size:
            radix = 4 if bit * 4 <= size else 2
            got = [value]
            for m in range(1, radix):
                mask = m * bit
                got.append(lax.ppermute(value, axis, [(i, i ^ mask) for i in range(size)]))
            stacked = jnp.stack(got)
            local = (me // bit) % radix
            ordered = [stacked[local ^ j] for j in range(radix)]
            if radix == 4:
                value = (ordered[0] + ordered[1]) + (ordered[2] + ordered[3])
            else:
                value = ordered[0] + ordered[1]
            bit *= radix
    return value


def swap_add(value, axis):
    size = lax.axis_size(axis)
    if size != 2:
        return lax.psum(value, axis)
    return value + lax.ppermute(value, axis, [(0, 1), (1, 0)])


def correlate(left_rows, weighted):
    half_a = left_rows.shape[1] // 2
    half_b = weighted.shape[1] // 2
    products = jnp.einsum("fan,fbn->fab", left_rows, weighted, preferred_element_type=jnp.float32)
    corr_real = products[:, :half_a, :half_b] + products[:, half_a:, half_b:]
    corr_imag = products[:, half_a:, :half_b] - products[:, :half_a, half_b:]
    return jnp.stack([corr_real, corr_imag], axis=1)


def pair_products(mine, other, field, tile=3072):
    freq, rows, points = mine.shape
    def kernel(mine_ref, other_ref, field_ref, first_ref, second_ref):
        step = pl.program_id(1)
        @pl.when(step == 0)
        def _():
            first_ref[...] = jnp.zeros_like(first_ref)
            second_ref[...] = jnp.zeros_like(second_ref)
        for k in range(4):
            spread = field_ref[k]
            mine_tile = mine_ref[k]
            other_tile = other_ref[k]
            weighted_other = (other_tile.astype(jnp.float32) * spread).astype(jnp.bfloat16)
            weighted_mine = (mine_tile.astype(jnp.float32) * spread).astype(jnp.bfloat16)
            dims = (((1,), (1,)), ((), ()))
            first_ref[k] += jax.lax.dot_general(mine_tile, weighted_other, dims, preferred_element_type=jnp.float32)
            second_ref[k] += jax.lax.dot_general(other_tile, weighted_mine, dims, preferred_element_type=jnp.float32)
    spec = pl.BlockSpec((4, rows, tile), lambda f, t: (f, 0, t))
    out_spec = pl.BlockSpec((4, rows, rows), lambda f, t: (f, 0, 0))
    return pl.pallas_call(
        kernel,
        grid=(freq // 4, points // tile),
        in_specs=[spec, spec, pl.BlockSpec((4, 1, tile), lambda f, t: (f, 0, t))],
        out_specs=[out_spec, out_spec],
        out_shape=[jax.ShapeDtypeStruct((freq, rows, rows), jnp.float32)] * 2,
        compiler_params=pltpu.CompilerParams(dimension_semantics=("parallel", "arbitrary")),
    )(mine, other, field[:, None, :])


def combine(products, half_a, half_b):
    corr_real = products[:, :half_a, :half_b] + products[:, half_a:, half_b:]
    corr_imag = products[:, half_a:, :half_b] - products[:, :half_a, half_b:]
    return jnp.stack([corr_real, corr_imag], axis=1)


def adjoint_block(adjoint):
    adj_real = adjoint[:, 0]
    adj_imag = adjoint[:, 1]
    top_half = jnp.concatenate([adj_real, -adj_imag], axis=2)
    low_half = jnp.concatenate([adj_imag, adj_real], axis=2)
    return jnp.concatenate([top_half, low_half], axis=1)


def point_terms(adjoint, right_rows, left_rows, psd_field, quad_weight):
    accumulated = jnp.einsum(
        "fab,fbn->fan", adjoint_block(adjoint), right_rows, preferred_element_type=jnp.float32
    )
    return quad_weight * psd_field * jnp.sum(left_rows * accumulated, axis=1)


def broadcast_body(green_panel, log_psd, observed, pair_weights):
    freq_count, comp_count, span_j, local_pts = green_panel.shape
    span_i = observed.shape[2]
    piece = log_psd.shape[2]
    row_count = lax.axis_size("row")
    col_count = lax.axis_size("col")
    pts_count = lax.axis_size("pts")
    quad_weight = 1.0 / (pts_count * local_pts)
    entry_count = freq_count * pts_count * local_pts
    pair_scale = pair_weights.astype(jnp.float32)
    group_ratio = col_count // row_count
    pieces = []
    for member in range(group_ratio):
        pieces.append(from_root(green_panel, "col", lax.axis_index("row") * group_ratio + member))
    rows_block = jnp.concatenate(pieces, axis=2).reshape(freq_count, 2 * span_i, local_pts)
    cols_block = green_panel.reshape(freq_count, 2 * span_j, local_pts)

    slot = lax.axis_index("row") * col_count + lax.axis_index("col")
    offset = slot * piece
    placed = lax.dynamic_update_slice_in_dim(
        jnp.zeros((freq_count, local_pts), jnp.float32), log_psd[0], offset, axis=1
    )
    log_field = butterfly_sum(placed, ("row", "col"))

    for _ in range(ITERS):
        psd_field = jnp.exp(log_field)
        weighted = (green_panel * psd_field[:, None, None, :]).astype(jnp.bfloat16)
        weighted = weighted.reshape(freq_count, 2 * span_j, local_pts)
        pair_sum = swap_add(correlate(rows_block, weighted), "pts")
        adjoint = (pair_scale * (quad_weight * pair_sum - observed)).astype(jnp.bfloat16)
        point_part = point_terms(adjoint, cols_block, rows_block, psd_field, quad_weight)
        gradient = butterfly_sum(point_part, ("row", "col"))
        squares = swap_add(jnp.sum(gradient * gradient), "pts")
        log_field = log_field - descent * gradient / jnp.sqrt(squares / entry_count + epsilon)

    own = lax.dynamic_slice_in_dim(log_field, offset, piece, axis=1)
    return own[None]


PAIR_PLAN = ((0, 0, 1), (1, 2, 0), (2, 0, 3), (2, 2, 1), (1, 1, 3), (3, 3, 2))


def pair_tables(blocks):
    role = [0] * (blocks * blocks)
    panel_moves = []
    needs = []
    for line, sender, receiver in PAIR_PLAN:
        role[line * blocks + receiver] = 1
        panel_moves.append((line * blocks + sender, line * blocks + receiver))
        needs.append((line * blocks + receiver, 0, receiver * blocks + sender))
        needs.append((line * blocks + receiver, 1, sender * blocks + receiver))
    for plane in range(blocks):
        role[plane * blocks + plane] = 2
    rounds = []
    moved = [[0, 0] for _ in range(blocks * blocks)]
    for dest, which, owner in needs:
        if owner == dest:
            continue
        for number, (pairs, whiches) in enumerate(rounds):
            if all(s != owner and d != dest for s, d in pairs):
                pairs.append((owner, dest))
                whiches.append((dest, which))
                moved[dest][which] = number + 1
                break
        else:
            rounds.append(([(owner, dest)], [(dest, which)]))
            moved[dest][which] = len(rounds)
    return role, panel_moves, rounds, moved


def pair_body(green_panel, log_psd, observed, pair_weights):
    freq_count, comp_count, span_j, local_pts = green_panel.shape
    piece = log_psd.shape[2]
    blocks = lax.axis_size("col")
    pts_count = lax.axis_size("pts")
    quad_weight = 1.0 / (pts_count * local_pts)
    entry_count = freq_count * pts_count * local_pts
    role, panel_moves, rounds, moved = pair_tables(blocks)
    slot = lax.axis_index("row") * blocks + lax.axis_index("col")
    my_role = jnp.array(role, jnp.int32)[slot]
    is_diag = my_role == 2
    axes = ("row", "col")

    received = lax.ppermute(green_panel, axes, panel_moves)

    own_block = jnp.concatenate(
        [observed.reshape(-1, span_j, span_j), pair_weights.astype(jnp.float32)[None]], axis=0
    )
    planes = own_block.shape[0]
    half_planes = (planes + 1) // 2
    padded = jnp.concatenate(
        [own_block, jnp.zeros((2 * half_planes - planes,) + own_block.shape[1:], own_block.dtype)], axis=0
    )
    core = lax.axis_index("pts")
    own_half = lax.dynamic_slice_in_dim(padded, core * half_planes, half_planes, axis=0)
    halves = jnp.stack([lax.ppermute(own_half, axes, pairs) for pairs, _ in rounds])
    partner_halves = lax.ppermute(halves, "pts", [(0, 1), (1, 0)])
    joined = jnp.where(
        core == 0,
        jnp.concatenate([halves, partner_halves], axis=1),
        jnp.concatenate([partner_halves, halves], axis=1),
    )[:, :planes]
    arrived = jnp.concatenate([own_block[None], joined], axis=0)
    received, arrived = lax.optimization_barrier((received, arrived))
    other = lax.cond(is_diag, lambda: green_panel, lambda: received)
    mine_rows = green_panel.reshape(freq_count, 2 * span_j, local_pts)
    other_rows = other.reshape(freq_count, 2 * span_j, local_pts)
    moved_table = jnp.array(moved, jnp.int32)[slot]
    first_block = arrived[moved_table[0]]
    second_block = arrived[moved_table[1]]
    obs_first = first_block[:-1].reshape(observed.shape)
    obs_second = second_block[:-1].reshape(observed.shape)
    scale_first = first_block[-1]
    scale_second = second_block[-1]
    keep_first = my_role > 0
    keep_second = my_role == 1

    offset = slot * piece
    placed = lax.dynamic_update_slice_in_dim(
        jnp.zeros((freq_count, local_pts), jnp.float32), log_psd[0], offset, axis=1
    )
    log_field = butterfly_sum(placed, axes)

    def run_sweep(sweep_idx, log_field):
        psd_field = jnp.exp(log_field)
        spread = psd_field[:, None, None, :]
        product_first, product_second = pair_products(mine_rows, other_rows, psd_field)
        corr_first = combine(product_first, span_j, span_j)
        corr_second = combine(product_second, span_j, span_j)
        both = swap_add(jnp.stack([corr_first, corr_second]), "pts")
        adj_first = (scale_first * (quad_weight * both[0] - obs_first)).astype(jnp.bfloat16)
        adj_second = (scale_second * (quad_weight * both[1] - obs_second)).astype(jnp.bfloat16)
        term_first = point_terms(adj_first, other_rows, mine_rows, psd_field, quad_weight)
        term_second = point_terms(adj_second, mine_rows, other_rows, psd_field, quad_weight)
        point_part = jnp.where(keep_first, term_first, 0.0) + jnp.where(keep_second, term_second, 0.0)
        gradient = butterfly_sum(point_part, axes)
        squares = swap_add(jnp.sum(gradient * gradient), "pts")
        return log_field - descent * gradient / jnp.sqrt(squares / entry_count + epsilon)

    log_field = lax.fori_loop(0, ITERS, run_sweep, log_field)
    own = lax.dynamic_slice_in_dim(log_field, offset, piece, axis=1)
    return own[None]


def solution(mesh):
    shape = mesh.shape
    plan_fits = shape["row"] == 4 and shape["col"] == 4 and shape["pts"] == 2
    return jax.shard_map(
        pair_body if plan_fits else broadcast_body,
        mesh=mesh,
        in_specs=(
            P(None, None, "col", "pts"),
            P("pts", None, ("row", "col")),
            P(None, None, "row", "col"),
            P("row", "col"),
        ),
        out_specs=P("pts", None, ("row", "col")),
        check_vma=False,
    )
```
